32 devices in a mesh: tm: 4 (over y, x), series: 8 (over z, core).
Axes of the slice: x: 2, y: 2, z: 4, core: 2. Of those that a mesh axis runs over, the one named last changes fastest.
Arguments:
- codes: int32 [8, 512], P(None, ('tm', 'series')), may hold values from 0 to 916478, as said below
- owner_slot: int32 [8], replicated, may hold values from 0 to 7, each once
- edges: int32 [4096], replicated, may hold values from 0 to 2096640, as said below
- w_in: bfloat16 [128, 2304], replicated, may hold values from -0.09375 to 0.09375
- w_dt: bfloat16 [128, 32], replicated, may hold values from -0.5 to 0.5
- dt_bias: float32 [32], replicated, may hold values from -1 to 1
- decay_rate: float32 [32], replicated, may hold values from 1e-05 to 0.1
- grad_out: bfloat16 [8, 512, 2048], P('series', 'tm'), may hold values from -6 to 6
Outputs:
- ssd_output: bfloat16 [8, 512, 2048], P('series', 'tm')
- grad_in: float32 [128, 2304], replicated
The draws below stay inside these ranges and needn't reach their ends.
Inputs may be any that keep to these rules, and one draw needn't show every extreme that they name: `codes`: each row is one series in the order of ingestion slots. edges[0] is 0 and edges rise strictly.
All inputs are finite; a program needn't handle non-finite values.
Results may differ from the reference program's by a relative error of at most 0.0062.
The reference program's roundings to bfloat16 on the way count: a program that leaves them out, or rounds other values in their place, can miss the bound.
Values sent between devices are 32-bit elements; how exact they have to be, the bound alone decides.
No kernel may reach another device: no remote copies, remote signals or barrier semaphores. Data moves between devices by JAX's collectives and lax.ppermute only.
A program may use at most 128 MiB of HBM per device.

```python
import math
import jax
import jax.numpy as jnp
from jax import lax

HEAD_DIM = 64
STATE = 128
HEADS = 32
FEAT = 128
NBINS = 4096
TOK_DEV = 128
SERIES = 8
SEQ = 512
INNER = 2048
WIDE = 2304


def draw_codes(key, part):
    base_level = jax.random.randint(jax.random.fold_in(key, 11), (SERIES, 1), 0, 131072)
    noise_level = jax.random.randint(jax.random.fold_in(key, 12), (SERIES, SEQ), 0, 262144)
    trend_level = jnp.arange(SEQ, dtype=jnp.int32)[None, :] * (524288 // SEQ)
    values = (base_level + trend_level + noise_level).astype(jnp.int32)
    values = values.at[0, 0].set(0)
    values = values.at[0, SEQ - 1].set(131071 + (SEQ - 1) * (524288 // SEQ) + 262143)
    return values.astype(jnp.int32)


def draw_edges(key, part):
    gaps = jax.random.randint(jax.random.fold_in(key, 21), (NBINS - 1,), 1, 2097152 // NBINS)
    edges = jnp.concatenate([jnp.zeros((1,), jnp.int32), jnp.cumsum(gaps).astype(jnp.int32)])
    edges = edges.at[NBINS - 1].set((NBINS - 1) * (2097152 // NBINS))
    return edges.astype(jnp.int32)


def levels(own_key, extent, shards, least, top_value):
    gain = 1.0
    for position, blocks in shards:
        steps = jax.random.uniform(jax.random.fold_in(jax.random.fold_in(own_key, 6), position), (blocks,), jnp.float32, least / len(shards), top_value / len(shards))
        gain = gain * jnp.repeat(jnp.exp(steps), extent[position] // blocks).reshape((-1,) + (1,) * (len(extent) - 1 - position))
    return gain


def noise(key, extent, width, bound, cuts=(), kind=jnp.bfloat16):
    level = levels(key, extent, cuts, -0.22, 0.18) if cuts else 1.0
    result = jax.random.normal(key, extent, jnp.float32) * width * level
    return jnp.minimum(jnp.maximum(result, -bound), bound).astype(kind)


def setup_inputs(seed: int = 0) -> dict:
    splits = jax.random.split(jax.random.key(seed), 9)
    return {
        "codes": draw_codes(jax.random.fold_in(splits[8], 71), 0),
        "owner_slot": jax.random.permutation(splits[1], SERIES).astype(jnp.int32),
        "edges": draw_edges(jax.random.fold_in(splits[8], 71), 0),
        "w_in": noise(splits[3], (FEAT, WIDE), (32 * FEAT) ** -0.5, 0.09375),
        "w_dt": noise(splits[4], (FEAT, HEADS), FEAT ** -0.5, 0.5),
        "dt_bias": jnp.clip(jax.random.uniform(splits[5], (HEADS,), jnp.float32, -1.0, 1.0), -1.0, 1.0),
        "decay_rate": jnp.clip(jnp.exp(jax.random.uniform(splits[6], (HEADS,), jnp.float32, math.log(9.999999747378752e-06), math.log(0.1))), 9.999999747378752e-06, 0.1),
        "grad_out": noise(splits[7], (SERIES, SEQ, INNER), 1.0, 6.0, ((0, 8), (1, 4))),
    }


code_ceiling = 2097152.0

def decay_matrix(cum_decay):
    row_count = cum_decay.shape[0]
    causal = jnp.arange(row_count)[:, None] >= jnp.arange(row_count)[None, :]
    log_span = cum_decay.T[:, :, None] - cum_decay.T[:, None, :]
    return jnp.where(causal[None], jnp.exp(jnp.where(causal[None], log_span, -60.0)), 0.0)

def block_inputs(features, w_in, w_dt, dt_bias, decay_rate):
    row_count = features.shape[0]
    projected = jnp.dot(features, w_in, preferred_element_type=jnp.float32).astype(jnp.bfloat16)
    x_heads = projected[:, :INNER].reshape(row_count, HEADS, HEAD_DIM)
    b_proj = projected[:, INNER:INNER + STATE]
    c_proj = projected[:, INNER + STATE:]
    step_size = jax.nn.softplus(dt_bias + jnp.dot(features, w_dt, preferred_element_type=jnp.float32))
    cum_decay = jnp.cumsum(-step_size * decay_rate, axis=0)
    return (x_heads, b_proj, c_proj, step_size, cum_decay)

def block_common(features, grad_heads, w_in, w_dt, dt_bias, decay_rate):
    x_heads, b_proj, c_proj, step_size, cum_decay = block_inputs(features, w_in, w_dt, dt_bias, decay_rate)
    tail_factor = jnp.exp(cum_decay[-1][None, :] - cum_decay) * step_size
    x_weighted = (x_heads.astype(jnp.float32) * tail_factor[:, :, None]).astype(jnp.bfloat16)
    head_factor = jnp.exp(cum_decay)
    grad_weighted = (grad_heads.astype(jnp.float32) * head_factor[:, :, None]).astype(jnp.bfloat16)
    return (x_heads, b_proj, c_proj, step_size, cum_decay, tail_factor, x_weighted, head_factor, grad_weighted)

def block_summary(features, grad_heads, w_in, w_dt, dt_bias, decay_rate):
    parts = block_common(features, grad_heads, w_in, w_dt, dt_bias, decay_rate)
    b_proj, c_proj, cum_decay, x_weighted, grad_weighted = (parts[1], parts[2], parts[4], parts[6], parts[8])
    state_local = jnp.einsum('thp,tn->hpn', x_weighted.astype(jnp.float32), b_proj.astype(jnp.float32))
    adjoint_local = jnp.einsum('thp,tn->hpn', grad_weighted.astype(jnp.float32), c_proj.astype(jnp.float32))
    return (jnp.exp(cum_decay[-1]), state_local, adjoint_local)

def block_finish(features, grad_heads, state_in, adjoint_in, w_in, w_dt, dt_bias, decay_rate):
    row_count = features.shape[0]
    parts = block_common(features, grad_heads, w_in, w_dt, dt_bias, decay_rate)
    x_heads, b_proj, c_proj, step_size, cum_decay, tail_factor, x_weighted, head_factor, grad_weighted = parts
    fl = jnp.float32
    decay_mask = decay_matrix(cum_decay)
    scores = jnp.dot(c_proj, b_proj.T, preferred_element_type=fl)
    weights = (scores[None] * decay_mask * step_size.T[:, None, :]).astype(jnp.bfloat16)
    state_half = state_in.astype(jnp.bfloat16).astype(fl)
    adjoint_half = adjoint_in.astype(jnp.bfloat16).astype(fl)
    output = jnp.einsum('hts,shp->thp', weights.astype(fl), x_heads.astype(fl))
    output = output + jnp.einsum('tn,hpn->thp', c_proj.astype(fl), state_half) * head_factor[:, :, None]
    grad_x = jnp.einsum('hts,thp->shp', weights.astype(fl), grad_heads.astype(fl))
    grad_x = grad_x + jnp.einsum('sn,hpn->shp', b_proj.astype(fl), adjoint_half) * tail_factor[:, :, None]
    pair_scores = jnp.einsum('thp,shp->hts', grad_heads.astype(fl), x_heads.astype(fl))
    pair_mixed = lax.optimization_barrier(jnp.sum(pair_scores * decay_mask * step_size.T[:, None, :], axis=0)).astype(jnp.bfloat16)
    grad_b = jnp.dot(pair_mixed.T, c_proj, preferred_element_type=fl)
    grad_b = grad_b + jnp.einsum('shp,hpn->sn', x_weighted.astype(fl), adjoint_half)
    grad_c = jnp.dot(pair_mixed, b_proj, preferred_element_type=fl)
    grad_c = grad_c + jnp.einsum('thp,hpn->tn', grad_weighted.astype(fl), state_half)
    grad_rows = jnp.concatenate([grad_x.reshape(row_count, INNER).astype(jnp.bfloat16), grad_b.astype(jnp.bfloat16), grad_c.astype(jnp.bfloat16)], axis=1)
    grad_block = jnp.einsum('tf,tw->fw', features.astype(fl), grad_rows.astype(fl))
    return (output.reshape(row_count, INNER).astype(jnp.bfloat16), grad_block)

def reference(codes, owner_slot, edges, w_in, w_dt, dt_bias, decay_rate, grad_out):
    ordered = jnp.take(codes, owner_slot, axis=0)
    bins = (jnp.searchsorted(edges, ordered, side='right') - 1).astype(jnp.int32)

    def count_row(bin_row):
        return jnp.zeros((NBINS,), jnp.float32).at[bin_row].add(1.0)
    counts = jax.vmap(count_row)(bins)
    edge_float = edges.astype(jnp.float32)
    upper_edge = jnp.concatenate([edge_float[1:], jnp.full((1,), code_ceiling, jnp.float32)])
    before = jnp.cumsum(counts, axis=1) - counts
    reading = ordered.astype(jnp.float32)
    within_bin = (reading - edge_float[bins]) / (upper_edge - edge_float)[bins]
    quantile = (jnp.take_along_axis(before, bins, axis=1) + jnp.take_along_axis(counts, bins, axis=1) * within_bin) / SEQ
    frequency = (jnp.arange(FEAT, dtype=jnp.float32) + 0.5) * math.pi
    features = jnp.cos(quantile[:, :, None] * frequency).astype(jnp.bfloat16)
    blocks = SEQ // TOK_DEV

    def one_series(series_in):
        feature_blocks = series_in[0].reshape(blocks, TOK_DEV, FEAT)
        grad_blocks = series_in[1].reshape(blocks, TOK_DEV, HEADS, HEAD_DIM)

        def first_pass(item):
            return block_summary(item[0], item[1], w_in, w_dt, dt_bias, decay_rate)
        gates, states, adjoints = lax.map(first_pass, (feature_blocks, grad_blocks))
        zero_state = jnp.zeros((HEADS, HEAD_DIM, STATE), jnp.float32)

        def advance(carry, item):
            return (item[0][:, None, None] * carry + item[1], carry)
        _, state_in = lax.scan(advance, zero_state, (gates, states))
        _, adjoint_in = lax.scan(advance, zero_state, (gates, adjoints), reverse=True)

        def second_pass(item):
            return block_finish(item[0], item[1], item[2], item[3], w_in, w_dt, dt_bias, decay_rate)
        outputs, grad_parts = lax.map(second_pass, (feature_blocks, grad_blocks, state_in, adjoint_in))
        return (outputs.reshape(SEQ, INNER), lax.optimization_barrier(jnp.sum(grad_parts, axis=0)))
    outputs, grads_all = lax.map(one_series, (features, grad_out))
    grad_in = lax.optimization_barrier(jnp.sum(grads_all, axis=0)) / math.sqrt(SERIES * SEQ)
    return (outputs, grad_in)
```

```python
import math

import jax
import jax.numpy as jnp
from jax import lax
from jax.sharding import PartitionSpec as P

code_ceiling = 2097152.0


def decay_matrix(cum_decay):
    row_count = cum_decay.shape[0]
    causal = jnp.arange(row_count)[:, None] >= jnp.arange(row_count)[None, :]
    log_span = cum_decay.T[:, :, None] - cum_decay.T[:, None, :]
    return jnp.where(causal[None], jnp.exp(jnp.where(causal[None], log_span, -60.0)), 0.0)


def on_device(codes, owner_slot, edges, w_in, w_dt, dt_bias, decay_rate, grad_out):
    fl = jnp.float32
    half = jnp.bfloat16
    tok_rows = grad_out.shape[1]
    head_count = dt_bias.shape[0]
    inner_width = grad_out.shape[2]
    head_dim = inner_width // head_count
    state_dim = (w_in.shape[1] - inner_width) // 2
    n_blocks = lax.axis_size("tm")
    seq_len = tok_rows * n_blocks
    series_count = lax.axis_size("series")
    my_block = lax.axis_index("tm")
    my_series = lax.axis_index("series")

    all_codes = lax.all_gather(codes, ("tm", "series"), axis=1, tiled=True)
    row = lax.dynamic_index_in_dim(all_codes, owner_slot[my_series], axis=0, keepdims=False)
    reading = row.astype(fl)
    edge_float = edges.astype(fl)
    upper_edge = jnp.concatenate([edge_float[1:], jnp.full((1,), code_ceiling, fl)])
    onehot = (
        (edge_float[None, :] <= reading[:, None]) & (upper_edge[None, :] > reading[:, None])
    ).astype(fl)
    counts = jnp.sum(onehot, axis=0)
    before = jnp.cumsum(counts) - counts
    bin_table = jnp.stack([before, counts, edge_float, upper_edge - edge_float], axis=1)
    picked = jnp.dot(onehot, bin_table, precision=lax.Precision.HIGHEST)
    within_bin = (reading - picked[:, 2]) / picked[:, 3]
    quantile = (picked[:, 0] + picked[:, 1] * within_bin) / seq_len
    frequency = (jnp.arange(w_in.shape[0], dtype=fl) + 0.5) * math.pi
    features_all = jnp.cos(quantile[:, None] * frequency).astype(half)

    projected_all = jnp.dot(features_all, w_in, preferred_element_type=fl).astype(half)
    projected_all = projected_all.reshape(n_blocks, tok_rows, -1)
    x_all = projected_all[:, :, :inner_width].reshape(n_blocks, tok_rows, head_count, head_dim)
    b_all = projected_all[:, :, inner_width : inner_width + state_dim]
    c_all = projected_all[:, :, inner_width + state_dim :]
    step_all = jax.nn.softplus(
        dt_bias + jnp.dot(features_all, w_dt, preferred_element_type=fl)
    ).reshape(n_blocks, tok_rows, head_count)
    cum_all = jnp.cumsum(-step_all * decay_rate, axis=1)
    gate_all = jnp.exp(cum_all[:, -1])
    tail_all = jnp.exp(cum_all[:, -1:, :] - cum_all) * step_all
    xw_all = (x_all * tail_all[..., None]).astype(half)
    state_local_all = jnp.einsum("bthp,btn->bhpn", xw_all, b_all, preferred_element_type=fl)

    state_in = jnp.zeros((head_count, head_dim, state_dim), fl)
    for k in range(n_blocks - 1):
        new = gate_all[k][:, None, None] * state_in + state_local_all[k]
        state_in = jnp.where(k < my_block, new, state_in)

    def mine(a):
        return lax.dynamic_index_in_dim(a, my_block, axis=0, keepdims=False)

    features = mine(features_all.reshape(n_blocks, tok_rows, -1))
    x_heads = mine(x_all)
    b_proj = mine(b_all)
    c_proj = mine(c_all)
    step_size = mine(step_all)
    cum_decay = mine(cum_all)
    tail_factor = mine(tail_all)
    x_weighted = mine(xw_all)
    head_factor = jnp.exp(cum_decay)

    grad_heads = grad_out[0].reshape(tok_rows, head_count, head_dim)
    grad_weighted = (grad_heads * head_factor[:, :, None]).astype(half)
    adjoint_local = jnp.einsum("thp,tn->hpn", grad_weighted, c_proj, preferred_element_type=fl)
    adjoint_all = lax.all_gather(adjoint_local, "tm")
    adjoint_in = jnp.zeros((head_count, head_dim, state_dim), fl)
    for k in range(n_blocks - 1, 0, -1):
        new = gate_all[k][:, None, None] * adjoint_in + adjoint_all[k]
        adjoint_in = jnp.where(k > my_block, new, adjoint_in)

    masked = decay_matrix(cum_decay) * step_size.T[:, None, :]
    scores = jnp.dot(c_proj, b_proj.T, preferred_element_type=fl)
    weights = (scores[None] * masked).astype(half)
    state_half = state_in.astype(half)
    adjoint_half = adjoint_in.astype(half)
    output = jnp.einsum("hts,shp->thp", weights, x_heads, preferred_element_type=fl)
    output = (
        output
        + jnp.einsum("tn,hpn->thp", c_proj, state_half, preferred_element_type=fl)
        * head_factor[:, :, None]
    )
    ssd_output = output.reshape(1, tok_rows, inner_width).astype(half)
    grad_x = jnp.einsum("hts,thp->shp", weights, grad_heads, preferred_element_type=fl)
    grad_x = (
        grad_x
        + jnp.einsum("sn,hpn->shp", b_proj, adjoint_half, preferred_element_type=fl)
        * tail_factor[:, :, None]
    )
    pair_scores = jnp.einsum("thp,shp->hts", grad_heads, x_heads, preferred_element_type=fl)
    pair_mixed = jnp.sum(pair_scores * masked, axis=0).astype(half)
    grad_b = jnp.dot(pair_mixed.T, c_proj, preferred_element_type=fl)
    grad_b = grad_b + jnp.einsum("shp,hpn->sn", x_weighted, adjoint_half, preferred_element_type=fl)
    grad_c = jnp.dot(pair_mixed, b_proj, preferred_element_type=fl)
    grad_c = grad_c + jnp.einsum(
        "thp,hpn->tn", grad_weighted, state_half, preferred_element_type=fl
    )
    grad_rows = jnp.concatenate(
        [
            grad_x.reshape(tok_rows, inner_width).astype(half),
            grad_b.astype(half),
            grad_c.astype(half),
        ],
        axis=1,
    )
    local_grad = jnp.einsum("tf,tw->fw", features, grad_rows, preferred_element_type=fl)
    share_grad = lax.psum_scatter(local_grad, "series", scatter_dimension=1, tiled=True)
    share_grad = lax.psum(share_grad, "tm")
    total_grad = lax.all_gather(share_grad, "series", axis=1, tiled=True)
    grad_in = total_grad / math.sqrt(series_count * seq_len)
    return (ssd_output, grad_in)


def solution(mesh):
    return jax.shard_map(
        on_device,
        mesh=mesh,
        in_specs=(P(None, ("tm", "series")), P(), P(), P(), P(), P(), P(), P("series", "tm", None)),
        out_specs=(P("series", "tm", None), P()),
        check_vma=False,
    )
```

```python
import math

import jax
import jax.numpy as jnp
from jax import lax
from jax.sharding import PartitionSpec as P

code_ceiling = 2097152.0


def decay_matrix(cum_decay):
    row_count = cum_decay.shape[0]
    causal = jnp.arange(row_count)[:, None] >= jnp.arange(row_count)[None, :]
    log_span = cum_decay.T[:, :, None] - cum_decay.T[:, None, :]
    return jnp.where(causal[None], jnp.exp(jnp.where(causal[None], log_span, -60.0)), 0.0)


def on_device(codes, owner_slot, edges, w_in, w_dt, dt_bias, decay_rate, grad_out):
    fl = jnp.float32
    half = jnp.bfloat16
    tok_rows = grad_out.shape[1]
    head_count = dt_bias.shape[0]
    inner_width = grad_out.shape[2]
    head_dim = inner_width // head_count
    state_dim = (w_in.shape[1] - inner_width) // 2
    n_blocks = lax.axis_size("tm")
    seq_len = tok_rows * n_blocks
    series_count = lax.axis_size("series")
    my_block = lax.axis_index("tm")

    ordered = jnp.take(codes, owner_slot, axis=0).astype(fl)
    own_block = lax.all_to_all(ordered, "series", split_axis=0, concat_axis=1, tiled=True)
    reading = lax.all_gather(own_block, "tm", axis=1, tiled=True)[0]
    edge_float = edges.astype(fl)
    upper_edge = jnp.concatenate([edge_float[1:], jnp.full((1,), code_ceiling, fl)])
    onehot = (
        (edge_float[None, :] <= reading[:, None]) & (upper_edge[None, :] > reading[:, None])
    ).astype(fl)
    counts = jnp.sum(onehot, axis=0)
    before = jnp.cumsum(counts) - counts
    bin_table = jnp.stack([before, counts, edge_float, upper_edge - edge_float], axis=1)
    picked = jnp.dot(onehot, bin_table, precision=lax.Precision.HIGHEST)
    within_bin = (reading - picked[:, 2]) / picked[:, 3]
    quantile = (picked[:, 0] + picked[:, 1] * within_bin) / seq_len
    frequency = (jnp.arange(w_in.shape[0], dtype=fl) + 0.5) * math.pi
    features_all = jnp.cos(quantile[:, None] * frequency).astype(half)

    def mine(a):
        return lax.dynamic_index_in_dim(a, my_block, axis=0, keepdims=False)

    features_blocks = features_all.reshape(n_blocks, tok_rows, -1)
    features = mine(features_blocks)
    projected = jnp.dot(features, w_in, preferred_element_type=fl).astype(half)
    x_heads = projected[:, :inner_width].reshape(tok_rows, head_count, head_dim)
    b_proj = projected[:, inner_width : inner_width + state_dim]
    c_proj = projected[:, inner_width + state_dim :]
    step_size = jax.nn.softplus(dt_bias + jnp.dot(features, w_dt, preferred_element_type=fl))
    cum_decay = jnp.cumsum(-step_size * decay_rate, axis=0)
    tail_factor = jnp.exp(cum_decay[-1][None, :] - cum_decay) * step_size
    head_factor = jnp.exp(cum_decay)
    x_weighted = (x_heads * tail_factor[:, :, None]).astype(half)

    projected_all = jnp.dot(features_all, w_in, preferred_element_type=fl).astype(half)
    projected_all = projected_all.reshape(n_blocks, tok_rows, -1)
    x_all = projected_all[:, :, :inner_width].reshape(n_blocks, tok_rows, head_count, head_dim)
    b_all = projected_all[:, :, inner_width : inner_width + state_dim]
    step_all = jax.nn.softplus(
        dt_bias + jnp.dot(features_all, w_dt, preferred_element_type=fl)
    ).reshape(n_blocks, tok_rows, head_count)
    cum_all = jnp.cumsum(-step_all * decay_rate, axis=1)
    gate_all = jnp.exp(cum_all[:, -1])
    tail_all = jnp.exp(cum_all[:, -1:, :] - cum_all) * step_all
    xw_all = (x_all * tail_all[..., None]).astype(half)
    state_local_all = jnp.einsum("bthp,btn->bhpn", xw_all, b_all, preferred_element_type=fl)

    state_in = jnp.zeros((head_count, head_dim, state_dim), fl)
    for k in range(n_blocks - 1):
        new = gate_all[k][:, None, None] * state_in + state_local_all[k]
        state_in = jnp.where(k < my_block, new, state_in)

    grad_heads = grad_out[0].reshape(tok_rows, head_count, head_dim)
    grad_weighted = (grad_heads * head_factor[:, :, None]).astype(half)
    adjoint_local = jnp.einsum("thp,tn->hpn", grad_weighted, c_proj, preferred_element_type=fl)
    adjoint_all = lax.all_gather(adjoint_local, "tm")
    adjoint_in = jnp.zeros((head_count, head_dim, state_dim), fl)
    for k in range(n_blocks - 1, 0, -1):
        new = gate_all[k][:, None, None] * adjoint_in + adjoint_all[k]
        adjoint_in = jnp.where(k > my_block, new, adjoint_in)

    masked = decay_matrix(cum_decay) * step_size.T[:, None, :]
    scores = jnp.dot(c_proj, b_proj.T, preferred_element_type=fl)
    weights = (scores[None] * masked).astype(half)
    state_half = state_in.astype(half)
    adjoint_half = adjoint_in.astype(half)
    output = jnp.einsum("hts,shp->thp", weights, x_heads, preferred_element_type=fl)
    output = (
        output
        + jnp.einsum("tn,hpn->thp", c_proj, state_half, preferred_element_type=fl)
        * head_factor[:, :, None]
    )
    ssd_output = output.reshape(1, tok_rows, inner_width).astype(half)
    grad_x = jnp.einsum("hts,thp->shp", weights, grad_heads, preferred_element_type=fl)
    grad_x = (
        grad_x
        + jnp.einsum("sn,hpn->shp", b_proj, adjoint_half, preferred_element_type=fl)
        * tail_factor[:, :, None]
    )
    pair_scores = jnp.einsum("thp,shp->hts", grad_heads, x_heads, preferred_element_type=fl)
    pair_mixed = jnp.sum(pair_scores * masked, axis=0).astype(half)
    grad_b = jnp.dot(pair_mixed.T, c_proj, preferred_element_type=fl)
    grad_b = grad_b + jnp.einsum("shp,hpn->sn", x_weighted, adjoint_half, preferred_element_type=fl)
    grad_c = jnp.dot(pair_mixed, b_proj, preferred_element_type=fl)
    grad_c = grad_c + jnp.einsum(
        "thp,hpn->tn", grad_weighted, state_half, preferred_element_type=fl
    )
    grad_rows = jnp.concatenate(
        [
            grad_x.reshape(tok_rows, inner_width).astype(half),
            grad_b.astype(half),
            grad_c.astype(half),
        ],
        axis=1,
    )
    local_grad = jnp.einsum("tf,tw->fw", features, grad_rows, preferred_element_type=fl)
    share_grad = lax.psum_scatter(local_grad, "series", scatter_dimension=1, tiled=True)
    share_grad = lax.psum(share_grad, "tm")
    total_grad = lax.all_gather(share_grad, "series", axis=1, tiled=True)
    grad_in = total_grad / math.sqrt(series_count * seq_len)
    return (ssd_output, grad_in)


def solution(mesh):
    return jax.shard_map(
        on_device,
        mesh=mesh,
        in_specs=(P(None, ("tm", "series")), P(), P(), P(), P(), P(), P(), P("series", "tm", None)),
        out_specs=(P("series", "tm", None), P()),
        check_vma=False,
    )
```

```python
import math

import jax
import jax.numpy as jnp
from jax import lax
from jax.sharding import PartitionSpec as P

code_ceiling = 2097152.0


def decay_matrix(cum_decay):
    row_count = cum_decay.shape[0]
    causal = jnp.arange(row_count)[:, None] >= jnp.arange(row_count)[None, :]
    log_span = cum_decay.T[:, :, None] - cum_decay.T[:, None, :]
    return jnp.where(causal[None], jnp.exp(jnp.where(causal[None], log_span, -60.0)), 0.0)


def axis_bits(axis):
    size = lax.axis_size(axis)
    assert size & (size - 1) == 0
    return [1 << k for k in range(size.bit_length() - 1)]


def exchange(value, axis, bit):
    pairs = [(i, i ^ bit) for i in range(lax.axis_size(axis))]
    return lax.ppermute(value, axis, pairs)


def tree_psum(value):
    steps = [("series", 1)] + [("tm", b) for b in axis_bits("tm")]
    steps += [("series", b) for b in axis_bits("series") if b > 1]
    done = []
    for axis, bit in steps:
        rows = value.shape[0]
        if rows % 16 == 0:
            upper = (lax.axis_index(axis) // bit) % 2
            keep = lax.dynamic_slice_in_dim(value, upper * (rows // 2), rows // 2)
            send = lax.dynamic_slice_in_dim(value, (1 - upper) * (rows // 2), rows // 2)
            value = keep + exchange(send, axis, bit)
            done.append((axis, bit, upper))
        else:
            value = value + exchange(value, axis, bit)
    for axis, bit, upper in reversed(done):
        other = exchange(value, axis, bit)
        value = jnp.where(
            upper == 1,
            jnp.concatenate([other, value]),
            jnp.concatenate([value, other]),
        )
    return value


def on_device(codes, owner_slot, edges, w_in, w_dt, dt_bias, decay_rate, grad_out):
    fl = jnp.float32
    half = jnp.bfloat16
    tok_rows = grad_out.shape[1]
    head_count = dt_bias.shape[0]
    inner_width = grad_out.shape[2]
    head_dim = inner_width // head_count
    state_dim = (w_in.shape[1] - inner_width) // 2
    n_blocks = lax.axis_size("tm")
    seq_len = tok_rows * n_blocks
    series_count = lax.axis_size("series")
    my_block = lax.axis_index("tm")

    ordered = jnp.take(codes, owner_slot, axis=0).astype(fl)
    own_block = lax.all_to_all(ordered, "series", split_axis=0, concat_axis=1, tiled=True)
    reading = lax.all_gather(own_block, "tm", axis=1, tiled=True)[0]
    edge_float = edges.astype(fl)
    upper_edge = jnp.concatenate([edge_float[1:], jnp.full((1,), code_ceiling, fl)])
    onehot = (
        (edge_float[None, :] <= reading[:, None]) & (upper_edge[None, :] > reading[:, None])
    ).astype(fl)
    counts = jnp.sum(onehot, axis=0)
    before = jnp.cumsum(counts) - counts
    bin_table = jnp.stack([before, counts, edge_float, upper_edge - edge_float], axis=1)
    picked = jnp.dot(onehot, bin_table, precision=lax.Precision.HIGHEST)
    within_bin = (reading - picked[:, 2]) / picked[:, 3]
    quantile = (picked[:, 0] + picked[:, 1] * within_bin) / seq_len
    frequency = (jnp.arange(w_in.shape[0], dtype=fl) + 0.5) * math.pi
    features_all = jnp.cos(quantile[:, None] * frequency).astype(half)

    def mine(a):
        return lax.dynamic_index_in_dim(a, my_block, axis=0, keepdims=False)

    features_blocks = features_all.reshape(n_blocks, tok_rows, -1)
    features = mine(features_blocks)
    projected = jnp.dot(features, w_in, preferred_element_type=fl).astype(half)
    x_heads = projected[:, :inner_width].reshape(tok_rows, head_count, head_dim)
    b_proj = projected[:, inner_width : inner_width + state_dim]
    c_proj = projected[:, inner_width + state_dim :]
    step_size = jax.nn.softplus(dt_bias + jnp.dot(features, w_dt, preferred_element_type=fl))
    cum_decay = jnp.cumsum(-step_size * decay_rate, axis=0)
    tail_factor = jnp.exp(cum_decay[-1][None, :] - cum_decay) * step_size
    head_factor = jnp.exp(cum_decay)
    x_weighted = (x_heads * tail_factor[:, :, None]).astype(half)

    projected_all = jnp.dot(features_all, w_in, preferred_element_type=fl).astype(half)
    projected_all = projected_all.reshape(n_blocks, tok_rows, -1)
    x_all = projected_all[:, :, :inner_width].reshape(n_blocks, tok_rows, head_count, head_dim)
    b_all = projected_all[:, :, inner_width : inner_width + state_dim]
    step_all = jax.nn.softplus(
        dt_bias + jnp.dot(features_all, w_dt, preferred_element_type=fl)
    ).reshape(n_blocks, tok_rows, head_count)
    cum_all = jnp.cumsum(-step_all * decay_rate, axis=1)
    gate_all = jnp.exp(cum_all[:, -1])
    tail_all = jnp.exp(cum_all[:, -1:, :] - cum_all) * step_all
    xw_all = (x_all * tail_all[..., None]).astype(half)
    state_local_all = jnp.einsum("bthp,btn->bhpn", xw_all, b_all, preferred_element_type=fl)

    state_in = jnp.zeros((head_count, head_dim, state_dim), fl)
    for k in range(n_blocks - 1):
        new = gate_all[k][:, None, None] * state_in + state_local_all[k]
        state_in = jnp.where(k < my_block, new, state_in)

    grad_heads = grad_out[0].reshape(tok_rows, head_count, head_dim)
    grad_weighted = (grad_heads * head_factor[:, :, None]).astype(half)
    adjoint_local = jnp.einsum("thp,tn->hpn", grad_weighted, c_proj, preferred_element_type=fl)
    adjoint_all = lax.all_gather(adjoint_local, "tm")
    adjoint_in = jnp.zeros((head_count, head_dim, state_dim), fl)
    for k in range(n_blocks - 1, 0, -1):
        new = gate_all[k][:, None, None] * adjoint_in + adjoint_all[k]
        adjoint_in = jnp.where(k > my_block, new, adjoint_in)

    masked = decay_matrix(cum_decay) * step_size.T[:, None, :]
    scores = jnp.dot(c_proj, b_proj.T, preferred_element_type=fl)
    weights = (scores[None] * masked).astype(half)
    state_half = state_in.astype(half)
    adjoint_half = adjoint_in.astype(half)
    output = jnp.einsum("hts,shp->thp", weights, x_heads, preferred_element_type=fl)
    output = (
        output
        + jnp.einsum("tn,hpn->thp", c_proj, state_half, preferred_element_type=fl)
        * head_factor[:, :, None]
    )
    ssd_output = output.reshape(1, tok_rows, inner_width).astype(half)
    grad_x = jnp.einsum("hts,thp->shp", weights, grad_heads, preferred_element_type=fl)
    grad_x = (
        grad_x
        + jnp.einsum("sn,hpn->shp", b_proj, adjoint_half, preferred_element_type=fl)
        * tail_factor[:, :, None]
    )
    pair_scores = jnp.einsum("thp,shp->hts", grad_heads, x_heads, preferred_element_type=fl)
    pair_mixed = jnp.sum(pair_scores * masked, axis=0).astype(half)
    grad_b = jnp.dot(pair_mixed.T, c_proj, preferred_element_type=fl)
    grad_b = grad_b + jnp.einsum("shp,hpn->sn", x_weighted, adjoint_half, preferred_element_type=fl)
    grad_c = jnp.dot(pair_mixed, b_proj, preferred_element_type=fl)
    grad_c = grad_c + jnp.einsum(
        "thp,hpn->tn", grad_weighted, state_half, preferred_element_type=fl
    )
    grad_rows = jnp.concatenate(
        [
            grad_x.reshape(tok_rows, inner_width).astype(half),
            grad_b.astype(half),
            grad_c.astype(half),
        ],
        axis=1,
    )
    local_grad = jnp.einsum("tw,tf->wf", grad_rows, features, preferred_element_type=fl)
    total_grad = tree_psum(local_grad).T
    grad_in = total_grad / math.sqrt(series_count * seq_len)
    return (ssd_output, grad_in)


def solution(mesh):
    return jax.shard_map(
        on_device,
        mesh=mesh,
        in_specs=(P(None, ("tm", "series")), P(), P(), P(), P(), P(), P(), P("series", "tm", None)),
        out_specs=(P("series", "tm", None), P()),
        check_vma=False,
    )
```

```python
import math

import jax
import jax.numpy as jnp
from jax import lax
from jax.sharding import PartitionSpec as P

code_ceiling = 2097152.0


def decay_matrix(cum_decay):
    row_count = cum_decay.shape[0]
    causal = jnp.arange(row_count)[:, None] >= jnp.arange(row_count)[None, :]
    log_span = cum_decay.T[:, :, None] - cum_decay.T[:, None, :]
    return jnp.where(causal[None], jnp.exp(jnp.where(causal[None], log_span, -60.0)), 0.0)


def axis_bits(axis):
    size = lax.axis_size(axis)
    assert size & (size - 1) == 0
    return [1 << k for k in range(size.bit_length() - 1)]


def exchange(value, axis, bit):
    pairs = [(i, i ^ bit) for i in range(lax.axis_size(axis))]
    return lax.ppermute(value, axis, pairs)


def tree_psum(value):
    steps = [("series", 1)] + [("tm", b) for b in axis_bits("tm")]
    steps += [("series", b) for b in axis_bits("series") if b > 1]
    done = []
    for axis, bit in steps:
        rows = value.shape[0]
        if rows % 16 == 0:
            upper = (lax.axis_index(axis) // bit) % 2
            keep = lax.dynamic_slice_in_dim(value, upper * (rows // 2), rows // 2)
            send = lax.dynamic_slice_in_dim(value, (1 - upper) * (rows // 2), rows // 2)
            value = keep + exchange(send, axis, bit)
            done.append((axis, bit, upper))
        else:
            value = value + exchange(value, axis, bit)
    for axis, bit, upper in reversed(done):
        other = exchange(value, axis, bit)
        value = jnp.where(
            upper == 1,
            jnp.concatenate([other, value]),
            jnp.concatenate([value, other]),
        )
    return value


def on_device(codes, owner_slot, edges, w_in, w_dt, dt_bias, decay_rate, grad_out):
    fl = jnp.float32
    half = jnp.bfloat16
    tok_rows = grad_out.shape[1]
    head_count = dt_bias.shape[0]
    inner_width = grad_out.shape[2]
    head_dim = inner_width // head_count
    state_dim = (w_in.shape[1] - inner_width) // 2
    n_blocks = lax.axis_size("tm")
    seq_len = tok_rows * n_blocks
    series_count = lax.axis_size("series")
    my_block = lax.axis_index("tm")

    ordered = jnp.take(codes, owner_slot, axis=0).astype(fl)
    outgoing = jnp.tile(ordered, (n_blocks, 1))
    reading = lax.all_to_all(outgoing, ("tm", "series"), split_axis=0, concat_axis=1, tiled=True)[0]
    edge_float = edges.astype(fl)
    upper_edge = jnp.concatenate([edge_float[1:], jnp.full((1,), code_ceiling, fl)])
    onehot = (
        (edge_float[None, :] <= reading[:, None]) & (upper_edge[None, :] > reading[:, None])
    ).astype(fl)
    counts = jnp.sum(onehot, axis=0)
    before = jnp.cumsum(counts) - counts
    bin_table = jnp.stack([before, counts, edge_float, upper_edge - edge_float], axis=1)
    picked = jnp.dot(onehot, bin_table, precision=lax.Precision.HIGHEST)
    within_bin = (reading - picked[:, 2]) / picked[:, 3]
    quantile = (picked[:, 0] + picked[:, 1] * within_bin) / seq_len
    frequency = (jnp.arange(w_in.shape[0], dtype=fl) + 0.5) * math.pi
    features_all = jnp.cos(quantile[:, None] * frequency).astype(half)

    def mine(a):
        return lax.dynamic_index_in_dim(a, my_block, axis=0, keepdims=False)

    features_blocks = features_all.reshape(n_blocks, tok_rows, -1)
    features = mine(features_blocks)
    projected = jnp.dot(features, w_in, preferred_element_type=fl).astype(half)
    x_heads = projected[:, :inner_width].reshape(tok_rows, head_count, head_dim)
    b_proj = projected[:, inner_width : inner_width + state_dim]
    c_proj = projected[:, inner_width + state_dim :]
    step_size = jax.nn.softplus(dt_bias + jnp.dot(features, w_dt, preferred_element_type=fl))
    cum_decay = jnp.cumsum(-step_size * decay_rate, axis=0)
    tail_factor = jnp.exp(cum_decay[-1][None, :] - cum_decay) * step_size
    head_factor = jnp.exp(cum_decay)
    x_weighted = (x_heads * tail_factor[:, :, None]).astype(half)

    projected_all = jnp.dot(features_all, w_in, preferred_element_type=fl).astype(half)
    projected_all = projected_all.reshape(n_blocks, tok_rows, -1)
    x_all = projected_all[:, :, :inner_width].reshape(n_blocks, tok_rows, head_count, head_dim)
    b_all = projected_all[:, :, inner_width : inner_width + state_dim]
    step_all = jax.nn.softplus(
        dt_bias + jnp.dot(features_all, w_dt, preferred_element_type=fl)
    ).reshape(n_blocks, tok_rows, head_count)
    cum_all = jnp.cumsum(-step_all * decay_rate, axis=1)
    gate_all = jnp.exp(cum_all[:, -1])
    tail_all = jnp.exp(cum_all[:, -1:, :] - cum_all) * step_all
    xw_all = (x_all * tail_all[..., None]).astype(half)
    state_local_all = jnp.einsum("bthp,btn->bhpn", xw_all, b_all, preferred_element_type=fl)

    state_in = jnp.zeros((head_count, head_dim, state_dim), fl)
    for k in range(n_blocks - 1):
        new = gate_all[k][:, None, None] * state_in + state_local_all[k]
        state_in = jnp.where(k < my_block, new, state_in)

    grad_heads = grad_out[0].reshape(tok_rows, head_count, head_dim)
    grad_weighted = (grad_heads * head_factor[:, :, None]).astype(half)
    adjoint_local = jnp.einsum("thp,tn->hpn", grad_weighted, c_proj, preferred_element_type=fl)
    adjoint_all = lax.all_gather(adjoint_local, "tm")
    adjoint_in = jnp.zeros((head_count, head_dim, state_dim), fl)
    for k in range(n_blocks - 1, 0, -1):
        new = gate_all[k][:, None, None] * adjoint_in + adjoint_all[k]
        adjoint_in = jnp.where(k > my_block, new, adjoint_in)

    masked = decay_matrix(cum_decay) * step_size.T[:, None, :]
    scores = jnp.dot(c_proj, b_proj.T, preferred_element_type=fl)
    weights = (scores[None] * masked).astype(half)
    state_half = state_in.astype(half)
    adjoint_half = adjoint_in.astype(half)
    output = jnp.einsum("hts,shp->thp", weights, x_heads, preferred_element_type=fl)
    output = (
        output
        + jnp.einsum("tn,hpn->thp", c_proj, state_half, preferred_element_type=fl)
        * head_factor[:, :, None]
    )
    ssd_output = output.reshape(1, tok_rows, inner_width).astype(half)
    grad_x = jnp.einsum("hts,thp->shp", weights, grad_heads, preferred_element_type=fl)
    grad_x = (
        grad_x
        + jnp.einsum("sn,hpn->shp", b_proj, adjoint_half, preferred_element_type=fl)
        * tail_factor[:, :, None]
    )
    pair_scores = jnp.einsum("thp,shp->hts", grad_heads, x_heads, preferred_element_type=fl)
    pair_mixed = jnp.sum(pair_scores * masked, axis=0).astype(half)
    grad_b = jnp.dot(pair_mixed.T, c_proj, preferred_element_type=fl)
    grad_b = grad_b + jnp.einsum("shp,hpn->sn", x_weighted, adjoint_half, preferred_element_type=fl)
    grad_c = jnp.dot(pair_mixed, b_proj, preferred_element_type=fl)
    grad_c = grad_c + jnp.einsum(
        "thp,hpn->tn", grad_weighted, state_half, preferred_element_type=fl
    )
    grad_rows = jnp.concatenate(
        [
            grad_x.reshape(tok_rows, inner_width).astype(half),
            grad_b.astype(half),
            grad_c.astype(half),
        ],
        axis=1,
    )
    local_grad = jnp.einsum("tw,tf->wf", grad_rows, features, preferred_element_type=fl)
    total_grad = tree_psum(local_grad).T
    grad_in = total_grad / math.sqrt(series_count * seq_len)
    return (ssd_output, grad_in)


def solution(mesh):
    return jax.shard_map(
        on_device,
        mesh=mesh,
        in_specs=(P(None, ("tm", "series")), P(), P(), P(), P(), P(), P(), P("series", "tm", None)),
        out_specs=(P("series", "tm", None), P()),
        check_vma=False,
    )
```

```python
import math

import jax
import jax.numpy as jnp
from jax import lax
from jax.sharding import PartitionSpec as P

code_ceiling = 2097152.0


def decay_matrix(cum_decay):
    row_count = cum_decay.shape[0]
    causal = jnp.arange(row_count)[:, None] >= jnp.arange(row_count)[None, :]
    log_span = cum_decay.T[:, :, None] - cum_decay.T[:, None, :]
    return jnp.where(causal[None], jnp.exp(jnp.where(causal[None], log_span, -60.0)), 0.0)


def axis_bits(axis):
    size = lax.axis_size(axis)
    assert size & (size - 1) == 0
    return [1 << k for k in range(size.bit_length() - 1)]


def exchange(value, axis, flip):
    pairs = [(i, i ^ flip) for i in range(lax.axis_size(axis))]
    return lax.ppermute(value, axis, pairs)


def bit_groups():
    tm_bits, series_bits = axis_bits("tm"), axis_bits("series")
    groups = [("series", series_bits[:1])] if series_bits else []
    for axis, bits in (("tm", tm_bits), ("series", series_bits[1:])):
        groups += [(axis, bits[i : i + 2]) for i in range(0, len(bits), 2)]
    return groups


def group_round(value, axis, bits, scatter):
    index = lax.axis_index(axis)
    coord = sum(((index // b) % 2) * (1 << j) for j, b in enumerate(bits))
    size = 1 << len(bits)

    def flip_of(m):
        return sum(b for j, b in enumerate(bits) if (m >> j) & 1)

    rows = value.shape[0]
    if scatter:
        part = rows // size
        keep = lax.dynamic_slice_in_dim(value, coord * part, part)
        got = [
            exchange(lax.dynamic_slice_in_dim(value, (coord ^ m) * part, part), axis, flip_of(m))
            for m in range(1, size)
        ]
        for piece in got:
            keep = keep + piece
        return keep
    got = [value] + [exchange(value, axis, flip_of(m)) for m in range(1, size)]
    stacked = jnp.stack(got)
    return [lax.dynamic_index_in_dim(stacked, coord ^ q, 0, keepdims=False) for q in range(size)]


def tree_psum(value):
    done = []
    for axis, bits in bit_groups():
        if value.shape[0] % (8 << len(bits)) == 0:
            value = group_round(value, axis, bits, True)
            done.append((axis, bits))
        else:
            pieces = group_round(value, axis, bits, False)
            value = pieces[0]
            for piece in pieces[1:]:
                value = value + piece
    for axis, bits in reversed(done):
        value = jnp.concatenate(group_round(value, axis, bits, False))
    return value


def on_device(codes, owner_slot, edges, w_in, w_dt, dt_bias, decay_rate, grad_out):
    fl = jnp.float32
    half = jnp.bfloat16
    tok_rows = grad_out.shape[1]
    head_count = dt_bias.shape[0]
    inner_width = grad_out.shape[2]
    head_dim = inner_width // head_count
    state_dim = (w_in.shape[1] - inner_width) // 2
    n_blocks = lax.axis_size("tm")
    seq_len = tok_rows * n_blocks
    series_count = lax.axis_size("series")
    my_block = lax.axis_index("tm")

    ordered = jnp.take(codes, owner_slot, axis=0).astype(fl)
    outgoing = jnp.tile(ordered, (n_blocks, 1))
    reading = lax.all_to_all(outgoing, ("tm", "series"), split_axis=0, concat_axis=1, tiled=True)[0]
    edge_float = edges.astype(fl)
    upper_edge = jnp.concatenate([edge_float[1:], jnp.full((1,), code_ceiling, fl)])
    onehot = (
        (edge_float[None, :] <= reading[:, None]) & (upper_edge[None, :] > reading[:, None])
    ).astype(fl)
    counts = jnp.sum(onehot, axis=0)
    before = jnp.cumsum(counts) - counts
    bin_table = jnp.stack([before, counts, edge_float, upper_edge - edge_float], axis=1)
    picked = jnp.dot(onehot, bin_table, precision=lax.Precision.HIGHEST)
    within_bin = (reading - picked[:, 2]) / picked[:, 3]
    quantile = (picked[:, 0] + picked[:, 1] * within_bin) / seq_len
    frequency = (jnp.arange(w_in.shape[0], dtype=fl) + 0.5) * math.pi
    features_all = jnp.cos(quantile[:, None] * frequency).astype(half)

    def mine(a):
        return lax.dynamic_index_in_dim(a, my_block, axis=0, keepdims=False)

    features_blocks = features_all.reshape(n_blocks, tok_rows, -1)
    features = mine(features_blocks)
    projected = jnp.dot(features, w_in, preferred_element_type=fl).astype(half)
    x_heads = projected[:, :inner_width].reshape(tok_rows, head_count, head_dim)
    b_proj = projected[:, inner_width : inner_width + state_dim]
    c_proj = projected[:, inner_width + state_dim :]
    step_size = jax.nn.softplus(dt_bias + jnp.dot(features, w_dt, preferred_element_type=fl))
    cum_decay = jnp.cumsum(-step_size * decay_rate, axis=0)
    tail_factor = jnp.exp(cum_decay[-1][None, :] - cum_decay) * step_size
    head_factor = jnp.exp(cum_decay)
    x_weighted = (x_heads * tail_factor[:, :, None]).astype(half)

    projected_all = jnp.dot(features_all, w_in, preferred_element_type=fl).astype(half)
    projected_all = projected_all.reshape(n_blocks, tok_rows, -1)
    x_all = projected_all[:, :, :inner_width].reshape(n_blocks, tok_rows, head_count, head_dim)
    b_all = projected_all[:, :, inner_width : inner_width + state_dim]
    step_all = jax.nn.softplus(
        dt_bias + jnp.dot(features_all, w_dt, preferred_element_type=fl)
    ).reshape(n_blocks, tok_rows, head_count)
    cum_all = jnp.cumsum(-step_all * decay_rate, axis=1)
    gate_all = jnp.exp(cum_all[:, -1])
    tail_all = jnp.exp(cum_all[:, -1:, :] - cum_all) * step_all
    xw_all = (x_all * tail_all[..., None]).astype(half)
    state_local_all = jnp.einsum("bthp,btn->bhpn", xw_all, b_all, preferred_element_type=fl)

    state_in = jnp.zeros((head_count, head_dim, state_dim), fl)
    for k in range(n_blocks - 1):
        new = gate_all[k][:, None, None] * state_in + state_local_all[k]
        state_in = jnp.where(k < my_block, new, state_in)

    grad_heads = grad_out[0].reshape(tok_rows, head_count, head_dim)
    grad_weighted = (grad_heads * head_factor[:, :, None]).astype(half)
    adjoint_local = jnp.einsum("thp,tn->hpn", grad_weighted, c_proj, preferred_element_type=fl)
    adjoint_all = lax.all_gather(adjoint_local, "tm")
    adjoint_in = jnp.zeros((head_count, head_dim, state_dim), fl)
    for k in range(n_blocks - 1, 0, -1):
        new = gate_all[k][:, None, None] * adjoint_in + adjoint_all[k]
        adjoint_in = jnp.where(k > my_block, new, adjoint_in)

    masked = decay_matrix(cum_decay) * step_size.T[:, None, :]
    scores = jnp.dot(c_proj, b_proj.T, preferred_element_type=fl)
    weights = (scores[None] * masked).astype(half)
    state_half = state_in.astype(half)
    adjoint_half = adjoint_in.astype(half)
    output = jnp.einsum("hts,shp->thp", weights, x_heads, preferred_element_type=fl)
    output = (
        output
        + jnp.einsum("tn,hpn->thp", c_proj, state_half, preferred_element_type=fl)
        * head_factor[:, :, None]
    )
    ssd_output = output.reshape(1, tok_rows, inner_width).astype(half)
    grad_x = jnp.einsum("hts,thp->shp", weights, grad_heads, preferred_element_type=fl)
    grad_x = (
        grad_x
        + jnp.einsum("sn,hpn->shp", b_proj, adjoint_half, preferred_element_type=fl)
        * tail_factor[:, :, None]
    )
    pair_scores = jnp.einsum("thp,shp->hts", grad_heads, x_heads, preferred_element_type=fl)
    pair_mixed = jnp.sum(pair_scores * masked, axis=0).astype(half)
    grad_b = jnp.dot(pair_mixed.T, c_proj, preferred_element_type=fl)
    grad_b = grad_b + jnp.einsum("shp,hpn->sn", x_weighted, adjoint_half, preferred_element_type=fl)
    grad_c = jnp.dot(pair_mixed, b_proj, preferred_element_type=fl)
    grad_c = grad_c + jnp.einsum(
        "thp,hpn->tn", grad_weighted, state_half, preferred_element_type=fl
    )
    grad_rows = jnp.concatenate(
        [
            grad_x.reshape(tok_rows, inner_width).astype(half),
            grad_b.astype(half),
            grad_c.astype(half),
        ],
        axis=1,
    )
    local_grad = jnp.einsum("tw,tf->wf", grad_rows, features, preferred_element_type=fl)
    total_grad = tree_psum(local_grad).T
    grad_in = total_grad / math.sqrt(series_count * seq_len)
    return (ssd_output, grad_in)


def solution(mesh):
    return jax.shard_map(
        on_device,
        mesh=mesh,
        in_specs=(P(None, ("tm", "series")), P(), P(), P(), P(), P(), P(), P("series", "tm", None)),
        out_specs=(P("series", "tm", None), P()),
        check_vma=False,
    )
```

```python
import math

import jax
import jax.numpy as jnp
from jax import lax
from jax.sharding import PartitionSpec as P

code_ceiling = 2097152.0


def decay_matrix(cum_decay):
    row_count = cum_decay.shape[0]
    causal = jnp.arange(row_count)[:, None] >= jnp.arange(row_count)[None, :]
    log_span = cum_decay.T[:, :, None] - cum_decay.T[:, None, :]
    return jnp.where(causal[None], jnp.exp(jnp.where(causal[None], log_span, -60.0)), 0.0)


ALL = ("tm", "series")


def exchange(value, flip):
    pairs = [(i, i ^ flip) for i in range(lax.axis_size(ALL))]
    return lax.ppermute(value, ALL, pairs)


def bit_groups(widest):
    size = lax.axis_size(ALL)
    assert size & (size - 1) == 0
    bits = [1 << k for k in range(size.bit_length() - 1)]
    return [bits[:1]] + [bits[i : i + widest] for i in range(1, len(bits), widest)]


def group_round(value, bits, scatter):
    index = lax.axis_index(ALL)
    coord = sum(((index // b) % 2) * (1 << j) for j, b in enumerate(bits))
    size = 1 << len(bits)

    def flip_of(m):
        return sum(b for j, b in enumerate(bits) if (m >> j) & 1)

    rows = value.shape[0]
    if scatter:
        part = rows // size
        keep = lax.dynamic_slice_in_dim(value, coord * part, part)
        got = [
            exchange(lax.dynamic_slice_in_dim(value, (coord ^ m) * part, part), flip_of(m))
            for m in range(1, size)
        ]
        for piece in got:
            keep = keep + piece
        return keep
    got = [value] + [exchange(value, flip_of(m)) for m in range(1, size)]
    stacked = jnp.stack(got)
    return [lax.dynamic_index_in_dim(stacked, coord ^ q, 0, keepdims=False) for q in range(size)]


def tree_psum(value, widest):
    done = []
    for bits in bit_groups(widest):
        if value.shape[0] % (8 << len(bits)) == 0:
            value = group_round(value, bits, True)
            done.append(bits)
        else:
            pieces = group_round(value, bits, False)
            value = pieces[0]
            for piece in pieces[1:]:
                value = value + piece
    for bits in reversed(done):
        value = jnp.concatenate(group_round(value, bits, False))
    return value


def on_device(codes, owner_slot, edges, w_in, w_dt, dt_bias, decay_rate, grad_out):
    fl = jnp.float32
    half = jnp.bfloat16
    tok_rows = grad_out.shape[1]
    head_count = dt_bias.shape[0]
    inner_width = grad_out.shape[2]
    head_dim = inner_width // head_count
    state_dim = (w_in.shape[1] - inner_width) // 2
    n_blocks = lax.axis_size("tm")
    seq_len = tok_rows * n_blocks
    series_count = lax.axis_size("series")
    my_block = lax.axis_index("tm")

    ordered = jnp.take(codes, owner_slot, axis=0).astype(fl)
    outgoing = jnp.tile(ordered, (n_blocks, 1))
    reading = lax.all_to_all(outgoing, ("tm", "series"), split_axis=0, concat_axis=1, tiled=True)[0]
    edge_float = edges.astype(fl)
    upper_edge = jnp.concatenate([edge_float[1:], jnp.full((1,), code_ceiling, fl)])
    onehot = (
        (edge_float[None, :] <= reading[:, None]) & (upper_edge[None, :] > reading[:, None])
    ).astype(fl)
    counts = jnp.sum(onehot, axis=0)
    before = jnp.cumsum(counts) - counts
    bin_table = jnp.stack([before, counts, edge_float, upper_edge - edge_float], axis=1)
    picked = jnp.dot(onehot, bin_table, precision=lax.Precision.HIGHEST)
    within_bin = (reading - picked[:, 2]) / picked[:, 3]
    quantile = (picked[:, 0] + picked[:, 1] * within_bin) / seq_len
    frequency = (jnp.arange(w_in.shape[0], dtype=fl) + 0.5) * math.pi
    features_all = jnp.cos(quantile[:, None] * frequency).astype(half)

    def mine(a):
        return lax.dynamic_index_in_dim(a, my_block, axis=0, keepdims=False)

    features_blocks = features_all.reshape(n_blocks, tok_rows, -1)
    features = mine(features_blocks)
    projected = jnp.dot(features, w_in, preferred_element_type=fl).astype(half)
    x_heads = projected[:, :inner_width].reshape(tok_rows, head_count, head_dim)
    b_proj = projected[:, inner_width : inner_width + state_dim]
    c_proj = projected[:, inner_width + state_dim :]
    step_size = jax.nn.softplus(dt_bias + jnp.dot(features, w_dt, preferred_element_type=fl))
    cum_decay = jnp.cumsum(-step_size * decay_rate, axis=0)
    tail_factor = jnp.exp(cum_decay[-1][None, :] - cum_decay) * step_size
    head_factor = jnp.exp(cum_decay)
    x_weighted = (x_heads * tail_factor[:, :, None]).astype(half)

    projected_all = jnp.dot(features_all, w_in, preferred_element_type=fl).astype(half)
    projected_all = projected_all.reshape(n_blocks, tok_rows, -1)
    x_all = projected_all[:, :, :inner_width].reshape(n_blocks, tok_rows, head_count, head_dim)
    b_all = projected_all[:, :, inner_width : inner_width + state_dim]
    step_all = jax.nn.softplus(
        dt_bias + jnp.dot(features_all, w_dt, preferred_element_type=fl)
    ).reshape(n_blocks, tok_rows, head_count)
    cum_all = jnp.cumsum(-step_all * decay_rate, axis=1)
    gate_all = jnp.exp(cum_all[:, -1])
    tail_all = jnp.exp(cum_all[:, -1:, :] - cum_all) * step_all
    xw_all = (x_all * tail_all[..., None]).astype(half)
    state_local_all = jnp.einsum("bthp,btn->bhpn", xw_all, b_all, preferred_element_type=fl)

    state_in = jnp.zeros((head_count, head_dim, state_dim), fl)
    for k in range(n_blocks - 1):
        new = gate_all[k][:, None, None] * state_in + state_local_all[k]
        state_in = jnp.where(k < my_block, new, state_in)

    grad_heads = grad_out[0].reshape(tok_rows, head_count, head_dim)
    grad_weighted = (grad_heads * head_factor[:, :, None]).astype(half)
    adjoint_local = jnp.einsum("thp,tn->hpn", grad_weighted, c_proj, preferred_element_type=fl)
    adjoint_all = lax.all_gather(adjoint_local, "tm")
    adjoint_in = jnp.zeros((head_count, head_dim, state_dim), fl)
    for k in range(n_blocks - 1, 0, -1):
        new = gate_all[k][:, None, None] * adjoint_in + adjoint_all[k]
        adjoint_in = jnp.where(k > my_block, new, adjoint_in)

    masked = decay_matrix(cum_decay) * step_size.T[:, None, :]
    scores = jnp.dot(c_proj, b_proj.T, preferred_element_type=fl)
    weights = (scores[None] * masked).astype(half)
    state_half = state_in.astype(half)
    adjoint_half = adjoint_in.astype(half)
    output = jnp.einsum("hts,shp->thp", weights, x_heads, preferred_element_type=fl)
    output = (
        output
        + jnp.einsum("tn,hpn->thp", c_proj, state_half, preferred_element_type=fl)
        * head_factor[:, :, None]
    )
    ssd_output = output.reshape(1, tok_rows, inner_width).astype(half)
    grad_x = jnp.einsum("hts,thp->shp", weights, grad_heads, preferred_element_type=fl)
    grad_x = (
        grad_x
        + jnp.einsum("sn,hpn->shp", b_proj, adjoint_half, preferred_element_type=fl)
        * tail_factor[:, :, None]
    )
    pair_scores = jnp.einsum("thp,shp->hts", grad_heads, x_heads, preferred_element_type=fl)
    pair_mixed = jnp.sum(pair_scores * masked, axis=0).astype(half)
    grad_b = jnp.dot(pair_mixed.T, c_proj, preferred_element_type=fl)
    grad_b = grad_b + jnp.einsum("shp,hpn->sn", x_weighted, adjoint_half, preferred_element_type=fl)
    grad_c = jnp.dot(pair_mixed, b_proj, preferred_element_type=fl)
    grad_c = grad_c + jnp.einsum(
        "thp,hpn->tn", grad_weighted, state_half, preferred_element_type=fl
    )
    grad_rows = jnp.concatenate(
        [
            grad_x.reshape(tok_rows, inner_width).astype(half),
            grad_b.astype(half),
            grad_c.astype(half),
        ],
        axis=1,
    )
    local_grad = jnp.einsum("tw,tf->wf", grad_rows, features, preferred_element_type=fl)
    total_grad = tree_psum(local_grad, 4).T
    grad_in = total_grad / math.sqrt(series_count * seq_len)
    return (ssd_output, grad_in)


def solution(mesh):
    return jax.shard_map(
        on_device,
        mesh=mesh,
        in_specs=(P(None, ("tm", "series")), P(), P(), P(), P(), P(), P(), P("series", "tm", None)),
        out_specs=(P("series", "tm", None), P()),
        check_vma=False,
    )
```

```python
import math

import jax
import jax.numpy as jnp
from jax import lax
from jax.sharding import PartitionSpec as P

code_ceiling = 2097152.0


def decay_matrix(cum_decay):
    row_count = cum_decay.shape[0]
    causal = jnp.arange(row_count)[:, None] >= jnp.arange(row_count)[None, :]
    log_span = cum_decay.T[:, :, None] - cum_decay.T[:, None, :]
    return jnp.where(causal[None], jnp.exp(jnp.where(causal[None], log_span, -60.0)), 0.0)


def axis_bits(axis):
    size = lax.axis_size(axis)
    assert size & (size - 1) == 0
    return [1 << k for k in range(size.bit_length() - 1)]


def exchange(value, axis, flip):
    pairs = [(i, i ^ flip) for i in range(lax.axis_size(axis))]
    return lax.ppermute(value, axis, pairs)


def bit_groups():
    tm_bits, series_bits = axis_bits("tm"), axis_bits("series")
    groups = [("series", series_bits[:1])] if series_bits else []
    for axis, bits in (("tm", tm_bits), ("series", series_bits[1:])):
        groups += [(axis, bits[i : i + 2]) for i in range(0, len(bits), 2)]
    return groups


def group_round(value, axis, bits, scatter):
    index = lax.axis_index(axis)
    coord = sum(((index // b) % 2) * (1 << j) for j, b in enumerate(bits))
    size = 1 << len(bits)

    def flip_of(m):
        return sum(b for j, b in enumerate(bits) if (m >> j) & 1)

    rows = value.shape[0]
    if scatter:
        part = rows // size
        keep = lax.dynamic_slice_in_dim(value, coord * part, part)
        got = [
            exchange(lax.dynamic_slice_in_dim(value, (coord ^ m) * part, part), axis, flip_of(m))
            for m in range(1, size)
        ]
        for piece in got:
            keep = keep + piece
        return keep
    got = [value] + [exchange(value, axis, flip_of(m)) for m in range(1, size)]
    stacked = jnp.stack(got)
    return [lax.dynamic_index_in_dim(stacked, coord ^ q, 0, keepdims=False) for q in range(size)]


def tree_psum(value):
    done = []
    for axis, bits in bit_groups():
        if value.shape[0] % (8 << len(bits)) == 0:
            value = group_round(value, axis, bits, True)
            done.append((axis, bits))
        else:
            pieces = group_round(value, axis, bits, False)
            value = pieces[0]
            for piece in pieces[1:]:
                value = value + piece
    for axis, bits in reversed(done):
        value = jnp.concatenate(group_round(value, axis, bits, False))
    return value


def on_device(codes, owner_slot, edges, w_in, w_dt, dt_bias, decay_rate, grad_out):
    fl = jnp.float32
    half = jnp.bfloat16
    tok_rows = grad_out.shape[1]
    head_count = dt_bias.shape[0]
    inner_width = grad_out.shape[2]
    head_dim = inner_width // head_count
    state_dim = (w_in.shape[1] - inner_width) // 2
    n_blocks = lax.axis_size("tm")
    seq_len = tok_rows * n_blocks
    series_count = lax.axis_size("series")
    my_block = lax.axis_index("tm")

    ordered = jnp.take(codes, owner_slot, axis=0).astype(fl)
    outgoing = jnp.tile(ordered, (n_blocks, 1))
    reading = lax.all_to_all(outgoing, ("tm", "series"), split_axis=0, concat_axis=1, tiled=True)[0]
    edge_float = edges.astype(fl)
    upper_edge = jnp.concatenate([edge_float[1:], jnp.full((1,), code_ceiling, fl)])
    onehot = (
        (edge_float[None, :] <= reading[:, None]) & (upper_edge[None, :] > reading[:, None])
    ).astype(fl)
    counts = jnp.sum(onehot, axis=0)
    before = jnp.cumsum(counts) - counts
    bin_table = jnp.stack([before, counts, edge_float, upper_edge - edge_float], axis=1)
    picked = jnp.dot(onehot, bin_table, precision=lax.Precision.HIGHEST)
    within_bin = (reading - picked[:, 2]) / picked[:, 3]
    quantile = (picked[:, 0] + picked[:, 1] * within_bin) / seq_len
    frequency = (jnp.arange(w_in.shape[0], dtype=fl) + 0.5) * math.pi
    features_all = jnp.cos(quantile[:, None] * frequency).astype(half)

    def mine(a):
        return lax.dynamic_index_in_dim(a, my_block, axis=0, keepdims=False)

    features_blocks = features_all.reshape(n_blocks, tok_rows, -1)
    features = mine(features_blocks)
    projected = jnp.dot(features, w_in, preferred_element_type=fl).astype(half)
    x_heads = projected[:, :inner_width].reshape(tok_rows, head_count, head_dim)
    b_proj = projected[:, inner_width : inner_width + state_dim]
    c_proj = projected[:, inner_width + state_dim :]
    step_size = jax.nn.softplus(dt_bias + jnp.dot(features, w_dt, preferred_element_type=fl))
    cum_decay = jnp.cumsum(-step_size * decay_rate, axis=0)
    tail_factor = jnp.exp(cum_decay[-1][None, :] - cum_decay) * step_size
    head_factor = jnp.exp(cum_decay)
    x_weighted = (x_heads * tail_factor[:, :, None]).astype(half)

    projected_all = jnp.dot(features_all, w_in, preferred_element_type=fl).astype(half)
    projected_all = projected_all.reshape(n_blocks, tok_rows, -1)
    x_all = projected_all[:, :, :inner_width].reshape(n_blocks, tok_rows, head_count, head_dim)
    b_all = projected_all[:, :, inner_width : inner_width + state_dim]
    step_all = jax.nn.softplus(
        dt_bias + jnp.dot(features_all, w_dt, preferred_element_type=fl)
    ).reshape(n_blocks, tok_rows, head_count)
    cum_all = jnp.cumsum(-step_all * decay_rate, axis=1)
    gate_all = jnp.exp(cum_all[:, -1])
    tail_all = jnp.exp(cum_all[:, -1:, :] - cum_all) * step_all
    xw_all = (x_all * tail_all[..., None]).astype(half)
    state_local_all = jnp.einsum("bthp,btn->bhpn", xw_all, b_all, preferred_element_type=fl)

    state_in = jnp.zeros((head_count, head_dim, state_dim), fl)
    for k in range(n_blocks - 1):
        new = gate_all[k][:, None, None] * state_in + state_local_all[k]
        state_in = jnp.where(k < my_block, new, state_in)

    grad_heads = grad_out[0].reshape(tok_rows, head_count, head_dim)
    grad_weighted = (grad_heads * head_factor[:, :, None]).astype(half)
    adjoint_local = jnp.einsum("thp,tn->hpn", grad_weighted, c_proj, preferred_element_type=fl)
    adjoint_in = jnp.zeros((head_count, head_dim, state_dim), fl)
    if n_blocks == 4:
        first = lax.ppermute(adjoint_local, "tm", [(3, 2), (1, 0)])
        second = lax.ppermute(adjoint_local, "tm", [(3, 1), (2, 0)])
        third = lax.ppermute(second, "tm", [(0, 1)])
        fourth = lax.ppermute(first, "tm", [(2, 0)])
        seen = [
            first,
            jnp.where(my_block == 1, third, second),
            jnp.where(my_block == 2, first, jnp.where(my_block == 1, second, fourth)),
        ]
        for k in range(n_blocks - 1, 0, -1):
            new = gate_all[k][:, None, None] * adjoint_in + seen[k - 1]
            adjoint_in = jnp.where(k > my_block, new, adjoint_in)
    else:
        adjoint_all = lax.all_gather(adjoint_local, "tm")
        for k in range(n_blocks - 1, 0, -1):
            new = gate_all[k][:, None, None] * adjoint_in + adjoint_all[k]
            adjoint_in = jnp.where(k > my_block, new, adjoint_in)

    masked = decay_matrix(cum_decay) * step_size.T[:, None, :]
    scores = jnp.dot(c_proj, b_proj.T, preferred_element_type=fl)
    weights = (scores[None] * masked).astype(half)
    state_half = state_in.astype(half)
    adjoint_half = adjoint_in.astype(half)
    output = jnp.einsum("hts,shp->thp", weights, x_heads, preferred_element_type=fl)
    output = (
        output
        + jnp.einsum("tn,hpn->thp", c_proj, state_half, preferred_element_type=fl)
        * head_factor[:, :, None]
    )
    ssd_output = output.reshape(1, tok_rows, inner_width).astype(half)
    grad_x = jnp.einsum("hts,thp->shp", weights, grad_heads, preferred_element_type=fl)
    grad_x = (
        grad_x
        + jnp.einsum("sn,hpn->shp", b_proj, adjoint_half, preferred_element_type=fl)
        * tail_factor[:, :, None]
    )
    pair_scores = jnp.einsum("thp,shp->hts", grad_heads, x_heads, preferred_element_type=fl)
    pair_mixed = jnp.sum(pair_scores * masked, axis=0).astype(half)
    grad_b = jnp.dot(pair_mixed.T, c_proj, preferred_element_type=fl)
    grad_b = grad_b + jnp.einsum("shp,hpn->sn", x_weighted, adjoint_half, preferred_element_type=fl)
    grad_c = jnp.dot(pair_mixed, b_proj, preferred_element_type=fl)
    grad_c = grad_c + jnp.einsum(
        "thp,hpn->tn", grad_weighted, state_half, preferred_element_type=fl
    )
    grad_rows = jnp.concatenate(
        [
            grad_x.reshape(tok_rows, inner_width).astype(half),
            grad_b.astype(half),
            grad_c.astype(half),
        ],
        axis=1,
    )
    local_grad = jnp.einsum("tw,tf->wf", grad_rows, features, preferred_element_type=fl)
    total_grad = tree_psum(local_grad).T
    grad_in = total_grad / math.sqrt(series_count * seq_len)
    return (ssd_output, grad_in)


def solution(mesh):
    return jax.shard_map(
        on_device,
        mesh=mesh,
        in_specs=(P(None, ("tm", "series")), P(), P(), P(), P(), P(), P(), P("series", "tm", None)),
        out_specs=(P("series", "tm", None), P()),
        check_vma=False,
    )
```

```python
import math

import jax
import jax.numpy as jnp
from jax import lax
from jax.sharding import PartitionSpec as P

code_ceiling = 2097152.0


def decay_matrix(cum_decay):
    row_count = cum_decay.shape[0]
    causal = jnp.arange(row_count)[:, None] >= jnp.arange(row_count)[None, :]
    log_span = cum_decay.T[:, :, None] - cum_decay.T[:, None, :]
    return jnp.where(causal[None], jnp.exp(jnp.where(causal[None], log_span, -60.0)), 0.0)


def axis_bits(axis):
    size = lax.axis_size(axis)
    assert size & (size - 1) == 0
    return [1 << k for k in range(size.bit_length() - 1)]


def exchange(value, axis, flip):
    pairs = [(i, i ^ flip) for i in range(lax.axis_size(axis))]
    return lax.ppermute(value, axis, pairs)


def bit_groups():
    tm_bits, series_bits = axis_bits("tm"), axis_bits("series")
    groups = [("series", series_bits[:1])] if series_bits else []
    for axis, bits in (("tm", tm_bits), ("series", series_bits[1:])):
        groups += [(axis, bits[i : i + 2]) for i in range(0, len(bits), 2)]
    return groups


def group_round(value, axis, bits, scatter):
    index = lax.axis_index(axis)
    coord = sum(((index // b) % 2) * (1 << j) for j, b in enumerate(bits))
    size = 1 << len(bits)

    def flip_of(m):
        return sum(b for j, b in enumerate(bits) if (m >> j) & 1)

    rows = value.shape[0]
    if scatter:
        part = rows // size
        keep = lax.dynamic_slice_in_dim(value, coord * part, part)
        got = [
            exchange(lax.dynamic_slice_in_dim(value, (coord ^ m) * part, part), axis, flip_of(m))
            for m in range(1, size)
        ]
        for piece in got:
            keep = keep + piece
        return keep
    got = [value] + [exchange(value, axis, flip_of(m)) for m in range(1, size)]
    stacked = jnp.stack(got)
    return [lax.dynamic_index_in_dim(stacked, coord ^ q, 0, keepdims=False) for q in range(size)]


def tree_psum(value):
    done = []
    for axis, bits in bit_groups():
        if value.shape[0] % (8 << len(bits)) == 0:
            value = group_round(value, axis, bits, True)
            done.append((axis, bits))
        else:
            pieces = group_round(value, axis, bits, False)
            value = pieces[0]
            for piece in pieces[1:]:
                value = value + piece
    for axis, bits in reversed(done):
        value = jnp.concatenate(group_round(value, axis, bits, False))
    return value


def on_device(codes, owner_slot, edges, w_in, w_dt, dt_bias, decay_rate, grad_out):
    fl = jnp.float32
    half = jnp.bfloat16
    tok_rows = grad_out.shape[1]
    head_count = dt_bias.shape[0]
    inner_width = grad_out.shape[2]
    head_dim = inner_width // head_count
    state_dim = (w_in.shape[1] - inner_width) // 2
    n_blocks = lax.axis_size("tm")
    seq_len = tok_rows * n_blocks
    series_count = lax.axis_size("series")
    my_block = lax.axis_index("tm")

    ordered = jnp.take(codes, owner_slot, axis=0).astype(fl)
    outgoing = jnp.tile(ordered, (n_blocks, 1))
    reading = lax.all_to_all(outgoing, ("tm", "series"), split_axis=0, concat_axis=1, tiled=True)[0]
    edge_float = edges.astype(fl)
    upper_edge = jnp.concatenate([edge_float[1:], jnp.full((1,), code_ceiling, fl)])
    onehot = (
        (edge_float[None, :] <= reading[:, None]) & (upper_edge[None, :] > reading[:, None])
    ).astype(fl)
    counts = jnp.sum(onehot, axis=0)
    before = jnp.cumsum(counts) - counts
    bin_table = jnp.stack([before, counts, edge_float, upper_edge - edge_float], axis=1)
    picked = jnp.dot(onehot, bin_table, precision=lax.Precision.HIGHEST)
    within_bin = (reading - picked[:, 2]) / picked[:, 3]
    quantile = (picked[:, 0] + picked[:, 1] * within_bin) / seq_len
    frequency = (jnp.arange(w_in.shape[0], dtype=fl) + 0.5) * math.pi
    features_all = jnp.cos(quantile[:, None] * frequency).astype(half)

    def mine(a):
        return lax.dynamic_index_in_dim(a, my_block, axis=0, keepdims=False)

    features_blocks = features_all.reshape(n_blocks, tok_rows, -1)
    features = mine(features_blocks)
    projected = jnp.dot(features, w_in, preferred_element_type=fl).astype(half)
    x_heads = projected[:, :inner_width].reshape(tok_rows, head_count, head_dim)
    b_proj = projected[:, inner_width : inner_width + state_dim]
    c_proj = projected[:, inner_width + state_dim :]
    step_size = jax.nn.softplus(dt_bias + jnp.dot(features, w_dt, preferred_element_type=fl))
    cum_decay = jnp.cumsum(-step_size * decay_rate, axis=0)
    tail_factor = jnp.exp(cum_decay[-1][None, :] - cum_decay) * step_size
    head_factor = jnp.exp(cum_decay)
    x_weighted = (x_heads * tail_factor[:, :, None]).astype(half)

    projected_all = jnp.dot(features_all, w_in, preferred_element_type=fl).astype(half)
    projected_all = projected_all.reshape(n_blocks, tok_rows, -1)
    x_all = projected_all[:, :, :inner_width].reshape(n_blocks, tok_rows, head_count, head_dim)
    b_all = projected_all[:, :, inner_width : inner_width + state_dim]
    step_all = jax.nn.softplus(
        dt_bias + jnp.dot(features_all, w_dt, preferred_element_type=fl)
    ).reshape(n_blocks, tok_rows, head_count)
    cum_all = jnp.cumsum(-step_all * decay_rate, axis=1)
    gate_all = jnp.exp(cum_all[:, -1])
    tail_all = jnp.exp(cum_all[:, -1:, :] - cum_all) * step_all
    xw_all = (x_all * tail_all[..., None]).astype(half)
    state_local_all = jnp.einsum("bthp,btn->bhpn", xw_all, b_all, preferred_element_type=fl)

    state_in = jnp.zeros((head_count, head_dim, state_dim), fl)
    for k in range(n_blocks - 1):
        new = gate_all[k][:, None, None] * state_in + state_local_all[k]
        state_in = jnp.where(k < my_block, new, state_in)

    grad_heads = grad_out[0].reshape(tok_rows, head_count, head_dim)
    grad_weighted = (grad_heads * head_factor[:, :, None]).astype(half)
    adjoint_local = jnp.einsum("thp,tn->hpn", grad_weighted, c_proj, preferred_element_type=fl)
    adjoint_in = jnp.zeros((head_count, head_dim, state_dim), fl)
    if n_blocks == 4:
        sent = grad_out[0].astype(fl)
        first = lax.ppermute(sent, "tm", [(3, 2), (1, 0)])
        second = lax.ppermute(sent, "tm", [(3, 1), (2, 0)])
        third = lax.ppermute(second, "tm", [(0, 1)])
        fourth = lax.ppermute(first, "tm", [(2, 0)])
        seen = [
            first,
            jnp.where(my_block == 1, third, second),
            jnp.where(my_block == 2, first, jnp.where(my_block == 1, second, fourth)),
        ]
        c_all = projected_all[:, :, inner_width + state_dim :]
        for k in range(n_blocks - 1, 0, -1):
            later = seen[k - 1].reshape(tok_rows, head_count, head_dim)
            later_weighted = (later * jnp.exp(cum_all[k])[:, :, None]).astype(half)
            later_local = jnp.einsum("thp,tn->hpn", later_weighted, c_all[k], preferred_element_type=fl)
            new = gate_all[k][:, None, None] * adjoint_in + later_local
            adjoint_in = jnp.where(k > my_block, new, adjoint_in)
    else:
        adjoint_all = lax.all_gather(adjoint_local, "tm")
        for k in range(n_blocks - 1, 0, -1):
            new = gate_all[k][:, None, None] * adjoint_in + adjoint_all[k]
            adjoint_in = jnp.where(k > my_block, new, adjoint_in)

    masked = decay_matrix(cum_decay) * step_size.T[:, None, :]
    scores = jnp.dot(c_proj, b_proj.T, preferred_element_type=fl)
    weights = (scores[None] * masked).astype(half)
    state_half = state_in.astype(half)
    adjoint_half = adjoint_in.astype(half)
    output = jnp.einsum("hts,shp->thp", weights, x_heads, preferred_element_type=fl)
    output = (
        output
        + jnp.einsum("tn,hpn->thp", c_proj, state_half, preferred_element_type=fl)
        * head_factor[:, :, None]
    )
    ssd_output = output.reshape(1, tok_rows, inner_width).astype(half)
    grad_x = jnp.einsum("hts,thp->shp", weights, grad_heads, preferred_element_type=fl)
    grad_x = (
        grad_x
        + jnp.einsum("sn,hpn->shp", b_proj, adjoint_half, preferred_element_type=fl)
        * tail_factor[:, :, None]
    )
    pair_scores = jnp.einsum("thp,shp->hts", grad_heads, x_heads, preferred_element_type=fl)
    pair_mixed = jnp.sum(pair_scores * masked, axis=0).astype(half)
    grad_b = jnp.dot(pair_mixed.T, c_proj, preferred_element_type=fl)
    grad_b = grad_b + jnp.einsum("shp,hpn->sn", x_weighted, adjoint_half, preferred_element_type=fl)
    grad_c = jnp.dot(pair_mixed, b_proj, preferred_element_type=fl)
    grad_c = grad_c + jnp.einsum(
        "thp,hpn->tn", grad_weighted, state_half, preferred_element_type=fl
    )
    grad_rows = jnp.concatenate(
        [
            grad_x.reshape(tok_rows, inner_width).astype(half),
            grad_b.astype(half),
            grad_c.astype(half),
        ],
        axis=1,
    )
    local_grad = jnp.einsum("tw,tf->wf", grad_rows, features, preferred_element_type=fl)
    total_grad = tree_psum(local_grad).T
    grad_in = total_grad / math.sqrt(series_count * seq_len)
    return (ssd_output, grad_in)


def solution(mesh):
    return jax.shard_map(
        on_device,
        mesh=mesh,
        in_specs=(P(None, ("tm", "series")), P(), P(), P(), P(), P(), P(), P("series", "tm", None)),
        out_specs=(P("series", "tm", None), P()),
        check_vma=False,
    )
```

```python
import math

import jax
import jax.numpy as jnp
from jax import lax
from jax.sharding import PartitionSpec as P

code_ceiling = 2097152.0


def decay_matrix(cum_decay):
    row_count = cum_decay.shape[0]
    causal = jnp.arange(row_count)[:, None] >= jnp.arange(row_count)[None, :]
    log_span = cum_decay.T[:, :, None] - cum_decay.T[:, None, :]
    return jnp.where(causal[None], jnp.exp(jnp.where(causal[None], log_span, -60.0)), 0.0)


def axis_bits(axis):
    size = lax.axis_size(axis)
    assert size & (size - 1) == 0
    return [1 << k for k in range(size.bit_length() - 1)]


def exchange(value, axis, flip):
    pairs = [(i, i ^ flip) for i in range(lax.axis_size(axis))]
    return lax.ppermute(value, axis, pairs)


def bit_groups():
    tm_bits, series_bits = axis_bits("tm"), axis_bits("series")
    groups = [("series", series_bits[:1])] if series_bits else []
    for axis, bits in (("tm", tm_bits), ("series", series_bits[1:])):
        groups += [(axis, bits[i : i + 2]) for i in range(0, len(bits), 2)]
    return groups


def group_round(value, axis, bits, scatter):
    index = lax.axis_index(axis)
    coord = sum(((index // b) % 2) * (1 << j) for j, b in enumerate(bits))
    size = 1 << len(bits)

    def flip_of(m):
        return sum(b for j, b in enumerate(bits) if (m >> j) & 1)

    rows = value.shape[0]
    if scatter:
        part = rows // size
        keep = lax.dynamic_slice_in_dim(value, coord * part, part)
        got = [
            exchange(lax.dynamic_slice_in_dim(value, (coord ^ m) * part, part), axis, flip_of(m))
            for m in range(1, size)
        ]
        for piece in got:
            keep = keep + piece
        return keep
    got = [value] + [exchange(value, axis, flip_of(m)) for m in range(1, size)]
    stacked = jnp.stack(got)
    return [lax.dynamic_index_in_dim(stacked, coord ^ q, 0, keepdims=False) for q in range(size)]


def tree_psum(value):
    done = []
    for axis, bits in bit_groups():
        if value.shape[0] % (8 << len(bits)) == 0:
            value = group_round(value, axis, bits, True)
            done.append((axis, bits))
        else:
            pieces = group_round(value, axis, bits, False)
            value = pieces[0]
            for piece in pieces[1:]:
                value = value + piece
    for axis, bits in reversed(done):
        value = jnp.concatenate(group_round(value, axis, bits, False))
    return value


def on_device(codes, owner_slot, edges, w_in, w_dt, dt_bias, decay_rate, grad_out):
    fl = jnp.float32
    half = jnp.bfloat16
    tok_rows = grad_out.shape[1]
    head_count = dt_bias.shape[0]
    inner_width = grad_out.shape[2]
    head_dim = inner_width // head_count
    state_dim = (w_in.shape[1] - inner_width) // 2
    n_blocks = lax.axis_size("tm")
    seq_len = tok_rows * n_blocks
    series_count = lax.axis_size("series")
    my_block = lax.axis_index("tm")

    ordered = jnp.take(codes, owner_slot, axis=0).astype(fl)
    outgoing = jnp.tile(ordered, (n_blocks, 1))
    reading = lax.all_to_all(outgoing, ("tm", "series"), split_axis=0, concat_axis=1, tiled=True)[0]
    edge_float = edges.astype(fl)
    upper_edge = jnp.concatenate([edge_float[1:], jnp.full((1,), code_ceiling, fl)])
    onehot = (
        (edge_float[None, :] <= reading[:, None]) & (upper_edge[None, :] > reading[:, None])
    ).astype(fl)
    counts = jnp.sum(onehot, axis=0)
    before = jnp.cumsum(counts) - counts
    bin_table = jnp.stack([before, counts, edge_float, upper_edge - edge_float], axis=1)
    picked = jnp.dot(onehot, bin_table, precision=lax.Precision.HIGHEST)
    within_bin = (reading - picked[:, 2]) / picked[:, 3]
    quantile = (picked[:, 0] + picked[:, 1] * within_bin) / seq_len
    frequency = (jnp.arange(w_in.shape[0], dtype=fl) + 0.5) * math.pi
    features_all = jnp.cos(quantile[:, None] * frequency).astype(half)

    def mine(a):
        return lax.dynamic_index_in_dim(a, my_block, axis=0, keepdims=False)

    features_blocks = features_all.reshape(n_blocks, tok_rows, -1)
    features = mine(features_blocks)
    projected = jnp.dot(features, w_in, preferred_element_type=fl).astype(half)
    x_heads = projected[:, :inner_width].reshape(tok_rows, head_count, head_dim)
    b_proj = projected[:, inner_width : inner_width + state_dim]
    c_proj = projected[:, inner_width + state_dim :]
    step_size = jax.nn.softplus(dt_bias + jnp.dot(features, w_dt, preferred_element_type=fl))
    cum_decay = jnp.cumsum(-step_size * decay_rate, axis=0)
    tail_factor = jnp.exp(cum_decay[-1][None, :] - cum_decay) * step_size
    head_factor = jnp.exp(cum_decay)
    x_weighted = (x_heads * tail_factor[:, :, None]).astype(half)

    projected_all = jnp.dot(features_all, w_in, preferred_element_type=fl).astype(half)
    projected_all = projected_all.reshape(n_blocks, tok_rows, -1)
    x_all = projected_all[:, :, :inner_width].reshape(n_blocks, tok_rows, head_count, head_dim)
    b_all = projected_all[:, :, inner_width : inner_width + state_dim]
    step_all = jax.nn.softplus(
        dt_bias + jnp.dot(features_all, w_dt, preferred_element_type=fl)
    ).reshape(n_blocks, tok_rows, head_count)
    cum_all = jnp.cumsum(-step_all * decay_rate, axis=1)
    gate_all = jnp.exp(cum_all[:, -1])
    tail_all = jnp.exp(cum_all[:, -1:, :] - cum_all) * step_all
    xw_all = (x_all * tail_all[..., None]).astype(half)
    state_local_all = jnp.einsum("bthp,btn->bhpn", xw_all, b_all, preferred_element_type=fl)

    state_in = jnp.zeros((head_count, head_dim, state_dim), fl)
    for k in range(n_blocks - 1):
        new = gate_all[k][:, None, None] * state_in + state_local_all[k]
        state_in = jnp.where(k < my_block, new, state_in)

    grad_heads = grad_out[0].reshape(tok_rows, head_count, head_dim)
    grad_weighted = (grad_heads * head_factor[:, :, None]).astype(half)
    adjoint_local = jnp.einsum("thp,tn->hpn", grad_weighted, c_proj, preferred_element_type=fl)
    adjoint_in = jnp.zeros((head_count, head_dim, state_dim), fl)
    if n_blocks == 4:
        sent, reading = lax.optimization_barrier((grad_out[0].astype(fl), reading))
        half_rows = tok_rows // 2
        first = lax.ppermute(sent, "tm", [(3, 2), (1, 0), (2, 3)])
        second = lax.ppermute(sent, "tm", [(3, 1), (2, 0)])
        third = lax.ppermute(second[:half_rows], "tm", [(0, 1), (1, 0)])
        fourth = lax.ppermute(first[half_rows:], "tm", [(3, 1), (2, 0)])
        joined = jnp.concatenate([third, fourth])
        seen = [
            first,
            jnp.where(my_block == 1, joined, second),
            jnp.where(my_block == 2, first, jnp.where(my_block == 1, second, joined)),
        ]
        c_all = projected_all[:, :, inner_width + state_dim :]
        for k in range(n_blocks - 1, 0, -1):
            later = seen[k - 1].reshape(tok_rows, head_count, head_dim)
            later_weighted = (later * jnp.exp(cum_all[k])[:, :, None]).astype(half)
            later_local = jnp.einsum("thp,tn->hpn", later_weighted, c_all[k], preferred_element_type=fl)
            new = gate_all[k][:, None, None] * adjoint_in + later_local
            adjoint_in = jnp.where(k > my_block, new, adjoint_in)
    else:
        adjoint_all = lax.all_gather(adjoint_local, "tm")
        for k in range(n_blocks - 1, 0, -1):
            new = gate_all[k][:, None, None] * adjoint_in + adjoint_all[k]
            adjoint_in = jnp.where(k > my_block, new, adjoint_in)

    masked = decay_matrix(cum_decay) * step_size.T[:, None, :]
    scores = jnp.dot(c_proj, b_proj.T, preferred_element_type=fl)
    weights = (scores[None] * masked).astype(half)
    state_half = state_in.astype(half)
    adjoint_half = adjoint_in.astype(half)
    output = jnp.einsum("hts,shp->thp", weights, x_heads, preferred_element_type=fl)
    output = (
        output
        + jnp.einsum("tn,hpn->thp", c_proj, state_half, preferred_element_type=fl)
        * head_factor[:, :, None]
    )
    ssd_output = output.reshape(1, tok_rows, inner_width).astype(half)
    grad_x = jnp.einsum("hts,thp->shp", weights, grad_heads, preferred_element_type=fl)
    grad_x = (
        grad_x
        + jnp.einsum("sn,hpn->shp", b_proj, adjoint_half, preferred_element_type=fl)
        * tail_factor[:, :, None]
    )
    pair_scores = jnp.einsum("thp,shp->hts", grad_heads, x_heads, preferred_element_type=fl)
    pair_mixed = jnp.sum(pair_scores * masked, axis=0).astype(half)
    grad_b = jnp.dot(pair_mixed.T, c_proj, preferred_element_type=fl)
    grad_b = grad_b + jnp.einsum("shp,hpn->sn", x_weighted, adjoint_half, preferred_element_type=fl)
    grad_c = jnp.dot(pair_mixed, b_proj, preferred_element_type=fl)
    grad_c = grad_c + jnp.einsum(
        "thp,hpn->tn", grad_weighted, state_half, preferred_element_type=fl
    )
    grad_rows = jnp.concatenate(
        [
            grad_x.reshape(tok_rows, inner_width).astype(half),
            grad_b.astype(half),
            grad_c.astype(half),
        ],
        axis=1,
    )
    local_grad = jnp.einsum("tw,tf->wf", grad_rows, features, preferred_element_type=fl)
    total_grad = tree_psum(local_grad).T
    grad_in = total_grad / math.sqrt(series_count * seq_len)
    return (ssd_output, grad_in)


def solution(mesh):
    return jax.shard_map(
        on_device,
        mesh=mesh,
        in_specs=(P(None, ("tm", "series")), P(), P(), P(), P(), P(), P(), P("series", "tm", None)),
        out_specs=(P("series", "tm", None), P()),
        check_vma=False,
    )
```

```python
import math

import jax
import jax.numpy as jnp
from jax import lax
from jax.sharding import PartitionSpec as P

code_ceiling = 2097152.0


def decay_matrix(cum_decay):
    row_count = cum_decay.shape[0]
    causal = jnp.arange(row_count)[:, None] >= jnp.arange(row_count)[None, :]
    log_span = cum_decay.T[:, :, None] - cum_decay.T[:, None, :]
    return jnp.where(causal[None], jnp.exp(jnp.where(causal[None], log_span, -60.0)), 0.0)


def axis_bits(axis):
    size = lax.axis_size(axis)
    assert size & (size - 1) == 0
    return [1 << k for k in range(size.bit_length() - 1)]


def exchange(value, axis, flip):
    pairs = [(i, i ^ flip) for i in range(lax.axis_size(axis))]
    return lax.ppermute(value, axis, pairs)


def bit_groups():
    tm_bits, series_bits = axis_bits("tm"), axis_bits("series")
    groups = [("series", series_bits[:1])] if series_bits else []
    for axis, bits in (("tm", tm_bits), ("series", series_bits[1:])):
        groups += [(axis, bits[i : i + 2]) for i in range(0, len(bits), 2)]
    return groups


def group_round(value, axis, bits, scatter):
    index = lax.axis_index(axis)
    coord = sum(((index // b) % 2) * (1 << j) for j, b in enumerate(bits))
    size = 1 << len(bits)

    def flip_of(m):
        return sum(b for j, b in enumerate(bits) if (m >> j) & 1)

    rows = value.shape[0]
    if scatter:
        part = rows // size
        keep = lax.dynamic_slice_in_dim(value, coord * part, part)
        got = [
            exchange(lax.dynamic_slice_in_dim(value, (coord ^ m) * part, part), axis, flip_of(m))
            for m in range(1, size)
        ]
        for piece in got:
            keep = keep + piece
        return keep
    got = [value] + [exchange(value, axis, flip_of(m)) for m in range(1, size)]
    stacked = jnp.stack(got)
    return [lax.dynamic_index_in_dim(stacked, coord ^ q, 0, keepdims=False) for q in range(size)]


def tree_psum(value):
    done = []
    for axis, bits in bit_groups():
        if value.shape[0] % (8 << len(bits)) == 0:
            value = group_round(value, axis, bits, True)
            done.append((axis, bits))
        else:
            pieces = group_round(value, axis, bits, False)
            value = pieces[0]
            for piece in pieces[1:]:
                value = value + piece
    for axis, bits in reversed(done):
        value = jnp.concatenate(group_round(value, axis, bits, False))
    return value


def on_device(codes, owner_slot, edges, w_in, w_dt, dt_bias, decay_rate, grad_out):
    fl = jnp.float32
    half = jnp.bfloat16
    tok_rows = grad_out.shape[1]
    head_count = dt_bias.shape[0]
    inner_width = grad_out.shape[2]
    head_dim = inner_width // head_count
    state_dim = (w_in.shape[1] - inner_width) // 2
    n_blocks = lax.axis_size("tm")
    seq_len = tok_rows * n_blocks
    series_count = lax.axis_size("series")
    my_block = lax.axis_index("tm")

    ordered = jnp.take(codes, owner_slot, axis=0).astype(fl)
    outgoing = jnp.tile(ordered, (n_blocks, 1))
    reading = lax.all_to_all(outgoing, ("tm", "series"), split_axis=0, concat_axis=1, tiled=True)[0]
    edge_float = edges.astype(fl)
    upper_edge = jnp.concatenate([edge_float[1:], jnp.full((1,), code_ceiling, fl)])
    onehot = (
        (edge_float[None, :] <= reading[:, None]) & (upper_edge[None, :] > reading[:, None])
    ).astype(fl)
    counts = jnp.sum(onehot, axis=0)
    before = jnp.cumsum(counts) - counts
    bin_table = jnp.stack([before, counts, edge_float, upper_edge - edge_float], axis=1)
    picked = jnp.dot(onehot, bin_table, precision=lax.Precision.HIGHEST)
    within_bin = (reading - picked[:, 2]) / picked[:, 3]
    quantile = (picked[:, 0] + picked[:, 1] * within_bin) / seq_len
    frequency = (jnp.arange(w_in.shape[0], dtype=fl) + 0.5) * math.pi
    features_all = jnp.cos(quantile[:, None] * frequency).astype(half)

    def mine(a):
        return lax.dynamic_index_in_dim(a, my_block, axis=0, keepdims=False)

    features_blocks = features_all.reshape(n_blocks, tok_rows, -1)
    features = mine(features_blocks)
    projected = jnp.dot(features, w_in, preferred_element_type=fl).astype(half)
    x_heads = projected[:, :inner_width].reshape(tok_rows, head_count, head_dim)
    b_proj = projected[:, inner_width : inner_width + state_dim]
    c_proj = projected[:, inner_width + state_dim :]
    step_size = jax.nn.softplus(dt_bias + jnp.dot(features, w_dt, preferred_element_type=fl))
    cum_decay = jnp.cumsum(-step_size * decay_rate, axis=0)
    tail_factor = jnp.exp(cum_decay[-1][None, :] - cum_decay) * step_size
    head_factor = jnp.exp(cum_decay)
    x_weighted = (x_heads * tail_factor[:, :, None]).astype(half)

    projected_all = jnp.dot(features_all, w_in, preferred_element_type=fl).astype(half)
    projected_all = projected_all.reshape(n_blocks, tok_rows, -1)
    x_all = projected_all[:, :, :inner_width].reshape(n_blocks, tok_rows, head_count, head_dim)
    b_all = projected_all[:, :, inner_width : inner_width + state_dim]
    step_all = jax.nn.softplus(
        dt_bias + jnp.dot(features_all, w_dt, preferred_element_type=fl)
    ).reshape(n_blocks, tok_rows, head_count)
    cum_all = jnp.cumsum(-step_all * decay_rate, axis=1)
    gate_all = jnp.exp(cum_all[:, -1])
    tail_all = jnp.exp(cum_all[:, -1:, :] - cum_all) * step_all
    head_all = jnp.exp(cum_all)
    earlier = n_blocks - 1
    xw_all = (x_all[:earlier] * tail_all[:earlier, :, :, None]).astype(half)
    xw_all = xw_all.reshape(earlier, tok_rows, inner_width)
    state_local_t = jnp.einsum("btn,btk->bnk", b_all[:earlier], xw_all, preferred_element_type=fl)

    state_t = jnp.zeros((state_dim, inner_width), fl)
    for k in range(earlier):
        gate_row = jnp.repeat(gate_all[k], head_dim)[None, :]
        new = gate_row * state_t + state_local_t[k]
        state_t = jnp.where(k < my_block, new, state_t)
    state_in = state_t.reshape(state_dim, head_count, head_dim).transpose(1, 2, 0)

    grad_heads = grad_out[0].reshape(tok_rows, head_count, head_dim)
    grad_weighted = (grad_heads * head_factor[:, :, None]).astype(half)
    adjoint_local = jnp.einsum("thp,tn->hpn", grad_weighted, c_proj, preferred_element_type=fl)
    adjoint_in = jnp.zeros((head_count, head_dim, state_dim), fl)
    if n_blocks == 4:
        sent = grad_out[0].astype(fl)
        first = lax.ppermute(sent, "tm", [(3, 2), (1, 0)])
        second = lax.ppermute(sent, "tm", [(3, 1), (2, 0)])
        third = lax.ppermute(second, "tm", [(0, 1)])
        fourth = lax.ppermute(first, "tm", [(2, 0)])
        seen = [
            first,
            jnp.where(my_block == 1, third, second),
            jnp.where(my_block == 2, first, jnp.where(my_block == 1, second, fourth)),
        ]
        c_all = projected_all[1:, :, inner_width + state_dim :]
        later = jnp.stack(seen).reshape(n_blocks - 1, tok_rows, head_count, head_dim)
        later_weighted = (later * head_all[1:, :, :, None]).astype(half)
        later_weighted = later_weighted.reshape(n_blocks - 1, tok_rows, inner_width)
        later_local_t = jnp.einsum("btn,btk->bnk", c_all, later_weighted, preferred_element_type=fl)
        adjoint_t = jnp.zeros((state_dim, inner_width), fl)
        for k in range(n_blocks - 1, 0, -1):
            gate_row = jnp.repeat(gate_all[k], head_dim)[None, :]
            new = gate_row * adjoint_t + later_local_t[k - 1]
            adjoint_t = jnp.where(k > my_block, new, adjoint_t)
        adjoint_in = adjoint_t.reshape(state_dim, head_count, head_dim).transpose(1, 2, 0)
    else:
        adjoint_all = lax.all_gather(adjoint_local, "tm")
        for k in range(n_blocks - 1, 0, -1):
            new = gate_all[k][:, None, None] * adjoint_in + adjoint_all[k]
            adjoint_in = jnp.where(k > my_block, new, adjoint_in)

    masked = decay_matrix(cum_decay) * step_size.T[:, None, :]
    scores = jnp.dot(c_proj, b_proj.T, preferred_element_type=fl)
    weights = (scores[None] * masked).astype(half)
    state_half = state_in.astype(half)
    adjoint_half = adjoint_in.astype(half)
    output = jnp.einsum("hts,shp->thp", weights, x_heads, preferred_element_type=fl)
    output = (
        output
        + jnp.einsum("tn,hpn->thp", c_proj, state_half, preferred_element_type=fl)
        * head_factor[:, :, None]
    )
    ssd_output = output.reshape(1, tok_rows, inner_width).astype(half)
    grad_x = jnp.einsum("hts,thp->shp", weights, grad_heads, preferred_element_type=fl)
    grad_x = (
        grad_x
        + jnp.einsum("sn,hpn->shp", b_proj, adjoint_half, preferred_element_type=fl)
        * tail_factor[:, :, None]
    )
    pair_scores = jnp.einsum("thp,shp->hts", grad_heads, x_heads, preferred_element_type=fl)
    pair_mixed = jnp.sum(pair_scores * masked, axis=0).astype(half)
    grad_b = jnp.dot(pair_mixed.T, c_proj, preferred_element_type=fl)
    grad_b = grad_b + jnp.einsum("shp,hpn->sn", x_weighted, adjoint_half, preferred_element_type=fl)
    grad_c = jnp.dot(pair_mixed, b_proj, preferred_element_type=fl)
    grad_c = grad_c + jnp.einsum(
        "thp,hpn->tn", grad_weighted, state_half, preferred_element_type=fl
    )
    grad_rows = jnp.concatenate(
        [
            grad_x.reshape(tok_rows, inner_width).astype(half),
            grad_b.astype(half),
            grad_c.astype(half),
        ],
        axis=1,
    )
    local_grad = jnp.einsum("tw,tf->wf", grad_rows, features, preferred_element_type=fl)
    total_grad = tree_psum(local_grad).T
    grad_in = total_grad / math.sqrt(series_count * seq_len)
    return (ssd_output, grad_in)


def solution(mesh):
    return jax.shard_map(
        on_device,
        mesh=mesh,
        in_specs=(P(None, ("tm", "series")), P(), P(), P(), P(), P(), P(), P("series", "tm", None)),
        out_specs=(P("series", "tm", None), P()),
        check_vma=False,
    )
```

```python
import math

import jax
import jax.numpy as jnp
from jax import lax
from jax.sharding import PartitionSpec as P

code_ceiling = 2097152.0


def decay_matrix(cum_decay):
    row_count = cum_decay.shape[0]
    causal = jnp.arange(row_count)[:, None] >= jnp.arange(row_count)[None, :]
    log_span = cum_decay.T[:, :, None] - cum_decay.T[:, None, :]
    return jnp.where(causal[None], jnp.exp(jnp.where(causal[None], log_span, -60.0)), 0.0)


def axis_bits(axis):
    size = lax.axis_size(axis)
    assert size & (size - 1) == 0
    return [1 << k for k in range(size.bit_length() - 1)]


def exchange(value, axis, flip):
    pairs = [(i, i ^ flip) for i in range(lax.axis_size(axis))]
    return lax.ppermute(value, axis, pairs)


def bit_groups():
    tm_bits, series_bits = axis_bits("tm"), axis_bits("series")
    groups = [("series", series_bits[:1])] if series_bits else []
    for axis, bits in (("tm", tm_bits), ("series", series_bits[1:])):
        groups += [(axis, bits[i : i + 2]) for i in range(0, len(bits), 2)]
    return groups


def group_round(value, axis, bits, scatter):
    index = lax.axis_index(axis)
    coord = sum(((index // b) % 2) * (1 << j) for j, b in enumerate(bits))
    size = 1 << len(bits)

    def flip_of(m):
        return sum(b for j, b in enumerate(bits) if (m >> j) & 1)

    rows = value.shape[0]
    if scatter:
        part = rows // size
        keep = lax.dynamic_slice_in_dim(value, coord * part, part)
        got = [
            exchange(lax.dynamic_slice_in_dim(value, (coord ^ m) * part, part), axis, flip_of(m))
            for m in range(1, size)
        ]
        for piece in got:
            keep = keep + piece
        return keep
    got = [value] + [exchange(value, axis, flip_of(m)) for m in range(1, size)]
    stacked = jnp.stack(got)
    return [lax.dynamic_index_in_dim(stacked, coord ^ q, 0, keepdims=False) for q in range(size)]


def tree_psum(value):
    done = []
    for axis, bits in bit_groups():
        if value.shape[0] % (8 << len(bits)) == 0:
            value = group_round(value, axis, bits, True)
            done.append((axis, bits))
        else:
            pieces = group_round(value, axis, bits, False)
            value = pieces[0]
            for piece in pieces[1:]:
                value = value + piece
    for axis, bits in reversed(done):
        value = jnp.concatenate(group_round(value, axis, bits, False))
    return value


def on_device(codes, owner_slot, edges, w_in, w_dt, dt_bias, decay_rate, grad_out):
    fl = jnp.float32
    half = jnp.bfloat16
    tok_rows = grad_out.shape[1]
    head_count = dt_bias.shape[0]
    inner_width = grad_out.shape[2]
    head_dim = inner_width // head_count
    state_dim = (w_in.shape[1] - inner_width) // 2
    n_blocks = lax.axis_size("tm")
    seq_len = tok_rows * n_blocks
    series_count = lax.axis_size("series")
    my_block = lax.axis_index("tm")

    ordered = jnp.take(codes, owner_slot, axis=0).astype(fl)
    outgoing = jnp.tile(ordered, (n_blocks, 1))
    reading = lax.all_to_all(outgoing, ("tm", "series"), split_axis=0, concat_axis=1, tiled=True)[0]
    edge_float = edges.astype(fl)
    upper_edge = jnp.concatenate([edge_float[1:], jnp.full((1,), code_ceiling, fl)])
    onehot = (
        (edge_float[None, :] <= reading[:, None]) & (upper_edge[None, :] > reading[:, None])
    ).astype(fl)
    counts = jnp.sum(onehot, axis=0)
    before = jnp.cumsum(counts) - counts
    bin_table = jnp.stack([before, counts, edge_float, upper_edge - edge_float], axis=1)
    picked = jnp.dot(onehot, bin_table, precision=lax.Precision.HIGHEST)
    within_bin = (reading - picked[:, 2]) / picked[:, 3]
    quantile = (picked[:, 0] + picked[:, 1] * within_bin) / seq_len
    frequency = (jnp.arange(w_in.shape[0], dtype=fl) + 0.5) * math.pi
    features_all = jnp.cos(quantile[:, None] * frequency).astype(half)

    def mine(a):
        return lax.dynamic_index_in_dim(a, my_block, axis=0, keepdims=False)

    features_blocks = features_all.reshape(n_blocks, tok_rows, -1)
    features = mine(features_blocks)
    projected = jnp.dot(features, w_in, preferred_element_type=fl).astype(half)
    x_heads = projected[:, :inner_width].reshape(tok_rows, head_count, head_dim)
    b_proj = projected[:, inner_width : inner_width + state_dim]
    c_proj = projected[:, inner_width + state_dim :]
    step_size = jax.nn.softplus(dt_bias + jnp.dot(features, w_dt, preferred_element_type=fl))
    cum_decay = jnp.cumsum(-step_size * decay_rate, axis=0)
    tail_factor = jnp.exp(cum_decay[-1][None, :] - cum_decay) * step_size
    head_factor = jnp.exp(cum_decay)
    x_weighted = (x_heads * tail_factor[:, :, None]).astype(half)

    projected_all = jnp.dot(features_all, w_in, preferred_element_type=fl).astype(half)
    projected_all = projected_all.reshape(n_blocks, tok_rows, -1)
    x_all = projected_all[:, :, :inner_width].reshape(n_blocks, tok_rows, head_count, head_dim)
    b_all = projected_all[:, :, inner_width : inner_width + state_dim]
    step_all = jax.nn.softplus(
        dt_bias + jnp.dot(features_all, w_dt, preferred_element_type=fl)
    ).reshape(n_blocks, tok_rows, head_count)
    cum_all = jnp.cumsum(-step_all * decay_rate, axis=1)
    gate_all = jnp.exp(cum_all[:, -1])
    tail_all = jnp.exp(cum_all[:, -1:, :] - cum_all) * step_all
    xw_all = (x_all * tail_all[..., None]).astype(half)
    state_local_all = jnp.einsum("bthp,btn->bhpn", xw_all, b_all, preferred_element_type=fl)

    state_in = jnp.zeros((head_count, head_dim, state_dim), fl)
    for k in range(n_blocks - 1):
        new = gate_all[k][:, None, None] * state_in + state_local_all[k]
        state_in = jnp.where(k < my_block, new, state_in)

    grad_heads = grad_out[0].reshape(tok_rows, head_count, head_dim)
    grad_weighted = (grad_heads * head_factor[:, :, None]).astype(half)
    adjoint_local = jnp.einsum("thp,tn->hpn", grad_weighted, c_proj, preferred_element_type=fl)
    adjoint_in = jnp.zeros((head_count, head_dim, state_dim), fl)
    if n_blocks == 4:
        sent = grad_out[0].astype(fl)
        along_x = lax.ppermute(sent, "tm", [(3, 2), (1, 0)])
        along_y = lax.ppermute(sent, "tm", [(3, 1), (2, 0)])
        diagonal = lax.ppermute(sent, "tm", [(2, 1), (3, 0)])
        seen = [
            along_x,
            jnp.where(my_block == 1, diagonal, along_y),
            jnp.where(my_block == 2, along_x, jnp.where(my_block == 1, along_y, diagonal)),
        ]
        c_all = projected_all[:, :, inner_width + state_dim :]
        for k in range(n_blocks - 1, 0, -1):
            later = seen[k - 1].reshape(tok_rows, head_count, head_dim)
            later_weighted = (later * jnp.exp(cum_all[k])[:, :, None]).astype(half)
            later_local = jnp.einsum("thp,tn->hpn", later_weighted, c_all[k], preferred_element_type=fl)
            new = gate_all[k][:, None, None] * adjoint_in + later_local
            adjoint_in = jnp.where(k > my_block, new, adjoint_in)
    else:
        adjoint_all = lax.all_gather(adjoint_local, "tm")
        for k in range(n_blocks - 1, 0, -1):
            new = gate_all[k][:, None, None] * adjoint_in + adjoint_all[k]
            adjoint_in = jnp.where(k > my_block, new, adjoint_in)

    masked = decay_matrix(cum_decay) * step_size.T[:, None, :]
    scores = jnp.dot(c_proj, b_proj.T, preferred_element_type=fl)
    weights = (scores[None] * masked).astype(half)
    state_half = state_in.astype(half)
    adjoint_half = adjoint_in.astype(half)
    output = jnp.einsum("hts,shp->thp", weights, x_heads, preferred_element_type=fl)
    output = (
        output
        + jnp.einsum("tn,hpn->thp", c_proj, state_half, preferred_element_type=fl)
        * head_factor[:, :, None]
    )
    ssd_output = output.reshape(1, tok_rows, inner_width).astype(half)
    grad_x = jnp.einsum("hts,thp->shp", weights, grad_heads, preferred_element_type=fl)
    grad_x = (
        grad_x
        + jnp.einsum("sn,hpn->shp", b_proj, adjoint_half, preferred_element_type=fl)
        * tail_factor[:, :, None]
    )
    pair_scores = jnp.einsum("thp,shp->hts", grad_heads, x_heads, preferred_element_type=fl)
    pair_mixed = jnp.sum(pair_scores * masked, axis=0).astype(half)
    grad_b = jnp.dot(pair_mixed.T, c_proj, preferred_element_type=fl)
    grad_b = grad_b + jnp.einsum("shp,hpn->sn", x_weighted, adjoint_half, preferred_element_type=fl)
    grad_c = jnp.dot(pair_mixed, b_proj, preferred_element_type=fl)
    grad_c = grad_c + jnp.einsum(
        "thp,hpn->tn", grad_weighted, state_half, preferred_element_type=fl
    )
    grad_rows = jnp.concatenate(
        [
            grad_x.reshape(tok_rows, inner_width).astype(half),
            grad_b.astype(half),
            grad_c.astype(half),
        ],
        axis=1,
    )
    local_grad = jnp.einsum("tw,tf->wf", grad_rows, features, preferred_element_type=fl)
    total_grad = tree_psum(local_grad).T
    grad_in = total_grad / math.sqrt(series_count * seq_len)
    return (ssd_output, grad_in)


def solution(mesh):
    return jax.shard_map(
        on_device,
        mesh=mesh,
        in_specs=(P(None, ("tm", "series")), P(), P(), P(), P(), P(), P(), P("series", "tm", None)),
        out_specs=(P("series", "tm", None), P()),
        check_vma=False,
    )
```

```python
import math

import jax
import jax.numpy as jnp
from jax import lax
from jax.sharding import PartitionSpec as P

code_ceiling = 2097152.0


def decay_matrix(cum_decay):
    row_count = cum_decay.shape[0]
    causal = jnp.arange(row_count)[:, None] >= jnp.arange(row_count)[None, :]
    log_span = cum_decay.T[:, :, None] - cum_decay.T[:, None, :]
    return jnp.where(causal[None], jnp.exp(jnp.where(causal[None], log_span, -60.0)), 0.0)


def axis_bits(axis):
    size = lax.axis_size(axis)
    assert size & (size - 1) == 0
    return [1 << k for k in range(size.bit_length() - 1)]


def exchange(value, axis, flip):
    pairs = [(i, i ^ flip) for i in range(lax.axis_size(axis))]
    return lax.ppermute(value, axis, pairs)


def bit_groups():
    tm_bits, series_bits = axis_bits("tm"), axis_bits("series")
    groups = [("series", series_bits[:1])] if series_bits else []
    for axis, bits in (("tm", tm_bits), ("series", series_bits[1:])):
        groups += [(axis, bits[i : i + 2]) for i in range(0, len(bits), 2)]
    return groups


def group_round(value, axis, bits, scatter):
    index = lax.axis_index(axis)
    coord = sum(((index // b) % 2) * (1 << j) for j, b in enumerate(bits))
    size = 1 << len(bits)

    def flip_of(m):
        return sum(b for j, b in enumerate(bits) if (m >> j) & 1)

    rows = value.shape[0]
    if scatter:
        part = rows // size
        keep = lax.dynamic_slice_in_dim(value, coord * part, part)
        got = [
            exchange(lax.dynamic_slice_in_dim(value, (coord ^ m) * part, part), axis, flip_of(m))
            for m in range(1, size)
        ]
        for piece in got:
            keep = keep + piece
        return keep
    got = [value] + [exchange(value, axis, flip_of(m)) for m in range(1, size)]
    stacked = jnp.stack(got)
    return [lax.dynamic_index_in_dim(stacked, coord ^ q, 0, keepdims=False) for q in range(size)]


def tree_psum(value):
    done = []
    for axis, bits in bit_groups():
        if value.shape[0] % (8 << len(bits)) == 0:
            value = group_round(value, axis, bits, True)
            done.append((axis, bits))
        else:
            pieces = group_round(value, axis, bits, False)
            value = pieces[0]
            for piece in pieces[1:]:
                value = value + piece
    for axis, bits in reversed(done):
        value = jnp.concatenate(group_round(value, axis, bits, False))
    return value


def on_device(codes, owner_slot, edges, w_in, w_dt, dt_bias, decay_rate, grad_out):
    fl = jnp.float32
    half = jnp.bfloat16
    tok_rows = grad_out.shape[1]
    head_count = dt_bias.shape[0]
    inner_width = grad_out.shape[2]
    head_dim = inner_width // head_count
    state_dim = (w_in.shape[1] - inner_width) // 2
    n_blocks = lax.axis_size("tm")
    seq_len = tok_rows * n_blocks
    series_count = lax.axis_size("series")
    my_block = lax.axis_index("tm")

    ordered = jnp.take(codes, owner_slot, axis=0).astype(fl)
    outgoing = jnp.tile(ordered, (n_blocks, 1))
    reading = lax.all_to_all(outgoing, ("tm", "series"), split_axis=0, concat_axis=1, tiled=True)[0]
    sent, reading = lax.optimization_barrier((grad_out[0].astype(fl), reading))
    edge_float = edges.astype(fl)
    upper_edge = jnp.concatenate([edge_float[1:], jnp.full((1,), code_ceiling, fl)])
    onehot = (
        (edge_float[None, :] <= reading[:, None]) & (upper_edge[None, :] > reading[:, None])
    ).astype(fl)
    counts = jnp.sum(onehot, axis=0)
    before = jnp.cumsum(counts) - counts
    bin_table = jnp.stack([before, counts, edge_float, upper_edge - edge_float], axis=1)
    picked = jnp.dot(onehot, bin_table, precision=lax.Precision.HIGHEST)
    within_bin = (reading - picked[:, 2]) / picked[:, 3]
    quantile = (picked[:, 0] + picked[:, 1] * within_bin) / seq_len
    frequency = (jnp.arange(w_in.shape[0], dtype=fl) + 0.5) * math.pi
    features_all = jnp.cos(quantile[:, None] * frequency).astype(half)

    def mine(a):
        return lax.dynamic_index_in_dim(a, my_block, axis=0, keepdims=False)

    features_blocks = features_all.reshape(n_blocks, tok_rows, -1)
    features = mine(features_blocks)
    projected = jnp.dot(features, w_in, preferred_element_type=fl).astype(half)
    x_heads = projected[:, :inner_width].reshape(tok_rows, head_count, head_dim)
    b_proj = projected[:, inner_width : inner_width + state_dim]
    c_proj = projected[:, inner_width + state_dim :]
    step_size = jax.nn.softplus(dt_bias + jnp.dot(features, w_dt, preferred_element_type=fl))
    cum_decay = jnp.cumsum(-step_size * decay_rate, axis=0)
    tail_factor = jnp.exp(cum_decay[-1][None, :] - cum_decay) * step_size
    head_factor = jnp.exp(cum_decay)
    x_weighted = (x_heads * tail_factor[:, :, None]).astype(half)

    projected_all = jnp.dot(features_all, w_in, preferred_element_type=fl).astype(half)
    projected_all = projected_all.reshape(n_blocks, tok_rows, -1)
    x_all = projected_all[:, :, :inner_width].reshape(n_blocks, tok_rows, head_count, head_dim)
    b_all = projected_all[:, :, inner_width : inner_width + state_dim]
    step_all = jax.nn.softplus(
        dt_bias + jnp.dot(features_all, w_dt, preferred_element_type=fl)
    ).reshape(n_blocks, tok_rows, head_count)
    cum_all = jnp.cumsum(-step_all * decay_rate, axis=1)
    gate_all = jnp.exp(cum_all[:, -1])
    tail_all = jnp.exp(cum_all[:, -1:, :] - cum_all) * step_all
    xw_all = (x_all * tail_all[..., None]).astype(half)
    state_local_all = jnp.einsum("bthp,btn->bhpn", xw_all, b_all, preferred_element_type=fl)

    state_in = jnp.zeros((head_count, head_dim, state_dim), fl)
    for k in range(n_blocks - 1):
        new = gate_all[k][:, None, None] * state_in + state_local_all[k]
        state_in = jnp.where(k < my_block, new, state_in)

    grad_heads = grad_out[0].reshape(tok_rows, head_count, head_dim)
    grad_weighted = (grad_heads * head_factor[:, :, None]).astype(half)
    adjoint_local = jnp.einsum("thp,tn->hpn", grad_weighted, c_proj, preferred_element_type=fl)
    adjoint_in = jnp.zeros((head_count, head_dim, state_dim), fl)
    if n_blocks == 4:
        along_x = lax.ppermute(sent, "tm", [(3, 2), (1, 0)])
        along_y = lax.ppermute(sent, "tm", [(3, 1), (2, 0)])
        diagonal = lax.ppermute(sent, "tm", [(2, 1), (3, 0)])
        seen = [
            along_x,
            jnp.where(my_block == 1, diagonal, along_y),
            jnp.where(my_block == 2, along_x, jnp.where(my_block == 1, along_y, diagonal)),
        ]
        c_all = projected_all[:, :, inner_width + state_dim :]
        for k in range(n_blocks - 1, 0, -1):
            later = seen[k - 1].reshape(tok_rows, head_count, head_dim)
            later_weighted = (later * jnp.exp(cum_all[k])[:, :, None]).astype(half)
            later_local = jnp.einsum("thp,tn->hpn", later_weighted, c_all[k], preferred_element_type=fl)
            new = gate_all[k][:, None, None] * adjoint_in + later_local
            adjoint_in = jnp.where(k > my_block, new, adjoint_in)
    else:
        adjoint_all = lax.all_gather(adjoint_local, "tm")
        for k in range(n_blocks - 1, 0, -1):
            new = gate_all[k][:, None, None] * adjoint_in + adjoint_all[k]
            adjoint_in = jnp.where(k > my_block, new, adjoint_in)

    masked = decay_matrix(cum_decay) * step_size.T[:, None, :]
    scores = jnp.dot(c_proj, b_proj.T, preferred_element_type=fl)
    weights = (scores[None] * masked).astype(half)
    state_half = state_in.astype(half)
    adjoint_half = adjoint_in.astype(half)
    output = jnp.einsum("hts,shp->thp", weights, x_heads, preferred_element_type=fl)
    output = (
        output
        + jnp.einsum("tn,hpn->thp", c_proj, state_half, preferred_element_type=fl)
        * head_factor[:, :, None]
    )
    ssd_output = output.reshape(1, tok_rows, inner_width).astype(half)
    grad_x = jnp.einsum("hts,thp->shp", weights, grad_heads, preferred_element_type=fl)
    grad_x = (
        grad_x
        + jnp.einsum("sn,hpn->shp", b_proj, adjoint_half, preferred_element_type=fl)
        * tail_factor[:, :, None]
    )
    pair_scores = jnp.einsum("thp,shp->hts", grad_heads, x_heads, preferred_element_type=fl)
    pair_mixed = jnp.sum(pair_scores * masked, axis=0).astype(half)
    grad_b = jnp.dot(pair_mixed.T, c_proj, preferred_element_type=fl)
    grad_b = grad_b + jnp.einsum("shp,hpn->sn", x_weighted, adjoint_half, preferred_element_type=fl)
    grad_c = jnp.dot(pair_mixed, b_proj, preferred_element_type=fl)
    grad_c = grad_c + jnp.einsum(
        "thp,hpn->tn", grad_weighted, state_half, preferred_element_type=fl
    )
    grad_rows = jnp.concatenate(
        [
            grad_x.reshape(tok_rows, inner_width).astype(half),
            grad_b.astype(half),
            grad_c.astype(half),
        ],
        axis=1,
    )
    local_grad = jnp.einsum("tw,tf->wf", grad_rows, features, preferred_element_type=fl)
    total_grad = tree_psum(local_grad).T
    grad_in = total_grad / math.sqrt(series_count * seq_len)
    return (ssd_output, grad_in)


def solution(mesh):
    return jax.shard_map(
        on_device,
        mesh=mesh,
        in_specs=(P(None, ("tm", "series")), P(), P(), P(), P(), P(), P(), P("series", "tm", None)),
        out_specs=(P("series", "tm", None), P()),
        check_vma=False,
    )
```

```python
import math

import jax
import jax.numpy as jnp
from jax import lax
from jax.sharding import PartitionSpec as P

code_ceiling = 2097152.0


def decay_matrix(cum_decay):
    row_count = cum_decay.shape[0]
    causal = jnp.arange(row_count)[:, None] >= jnp.arange(row_count)[None, :]
    log_span = cum_decay.T[:, :, None] - cum_decay.T[:, None, :]
    return jnp.where(causal[None], jnp.exp(jnp.where(causal[None], log_span, -60.0)), 0.0)


def axis_bits(axis):
    size = lax.axis_size(axis)
    assert size & (size - 1) == 0
    return [1 << k for k in range(size.bit_length() - 1)]


def exchange(value, axis, flip):
    pairs = [(i, i ^ flip) for i in range(lax.axis_size(axis))]
    return lax.ppermute(value, axis, pairs)


def bit_groups():
    tm_bits, series_bits = axis_bits("tm"), axis_bits("series")
    groups = [("series", series_bits[:1])] if series_bits else []
    for axis, bits in (("tm", tm_bits), ("series", series_bits[1:])):
        groups += [(axis, bits[i : i + 2]) for i in range(0, len(bits), 2)]
    return groups


def group_round(value, axis, bits, scatter):
    index = lax.axis_index(axis)
    coord = sum(((index // b) % 2) * (1 << j) for j, b in enumerate(bits))
    size = 1 << len(bits)

    def flip_of(m):
        return sum(b for j, b in enumerate(bits) if (m >> j) & 1)

    rows = value.shape[0]
    if scatter:
        part = rows // size
        keep = lax.dynamic_slice_in_dim(value, coord * part, part)
        got = [
            exchange(lax.dynamic_slice_in_dim(value, (coord ^ m) * part, part), axis, flip_of(m))
            for m in range(1, size)
        ]
        for piece in got:
            keep = keep + piece
        return keep
    got = [value] + [exchange(value, axis, flip_of(m)) for m in range(1, size)]
    stacked = jnp.stack(got)
    return [lax.dynamic_index_in_dim(stacked, coord ^ q, 0, keepdims=False) for q in range(size)]


def tree_psum(value):
    done = []
    for axis, bits in bit_groups():
        if value.shape[0] % (8 << len(bits)) == 0:
            value = group_round(value, axis, bits, True)
            done.append((axis, bits))
        else:
            pieces = group_round(value, axis, bits, False)
            value = pieces[0]
            for piece in pieces[1:]:
                value = value + piece
    for axis, bits in reversed(done):
        value = jnp.concatenate(group_round(value, axis, bits, False))
    return value


def on_device(codes, owner_slot, edges, w_in, w_dt, dt_bias, decay_rate, grad_out):
    fl = jnp.float32
    half = jnp.bfloat16
    tok_rows = grad_out.shape[1]
    head_count = dt_bias.shape[0]
    inner_width = grad_out.shape[2]
    head_dim = inner_width // head_count
    state_dim = (w_in.shape[1] - inner_width) // 2
    n_blocks = lax.axis_size("tm")
    seq_len = tok_rows * n_blocks
    series_count = lax.axis_size("series")
    my_block = lax.axis_index("tm")

    ordered = jnp.take(codes, owner_slot, axis=0).astype(fl)
    outgoing = jnp.tile(ordered, (n_blocks, 1))
    reading = lax.all_to_all(outgoing, ("tm", "series"), split_axis=0, concat_axis=1, tiled=True)[0]
    sent, reading = lax.optimization_barrier((grad_out[0].astype(fl), reading))
    edge_float = edges.astype(fl)
    upper_edge = jnp.concatenate([edge_float[1:], jnp.full((1,), code_ceiling, fl)])
    onehot = (
        (edge_float[None, :] <= reading[:, None]) & (upper_edge[None, :] > reading[:, None])
    ).astype(fl)
    counts = jnp.sum(onehot, axis=0)
    before = jnp.cumsum(counts) - counts
    bin_table = jnp.stack([before, counts, edge_float, upper_edge - edge_float], axis=1)
    picked = jnp.dot(onehot, bin_table, precision=lax.Precision.HIGHEST)
    within_bin = (reading - picked[:, 2]) / picked[:, 3]
    quantile = (picked[:, 0] + picked[:, 1] * within_bin) / seq_len
    frequency = (jnp.arange(w_in.shape[0], dtype=fl) + 0.5) * math.pi
    features_all = jnp.cos(quantile[:, None] * frequency).astype(half)

    def mine(a):
        return lax.dynamic_index_in_dim(a, my_block, axis=0, keepdims=False)

    features_blocks = features_all.reshape(n_blocks, tok_rows, -1)
    features = mine(features_blocks)
    projected = jnp.dot(features, w_in, preferred_element_type=fl).astype(half)
    x_heads = projected[:, :inner_width].reshape(tok_rows, head_count, head_dim)
    b_proj = projected[:, inner_width : inner_width + state_dim]
    c_proj = projected[:, inner_width + state_dim :]
    step_size = jax.nn.softplus(dt_bias + jnp.dot(features, w_dt, preferred_element_type=fl))
    cum_decay = jnp.cumsum(-step_size * decay_rate, axis=0)
    tail_factor = jnp.exp(cum_decay[-1][None, :] - cum_decay) * step_size
    head_factor = jnp.exp(cum_decay)
    x_weighted = (x_heads * tail_factor[:, :, None]).astype(half)

    projected_all = jnp.dot(features_all, w_in, preferred_element_type=fl).astype(half)
    projected_all = projected_all.reshape(n_blocks, tok_rows, -1)
    x_all = projected_all[:, :, :inner_width].reshape(n_blocks, tok_rows, head_count, head_dim)
    b_all = projected_all[:, :, inner_width : inner_width + state_dim]
    step_all = jax.nn.softplus(
        dt_bias + jnp.dot(features_all, w_dt, preferred_element_type=fl)
    ).reshape(n_blocks, tok_rows, head_count)
    cum_all = jnp.cumsum(-step_all * decay_rate, axis=1)
    gate_all = jnp.exp(cum_all[:, -1])
    tail_all = jnp.exp(cum_all[:, -1:, :] - cum_all) * step_all
    earlier = n_blocks - 1
    xw_all = (x_all[:earlier] * tail_all[:earlier, :, :, None]).astype(half)
    xw_all = xw_all.reshape(earlier, tok_rows, inner_width)
    state_local_t = jnp.einsum("btn,btk->bnk", b_all[:earlier], xw_all, preferred_element_type=fl)

    state_t = jnp.zeros((state_dim, inner_width), fl)
    for k in range(earlier):
        gate_row = jnp.repeat(gate_all[k], head_dim)[None, :]
        new = gate_row * state_t + state_local_t[k]
        state_t = jnp.where(k < my_block, new, state_t)
    state_in = state_t.reshape(state_dim, head_count, head_dim).transpose(1, 2, 0)

    grad_heads = grad_out[0].reshape(tok_rows, head_count, head_dim)
    grad_weighted = (grad_heads * head_factor[:, :, None]).astype(half)
    adjoint_local = jnp.einsum("thp,tn->hpn", grad_weighted, c_proj, preferred_element_type=fl)
    adjoint_in = jnp.zeros((head_count, head_dim, state_dim), fl)
    if n_blocks == 4:
        along_x = lax.ppermute(sent, "tm", [(3, 2), (1, 0)])
        along_y = lax.ppermute(sent, "tm", [(3, 1), (2, 0)])
        diagonal = lax.ppermute(sent, "tm", [(2, 1), (3, 0)])
        seen = [
            along_x,
            jnp.where(my_block == 1, diagonal, along_y),
            jnp.where(my_block == 2, along_x, jnp.where(my_block == 1, along_y, diagonal)),
        ]
        c_all = projected_all[:, :, inner_width + state_dim :]
        for k in range(n_blocks - 1, 0, -1):
            later = seen[k - 1].reshape(tok_rows, head_count, head_dim)
            later_weighted = (later * jnp.exp(cum_all[k])[:, :, None]).astype(half)
            later_local = jnp.einsum("thp,tn->hpn", later_weighted, c_all[k], preferred_element_type=fl)
            new = gate_all[k][:, None, None] * adjoint_in + later_local
            adjoint_in = jnp.where(k > my_block, new, adjoint_in)
    else:
        adjoint_all = lax.all_gather(adjoint_local, "tm")
        for k in range(n_blocks - 1, 0, -1):
            new = gate_all[k][:, None, None] * adjoint_in + adjoint_all[k]
            adjoint_in = jnp.where(k > my_block, new, adjoint_in)

    masked = decay_matrix(cum_decay) * step_size.T[:, None, :]
    scores = jnp.dot(c_proj, b_proj.T, preferred_element_type=fl)
    weights = (scores[None] * masked).astype(half)
    state_half = state_in.astype(half)
    adjoint_half = adjoint_in.astype(half)
    output = jnp.einsum("hts,shp->thp", weights, x_heads, preferred_element_type=fl)
    output = (
        output
        + jnp.einsum("tn,hpn->thp", c_proj, state_half, preferred_element_type=fl)
        * head_factor[:, :, None]
    )
    ssd_output = output.reshape(1, tok_rows, inner_width).astype(half)
    grad_x = jnp.einsum("hts,thp->shp", weights, grad_heads, preferred_element_type=fl)
    grad_x = (
        grad_x
        + jnp.einsum("sn,hpn->shp", b_proj, adjoint_half, preferred_element_type=fl)
        * tail_factor[:, :, None]
    )
    pair_scores = jnp.einsum("thp,shp->hts", grad_heads, x_heads, preferred_element_type=fl)
    pair_mixed = jnp.sum(pair_scores * masked, axis=0).astype(half)
    grad_b = jnp.dot(pair_mixed.T, c_proj, preferred_element_type=fl)
    grad_b = grad_b + jnp.einsum("shp,hpn->sn", x_weighted, adjoint_half, preferred_element_type=fl)
    grad_c = jnp.dot(pair_mixed, b_proj, preferred_element_type=fl)
    grad_c = grad_c + jnp.einsum(
        "thp,hpn->tn", grad_weighted, state_half, preferred_element_type=fl
    )
    grad_rows = jnp.concatenate(
        [
            grad_x.reshape(tok_rows, inner_width).astype(half),
            grad_b.astype(half),
            grad_c.astype(half),
        ],
        axis=1,
    )
    local_grad = jnp.einsum("tw,tf->wf", grad_rows, features, preferred_element_type=fl)
    total_grad = tree_psum(local_grad).T
    grad_in = total_grad / math.sqrt(series_count * seq_len)
    return (ssd_output, grad_in)


def solution(mesh):
    return jax.shard_map(
        on_device,
        mesh=mesh,
        in_specs=(P(None, ("tm", "series")), P(), P(), P(), P(), P(), P(), P("series", "tm", None)),
        out_specs=(P("series", "tm", None), P()),
        check_vma=False,
    )
```

```python
import math

import jax
import jax.numpy as jnp
from jax import lax
from jax.sharding import PartitionSpec as P

code_ceiling = 2097152.0


def decay_matrix(cum_decay):
    row_count = cum_decay.shape[0]
    causal = jnp.arange(row_count)[:, None] >= jnp.arange(row_count)[None, :]
    log_span = cum_decay.T[:, :, None] - cum_decay.T[:, None, :]
    return jnp.where(causal[None], jnp.exp(jnp.where(causal[None], log_span, -60.0)), 0.0)


def axis_bits(axis):
    size = lax.axis_size(axis)
    assert size & (size - 1) == 0
    return [1 << k for k in range(size.bit_length() - 1)]


def exchange(value, axis, flip):
    pairs = [(i, i ^ flip) for i in range(lax.axis_size(axis))]
    return lax.ppermute(value, axis, pairs)


def bit_groups():
    tm_bits, series_bits = axis_bits("tm"), axis_bits("series")
    groups = [("series", series_bits[:1])] if series_bits else []
    for axis, bits in (("tm", tm_bits), ("series", series_bits[1:])):
        groups += [(axis, bits[i : i + 2]) for i in range(0, len(bits), 2)]
    return groups


def group_round(value, axis, bits, scatter):
    index = lax.axis_index(axis)
    coord = sum(((index // b) % 2) * (1 << j) for j, b in enumerate(bits))
    size = 1 << len(bits)

    def flip_of(m):
        return sum(b for j, b in enumerate(bits) if (m >> j) & 1)

    rows = value.shape[0]
    if scatter:
        part = rows // size
        keep = lax.dynamic_slice_in_dim(value, coord * part, part)
        got = [
            exchange(lax.dynamic_slice_in_dim(value, (coord ^ m) * part, part), axis, flip_of(m))
            for m in range(1, size)
        ]
        for piece in got:
            keep = keep + piece
        return keep
    got = [value] + [exchange(value, axis, flip_of(m)) for m in range(1, size)]
    stacked = jnp.stack(got)
    return [lax.dynamic_index_in_dim(stacked, coord ^ q, 0, keepdims=False) for q in range(size)]


def tree_psum(value):
    done = []
    for axis, bits in bit_groups():
        if value.shape[0] % (8 << len(bits)) == 0:
            value = group_round(value, axis, bits, True)
            done.append((axis, bits))
        else:
            pieces = group_round(value, axis, bits, False)
            value = pieces[0]
            for piece in pieces[1:]:
                value = value + piece
    for axis, bits in reversed(done):
        value = jnp.concatenate(group_round(value, axis, bits, False))
    return value


def on_device(codes, owner_slot, edges, w_in, w_dt, dt_bias, decay_rate, grad_out):
    fl = jnp.float32
    half = jnp.bfloat16
    tok_rows = grad_out.shape[1]
    head_count = dt_bias.shape[0]
    inner_width = grad_out.shape[2]
    head_dim = inner_width // head_count
    state_dim = (w_in.shape[1] - inner_width) // 2
    n_blocks = lax.axis_size("tm")
    seq_len = tok_rows * n_blocks
    series_count = lax.axis_size("series")
    my_block = lax.axis_index("tm")

    ordered = jnp.take(codes, owner_slot, axis=0).astype(fl)
    outgoing = jnp.tile(ordered, (n_blocks, 1))
    reading = lax.all_to_all(outgoing, ("tm", "series"), split_axis=0, concat_axis=1, tiled=True)[0]
    sent, reading = lax.optimization_barrier((grad_out[0].astype(fl), reading))
    edge_float = edges.astype(fl)
    upper_edge = jnp.concatenate([edge_float[1:], jnp.full((1,), code_ceiling, fl)])
    onehot = (
        (edge_float[None, :] <= reading[:, None]) & (upper_edge[None, :] > reading[:, None])
    ).astype(fl)
    counts = jnp.sum(onehot, axis=0)
    before = jnp.cumsum(counts) - counts
    bin_table = jnp.stack([before, counts, edge_float, upper_edge - edge_float], axis=1)
    picked = jnp.dot(onehot, bin_table, precision=lax.Precision.HIGHEST)
    within_bin = (reading - picked[:, 2]) / picked[:, 3]
    quantile = (picked[:, 0] + picked[:, 1] * within_bin) / seq_len
    frequency = (jnp.arange(w_in.shape[0], dtype=fl) + 0.5) * math.pi
    features_all = jnp.cos(quantile[:, None] * frequency).astype(half)

    def mine(a):
        return lax.dynamic_index_in_dim(a, my_block, axis=0, keepdims=False)

    features_blocks = features_all.reshape(n_blocks, tok_rows, -1)
    features = mine(features_blocks)
    projected = jnp.dot(features, w_in, preferred_element_type=fl).astype(half)
    x_heads = projected[:, :inner_width].reshape(tok_rows, head_count, head_dim)
    b_proj = projected[:, inner_width : inner_width + state_dim]
    c_proj = projected[:, inner_width + state_dim :]
    step_size = jax.nn.softplus(dt_bias + jnp.dot(features, w_dt, preferred_element_type=fl))
    cum_decay = jnp.cumsum(-step_size * decay_rate, axis=0)
    tail_factor = jnp.exp(cum_decay[-1][None, :] - cum_decay) * step_size
    head_factor = jnp.exp(cum_decay)
    x_weighted = (x_heads * tail_factor[:, :, None]).astype(half)

    projected_all = jnp.dot(features_all, w_in, preferred_element_type=fl).astype(half)
    projected_all = projected_all.reshape(n_blocks, tok_rows, -1)
    x_all = projected_all[:, :, :inner_width].reshape(n_blocks, tok_rows, head_count, head_dim)
    b_all = projected_all[:, :, inner_width : inner_width + state_dim]
    step_all = jax.nn.softplus(
        dt_bias + jnp.dot(features_all, w_dt, preferred_element_type=fl)
    ).reshape(n_blocks, tok_rows, head_count)
    cum_all = jnp.cumsum(-step_all * decay_rate, axis=1)
    gate_all = jnp.exp(cum_all[:, -1])
    tail_all = jnp.exp(cum_all[:, -1:, :] - cum_all) * step_all
    head_all = jnp.exp(cum_all)
    earlier = n_blocks - 1
    xw_all = (x_all[:earlier] * tail_all[:earlier, :, :, None]).astype(half)
    state_local_all = jnp.einsum(
        "bthp,btn->bhpn", xw_all, b_all[:earlier], preferred_element_type=fl
    )

    state_in = jnp.zeros((head_count, head_dim, state_dim), fl)
    for k in range(n_blocks - 1):
        new = gate_all[k][:, None, None] * state_in + state_local_all[k]
        state_in = jnp.where(k < my_block, new, state_in)

    grad_heads = grad_out[0].reshape(tok_rows, head_count, head_dim)
    grad_weighted = (grad_heads * head_factor[:, :, None]).astype(half)
    adjoint_local = jnp.einsum("thp,tn->hpn", grad_weighted, c_proj, preferred_element_type=fl)
    adjoint_in = jnp.zeros((head_count, head_dim, state_dim), fl)
    if n_blocks == 4:
        along_x = lax.ppermute(sent, "tm", [(3, 2), (1, 0)])
        along_y = lax.ppermute(sent, "tm", [(3, 1), (2, 0)])
        diagonal = lax.ppermute(sent, "tm", [(2, 1), (3, 0)])
        seen = [
            along_x,
            jnp.where(my_block == 1, diagonal, along_y),
            jnp.where(my_block == 2, along_x, jnp.where(my_block == 1, along_y, diagonal)),
        ]
        c_all = projected_all[:, :, inner_width + state_dim :]
        for k in range(n_blocks - 1, 0, -1):
            later = seen[k - 1].reshape(tok_rows, head_count, head_dim)
            later_weighted = (later * head_all[k][:, :, None]).astype(half)
            later_local = jnp.einsum("thp,tn->hpn", later_weighted, c_all[k], preferred_element_type=fl)
            new = gate_all[k][:, None, None] * adjoint_in + later_local
            adjoint_in = jnp.where(k > my_block, new, adjoint_in)
    else:
        adjoint_all = lax.all_gather(adjoint_local, "tm")
        for k in range(n_blocks - 1, 0, -1):
            new = gate_all[k][:, None, None] * adjoint_in + adjoint_all[k]
            adjoint_in = jnp.where(k > my_block, new, adjoint_in)

    masked = decay_matrix(cum_decay) * step_size.T[:, None, :]
    scores = jnp.dot(c_proj, b_proj.T, preferred_element_type=fl)
    weights = (scores[None] * masked).astype(half)
    state_half = state_in.astype(half)
    adjoint_half = adjoint_in.astype(half)
    output = jnp.einsum("hts,shp->thp", weights, x_heads, preferred_element_type=fl)
    output = (
        output
        + jnp.einsum("tn,hpn->thp", c_proj, state_half, preferred_element_type=fl)
        * head_factor[:, :, None]
    )
    ssd_output = output.reshape(1, tok_rows, inner_width).astype(half)
    grad_x = jnp.einsum("hts,thp->shp", weights, grad_heads, preferred_element_type=fl)
    grad_x = (
        grad_x
        + jnp.einsum("sn,hpn->shp", b_proj, adjoint_half, preferred_element_type=fl)
        * tail_factor[:, :, None]
    )
    pair_scores = jnp.einsum("thp,shp->hts", grad_heads, x_heads, preferred_element_type=fl)
    pair_mixed = jnp.sum(pair_scores * masked, axis=0).astype(half)
    grad_b = jnp.dot(pair_mixed.T, c_proj, preferred_element_type=fl)
    grad_b = grad_b + jnp.einsum("shp,hpn->sn", x_weighted, adjoint_half, preferred_element_type=fl)
    grad_c = jnp.dot(pair_mixed, b_proj, preferred_element_type=fl)
    grad_c = grad_c + jnp.einsum(
        "thp,hpn->tn", grad_weighted, state_half, preferred_element_type=fl
    )
    grad_rows = jnp.concatenate(
        [
            grad_x.reshape(tok_rows, inner_width).astype(half),
            grad_b.astype(half),
            grad_c.astype(half),
        ],
        axis=1,
    )
    local_grad = jnp.einsum("tw,tf->wf", grad_rows, features, preferred_element_type=fl)
    total_grad = tree_psum(local_grad).T
    grad_in = total_grad / math.sqrt(series_count * seq_len)
    return (ssd_output, grad_in)


def solution(mesh):
    return jax.shard_map(
        on_device,
        mesh=mesh,
        in_specs=(P(None, ("tm", "series")), P(), P(), P(), P(), P(), P(), P("series", "tm", None)),
        out_specs=(P("series", "tm", None), P()),
        check_vma=False,
    )
```

```python
import math

import jax
import jax.numpy as jnp
from jax import lax
from jax.sharding import PartitionSpec as P

code_ceiling = 2097152.0


def decay_matrix(cum_decay):
    row_count = cum_decay.shape[0]
    causal = jnp.arange(row_count)[:, None] >= jnp.arange(row_count)[None, :]
    log_span = cum_decay.T[:, :, None] - cum_decay.T[:, None, :]
    return jnp.where(causal[None], jnp.exp(jnp.where(causal[None], log_span, -60.0)), 0.0)


def axis_bits(axis):
    size = lax.axis_size(axis)
    assert size & (size - 1) == 0
    return [1 << k for k in range(size.bit_length() - 1)]


def exchange(value, axis, flip):
    pairs = [(i, i ^ flip) for i in range(lax.axis_size(axis))]
    return lax.ppermute(value, axis, pairs)


def bit_groups():
    tm_bits, series_bits = axis_bits("tm"), axis_bits("series")
    groups = [("series", series_bits[:1])] if series_bits else []
    for axis, bits in (("tm", tm_bits), ("series", series_bits[1:])):
        groups += [(axis, bits[i : i + 2]) for i in range(0, len(bits), 2)]
    return groups


def group_round(value, axis, bits, scatter):
    index = lax.axis_index(axis)
    coord = sum(((index // b) % 2) * (1 << j) for j, b in enumerate(bits))
    size = 1 << len(bits)

    def flip_of(m):
        return sum(b for j, b in enumerate(bits) if (m >> j) & 1)

    rows = value.shape[0]
    if scatter:
        part = rows // size
        keep = lax.dynamic_slice_in_dim(value, coord * part, part)
        got = [
            exchange(lax.dynamic_slice_in_dim(value, (coord ^ m) * part, part), axis, flip_of(m))
            for m in range(1, size)
        ]
        for piece in got:
            keep = keep + piece
        return keep
    got = [value] + [exchange(value, axis, flip_of(m)) for m in range(1, size)]
    stacked = jnp.stack(got)
    return [lax.dynamic_index_in_dim(stacked, coord ^ q, 0, keepdims=False) for q in range(size)]


def tree_psum(value):
    done = []
    for axis, bits in bit_groups():
        if value.shape[0] % (8 << len(bits)) == 0:
            value = group_round(value, axis, bits, True)
            done.append((axis, bits))
        else:
            pieces = group_round(value, axis, bits, False)
            value = pieces[0]
            for piece in pieces[1:]:
                value = value + piece
    for axis, bits in reversed(done):
        value = jnp.concatenate(group_round(value, axis, bits, False))
    return value


def on_device(codes, owner_slot, edges, w_in, w_dt, dt_bias, decay_rate, grad_out):
    fl = jnp.float32
    half = jnp.bfloat16
    tok_rows = grad_out.shape[1]
    head_count = dt_bias.shape[0]
    inner_width = grad_out.shape[2]
    head_dim = inner_width // head_count
    state_dim = (w_in.shape[1] - inner_width) // 2
    n_blocks = lax.axis_size("tm")
    seq_len = tok_rows * n_blocks
    series_count = lax.axis_size("series")
    my_block = lax.axis_index("tm")

    ordered = jnp.take(codes, owner_slot, axis=0).astype(fl)
    outgoing = jnp.tile(ordered, (n_blocks, 1))
    reading = lax.all_to_all(outgoing, ("tm", "series"), split_axis=0, concat_axis=1, tiled=True)[0]
    sent, reading = lax.optimization_barrier((grad_out[0].astype(fl), reading))
    edge_float = edges.astype(fl)
    upper_edge = jnp.concatenate([edge_float[1:], jnp.full((1,), code_ceiling, fl)])
    onehot = (
        (edge_float[None, :] <= reading[:, None]) & (upper_edge[None, :] > reading[:, None])
    ).astype(fl)
    counts = jnp.sum(onehot, axis=0)
    before = jnp.cumsum(counts) - counts
    bin_table = jnp.stack([before, counts, edge_float, upper_edge - edge_float], axis=1)
    high = jnp.floor(bin_table / 65536.0) * 65536.0
    middle = jnp.floor((bin_table - high) / 256.0) * 256.0
    low = bin_table - high - middle
    pieces = jnp.concatenate([high, middle, low], axis=1).astype(half)
    picked3 = jnp.dot(onehot.astype(half), pieces, preferred_element_type=fl)
    width = bin_table.shape[1]
    picked = picked3[:, :width] + picked3[:, width : 2 * width] + picked3[:, 2 * width :]
    within_bin = (reading - picked[:, 2]) / picked[:, 3]
    quantile = (picked[:, 0] + picked[:, 1] * within_bin) / seq_len
    frequency = (jnp.arange(w_in.shape[0], dtype=fl) + 0.5) * math.pi
    features_all = jnp.cos(quantile[:, None] * frequency).astype(half)

    def mine(a):
        return lax.dynamic_index_in_dim(a, my_block, axis=0, keepdims=False)

    features_blocks = features_all.reshape(n_blocks, tok_rows, -1)
    features = mine(features_blocks)
    projected = jnp.dot(features, w_in, preferred_element_type=fl).astype(half)
    x_heads = projected[:, :inner_width].reshape(tok_rows, head_count, head_dim)
    b_proj = projected[:, inner_width : inner_width + state_dim]
    c_proj = projected[:, inner_width + state_dim :]
    step_size = jax.nn.softplus(dt_bias + jnp.dot(features, w_dt, preferred_element_type=fl))
    cum_decay = jnp.cumsum(-step_size * decay_rate, axis=0)
    tail_factor = jnp.exp(cum_decay[-1][None, :] - cum_decay) * step_size
    head_factor = jnp.exp(cum_decay)
    x_weighted = (x_heads * tail_factor[:, :, None]).astype(half)

    projected_all = jnp.dot(features_all, w_in, preferred_element_type=fl).astype(half)
    projected_all = projected_all.reshape(n_blocks, tok_rows, -1)
    x_all = projected_all[:, :, :inner_width].reshape(n_blocks, tok_rows, head_count, head_dim)
    b_all = projected_all[:, :, inner_width : inner_width + state_dim]
    step_all = jax.nn.softplus(
        dt_bias + jnp.dot(features_all, w_dt, preferred_element_type=fl)
    ).reshape(n_blocks, tok_rows, head_count)
    cum_all = jnp.cumsum(-step_all * decay_rate, axis=1)
    gate_all = jnp.exp(cum_all[:, -1])
    tail_all = jnp.exp(cum_all[:, -1:, :] - cum_all) * step_all
    head_all = jnp.exp(cum_all)
    earlier = n_blocks - 1
    xw_all = (x_all[:earlier] * tail_all[:earlier, :, :, None]).astype(half)
    state_local_all = jnp.einsum(
        "bthp,btn->bhpn", xw_all, b_all[:earlier], preferred_element_type=fl
    )

    state_in = jnp.zeros((head_count, head_dim, state_dim), fl)
    for k in range(n_blocks - 1):
        new = gate_all[k][:, None, None] * state_in + state_local_all[k]
        state_in = jnp.where(k < my_block, new, state_in)

    grad_heads = grad_out[0].reshape(tok_rows, head_count, head_dim)
    grad_weighted = (grad_heads * head_factor[:, :, None]).astype(half)
    adjoint_local = jnp.einsum("thp,tn->hpn", grad_weighted, c_proj, preferred_element_type=fl)
    adjoint_in = jnp.zeros((head_count, head_dim, state_dim), fl)
    if n_blocks == 4:
        along_x = lax.ppermute(sent, "tm", [(3, 2), (1, 0)])
        along_y = lax.ppermute(sent, "tm", [(3, 1), (2, 0)])
        diagonal = lax.ppermute(sent, "tm", [(2, 1), (3, 0)])
        seen = [
            along_x,
            jnp.where(my_block == 1, diagonal, along_y),
            jnp.where(my_block == 2, along_x, jnp.where(my_block == 1, along_y, diagonal)),
        ]
        c_all = projected_all[:, :, inner_width + state_dim :]
        for k in range(n_blocks - 1, 0, -1):
            later = seen[k - 1].reshape(tok_rows, head_count, head_dim)
            later_weighted = (later * head_all[k][:, :, None]).astype(half)
            later_local = jnp.einsum("thp,tn->hpn", later_weighted, c_all[k], preferred_element_type=fl)
            new = gate_all[k][:, None, None] * adjoint_in + later_local
            adjoint_in = jnp.where(k > my_block, new, adjoint_in)
    else:
        adjoint_all = lax.all_gather(adjoint_local, "tm")
        for k in range(n_blocks - 1, 0, -1):
            new = gate_all[k][:, None, None] * adjoint_in + adjoint_all[k]
            adjoint_in = jnp.where(k > my_block, new, adjoint_in)

    masked = decay_matrix(cum_decay) * step_size.T[:, None, :]
    scores = jnp.dot(c_proj, b_proj.T, preferred_element_type=fl)
    weights = (scores[None] * masked).astype(half)
    state_half = state_in.astype(half)
    adjoint_half = adjoint_in.astype(half)
    output = jnp.einsum("hts,shp->thp", weights, x_heads, preferred_element_type=fl)
    output = (
        output
        + jnp.einsum("tn,hpn->thp", c_proj, state_half, preferred_element_type=fl)
        * head_factor[:, :, None]
    )
    ssd_output = output.reshape(1, tok_rows, inner_width).astype(half)
    grad_x = jnp.einsum("hts,thp->shp", weights, grad_heads, preferred_element_type=fl)
    grad_x = (
        grad_x
        + jnp.einsum("sn,hpn->shp", b_proj, adjoint_half, preferred_element_type=fl)
        * tail_factor[:, :, None]
    )
    pair_scores = jnp.einsum("thp,shp->hts", grad_heads, x_heads, preferred_element_type=fl)
    pair_mixed = jnp.sum(pair_scores * masked, axis=0).astype(half)
    grad_b = jnp.dot(pair_mixed.T, c_proj, preferred_element_type=fl)
    grad_b = grad_b + jnp.einsum("shp,hpn->sn", x_weighted, adjoint_half, preferred_element_type=fl)
    grad_c = jnp.dot(pair_mixed, b_proj, preferred_element_type=fl)
    grad_c = grad_c + jnp.einsum(
        "thp,hpn->tn", grad_weighted, state_half, preferred_element_type=fl
    )
    grad_rows = jnp.concatenate(
        [
            grad_x.reshape(tok_rows, inner_width).astype(half),
            grad_b.astype(half),
            grad_c.astype(half),
        ],
        axis=1,
    )
    local_grad = jnp.einsum("tw,tf->wf", grad_rows, features, preferred_element_type=fl)
    total_grad = tree_psum(local_grad).T
    grad_in = total_grad / math.sqrt(series_count * seq_len)
    return (ssd_output, grad_in)


def solution(mesh):
    return jax.shard_map(
        on_device,
        mesh=mesh,
        in_specs=(P(None, ("tm", "series")), P(), P(), P(), P(), P(), P(), P("series", "tm", None)),
        out_specs=(P("series", "tm", None), P()),
        check_vma=False,
    )
```

```python
import math

import jax
import jax.numpy as jnp
from jax import lax
from jax.sharding import PartitionSpec as P

code_ceiling = 2097152.0


def decay_matrix(cum_decay):
    row_count = cum_decay.shape[0]
    causal = jnp.arange(row_count)[:, None] >= jnp.arange(row_count)[None, :]
    log_span = cum_decay.T[:, :, None] - cum_decay.T[:, None, :]
    return jnp.where(causal[None], jnp.exp(jnp.where(causal[None], log_span, -60.0)), 0.0)


def axis_bits(axis):
    size = lax.axis_size(axis)
    assert size & (size - 1) == 0
    return [1 << k for k in range(size.bit_length() - 1)]


def exchange(value, axis, flip):
    pairs = [(i, i ^ flip) for i in range(lax.axis_size(axis))]
    return lax.ppermute(value, axis, pairs)


def bit_groups():
    tm_bits, series_bits = axis_bits("tm"), axis_bits("series")
    groups = [("series", series_bits[:1])] if series_bits else []
    for axis, bits in (("tm", tm_bits), ("series", series_bits[1:])):
        groups += [(axis, bits[i : i + 2]) for i in range(0, len(bits), 2)]
    return groups


def group_round(value, axis, bits, scatter):
    index = lax.axis_index(axis)
    coord = sum(((index // b) % 2) * (1 << j) for j, b in enumerate(bits))
    size = 1 << len(bits)

    def flip_of(m):
        return sum(b for j, b in enumerate(bits) if (m >> j) & 1)

    rows = value.shape[0]
    if scatter:
        part = rows // size
        keep = lax.dynamic_slice_in_dim(value, coord * part, part)
        got = [
            exchange(lax.dynamic_slice_in_dim(value, (coord ^ m) * part, part), axis, flip_of(m))
            for m in range(1, size)
        ]
        for piece in got:
            keep = keep + piece
        return keep
    got = [value] + [exchange(value, axis, flip_of(m)) for m in range(1, size)]
    stacked = jnp.stack(got)
    return [lax.dynamic_index_in_dim(stacked, coord ^ q, 0, keepdims=False) for q in range(size)]


def tree_psum(value):
    done = []
    for axis, bits in bit_groups():
        if value.shape[0] % (8 << len(bits)) == 0:
            value = group_round(value, axis, bits, True)
            done.append((axis, bits))
        else:
            pieces = group_round(value, axis, bits, False)
            value = pieces[0]
            for piece in pieces[1:]:
                value = value + piece
    for axis, bits in reversed(done):
        value = jnp.concatenate(group_round(value, axis, bits, False))
    return value


def on_device(codes, owner_slot, edges, w_in, w_dt, dt_bias, decay_rate, grad_out):
    fl = jnp.float32
    half = jnp.bfloat16
    tok_rows = grad_out.shape[1]
    head_count = dt_bias.shape[0]
    inner_width = grad_out.shape[2]
    head_dim = inner_width // head_count
    state_dim = (w_in.shape[1] - inner_width) // 2
    n_blocks = lax.axis_size("tm")
    seq_len = tok_rows * n_blocks
    series_count = lax.axis_size("series")
    my_block = lax.axis_index("tm")

    ordered = jnp.take(codes, owner_slot, axis=0).astype(fl)
    outgoing = jnp.tile(ordered, (n_blocks, 1))
    reading = lax.all_to_all(outgoing, ("tm", "series"), split_axis=0, concat_axis=1, tiled=True)[0]
    sent, reading = lax.optimization_barrier((grad_out[0].astype(fl), reading))
    edge_float = edges.astype(fl)
    upper_edge = jnp.concatenate([edge_float[1:], jnp.full((1,), code_ceiling, fl)])
    onehot = (
        (edge_float[None, :] <= reading[:, None]) & (upper_edge[None, :] > reading[:, None])
    ).astype(fl)
    counts = jnp.sum(onehot, axis=0)
    before = jnp.cumsum(counts) - counts
    bin_table = jnp.stack([before, counts, edge_float, upper_edge - edge_float], axis=1)
    picked = jnp.dot(onehot, bin_table, precision=lax.Precision.HIGHEST)
    within_bin = (reading - picked[:, 2]) / picked[:, 3]
    quantile = (picked[:, 0] + picked[:, 1] * within_bin) / seq_len
    frequency = (jnp.arange(w_in.shape[0], dtype=fl) + 0.5) * math.pi
    features_all = jnp.cos(quantile[:, None] * frequency).astype(half)

    def mine(a):
        return lax.dynamic_index_in_dim(a, my_block, axis=0, keepdims=False)

    features_blocks = features_all.reshape(n_blocks, tok_rows, -1)
    features = mine(features_blocks)
    projected = jnp.dot(features, w_in, preferred_element_type=fl).astype(half)
    x_heads = projected[:, :inner_width].reshape(tok_rows, head_count, head_dim)
    b_proj = projected[:, inner_width : inner_width + state_dim]
    c_proj = projected[:, inner_width + state_dim :]
    step_size = jax.nn.softplus(dt_bias + jnp.dot(features, w_dt, preferred_element_type=fl))
    cum_decay = jnp.cumsum(-step_size * decay_rate, axis=0)
    tail_factor = jnp.exp(cum_decay[-1][None, :] - cum_decay) * step_size
    head_factor = jnp.exp(cum_decay)
    x_weighted = (x_heads * tail_factor[:, :, None]).astype(half)

    projected_all = jnp.dot(features_all, w_in, preferred_element_type=fl).astype(half)
    projected_all = projected_all.reshape(n_blocks, tok_rows, -1)
    x_all = projected_all[:, :, :inner_width].reshape(n_blocks, tok_rows, head_count, head_dim)
    b_all = projected_all[:, :, inner_width : inner_width + state_dim]
    step_all = jax.nn.softplus(
        dt_bias + jnp.dot(features_all, w_dt, preferred_element_type=fl)
    ).reshape(n_blocks, tok_rows, head_count)
    cum_all = jnp.cumsum(-step_all * decay_rate, axis=1)
    gate_all = jnp.exp(cum_all[:, -1])
    tail_all = jnp.exp(cum_all[:, -1:, :] - cum_all) * step_all
    head_all = jnp.exp(cum_all)
    earlier = n_blocks - 1
    xw_all = (x_all[:earlier] * tail_all[:earlier, :, :, None]).astype(half)
    xw_all = lax.optimization_barrier(xw_all)
    state_local_all = jnp.einsum(
        "bthp,btn->bhpn", xw_all, b_all[:earlier], preferred_element_type=fl
    )

    state_in = jnp.zeros((head_count, head_dim, state_dim), fl)
    for k in range(n_blocks - 1):
        new = gate_all[k][:, None, None] * state_in + state_local_all[k]
        state_in = jnp.where(k < my_block, new, state_in)

    grad_heads = grad_out[0].reshape(tok_rows, head_count, head_dim)
    grad_weighted = (grad_heads * head_factor[:, :, None]).astype(half)
    adjoint_local = jnp.einsum("thp,tn->hpn", grad_weighted, c_proj, preferred_element_type=fl)
    adjoint_in = jnp.zeros((head_count, head_dim, state_dim), fl)
    if n_blocks == 4:
        along_x = lax.ppermute(sent, "tm", [(3, 2), (1, 0)])
        along_y = lax.ppermute(sent, "tm", [(3, 1), (2, 0)])
        diagonal = lax.ppermute(sent, "tm", [(2, 1), (3, 0)])
        seen = [
            along_x,
            jnp.where(my_block == 1, diagonal, along_y),
            jnp.where(my_block == 2, along_x, jnp.where(my_block == 1, along_y, diagonal)),
        ]
        c_all = projected_all[:, :, inner_width + state_dim :]
        for k in range(n_blocks - 1, 0, -1):
            later = seen[k - 1].reshape(tok_rows, head_count, head_dim)
            later_weighted = (later * head_all[k][:, :, None]).astype(half)
            later_local = jnp.einsum("thp,tn->hpn", later_weighted, c_all[k], preferred_element_type=fl)
            new = gate_all[k][:, None, None] * adjoint_in + later_local
            adjoint_in = jnp.where(k > my_block, new, adjoint_in)
    else:
        adjoint_all = lax.all_gather(adjoint_local, "tm")
        for k in range(n_blocks - 1, 0, -1):
            new = gate_all[k][:, None, None] * adjoint_in + adjoint_all[k]
            adjoint_in = jnp.where(k > my_block, new, adjoint_in)

    masked = decay_matrix(cum_decay) * step_size.T[:, None, :]
    scores = jnp.dot(c_proj, b_proj.T, preferred_element_type=fl)
    weights = (scores[None] * masked).astype(half)
    state_half = state_in.astype(half)
    adjoint_half = adjoint_in.astype(half)
    output = jnp.einsum("hts,shp->thp", weights, x_heads, preferred_element_type=fl)
    output = (
        output
        + jnp.einsum("tn,hpn->thp", c_proj, state_half, preferred_element_type=fl)
        * head_factor[:, :, None]
    )
    ssd_output = output.reshape(1, tok_rows, inner_width).astype(half)
    grad_x = jnp.einsum("hts,thp->shp", weights, grad_heads, preferred_element_type=fl)
    grad_x = (
        grad_x
        + jnp.einsum("sn,hpn->shp", b_proj, adjoint_half, preferred_element_type=fl)
        * tail_factor[:, :, None]
    )
    pair_scores = jnp.einsum("thp,shp->hts", grad_heads, x_heads, preferred_element_type=fl)
    pair_mixed = jnp.sum(pair_scores * masked, axis=0).astype(half)
    grad_b = jnp.dot(pair_mixed.T, c_proj, preferred_element_type=fl)
    grad_b = grad_b + jnp.einsum("shp,hpn->sn", x_weighted, adjoint_half, preferred_element_type=fl)
    grad_c = jnp.dot(pair_mixed, b_proj, preferred_element_type=fl)
    grad_c = grad_c + jnp.einsum(
        "thp,hpn->tn", grad_weighted, state_half, preferred_element_type=fl
    )
    grad_rows = jnp.concatenate(
        [
            grad_x.reshape(tok_rows, inner_width).astype(half),
            grad_b.astype(half),
            grad_c.astype(half),
        ],
        axis=1,
    )
    local_grad = jnp.einsum("tw,tf->wf", grad_rows, features, preferred_element_type=fl)
    total_grad = tree_psum(local_grad).T
    grad_in = total_grad / math.sqrt(series_count * seq_len)
    return (ssd_output, grad_in)


def solution(mesh):
    return jax.shard_map(
        on_device,
        mesh=mesh,
        in_specs=(P(None, ("tm", "series")), P(), P(), P(), P(), P(), P(), P("series", "tm", None)),
        out_specs=(P("series", "tm", None), P()),
        check_vma=False,
    )
```

```python
import math

import jax
import jax.numpy as jnp
from jax import lax
from jax.sharding import PartitionSpec as P

code_ceiling = 2097152.0


def decay_matrix(cum_decay):
    row_count = cum_decay.shape[0]
    causal = jnp.arange(row_count)[:, None] >= jnp.arange(row_count)[None, :]
    log_span = cum_decay.T[:, :, None] - cum_decay.T[:, None, :]
    return jnp.where(causal[None], jnp.exp(jnp.where(causal[None], log_span, -60.0)), 0.0)


def axis_bits(axis):
    size = lax.axis_size(axis)
    assert size & (size - 1) == 0
    return [1 << k for k in range(size.bit_length() - 1)]


def exchange(value, axis, flip):
    pairs = [(i, i ^ flip) for i in range(lax.axis_size(axis))]
    return lax.ppermute(value, axis, pairs)


def bit_groups():
    tm_bits, series_bits = axis_bits("tm"), axis_bits("series")
    groups = [("series", series_bits[:1])] if series_bits else []
    for axis, bits in (("series", series_bits[1:]), ("tm", tm_bits)):
        groups += [(axis, bits[i : i + 2]) for i in range(0, len(bits), 2)]
    return groups


def group_round(value, axis, bits, scatter):
    index = lax.axis_index(axis)
    coord = sum(((index // b) % 2) * (1 << j) for j, b in enumerate(bits))
    size = 1 << len(bits)

    def flip_of(m):
        return sum(b for j, b in enumerate(bits) if (m >> j) & 1)

    rows = value.shape[0]
    if scatter:
        part = rows // size
        keep = lax.dynamic_slice_in_dim(value, coord * part, part)
        got = [
            exchange(lax.dynamic_slice_in_dim(value, (coord ^ m) * part, part), axis, flip_of(m))
            for m in range(1, size)
        ]
        for piece in got:
            keep = keep + piece
        return keep
    got = [value] + [exchange(value, axis, flip_of(m)) for m in range(1, size)]
    stacked = jnp.stack(got)
    return [lax.dynamic_index_in_dim(stacked, coord ^ q, 0, keepdims=False) for q in range(size)]


def tree_psum(value):
    done = []
    for axis, bits in bit_groups():
        if value.shape[0] % (8 << len(bits)) == 0:
            value = group_round(value, axis, bits, True)
            done.append((axis, bits))
        else:
            pieces = group_round(value, axis, bits, False)
            value = pieces[0]
            for piece in pieces[1:]:
                value = value + piece
    for axis, bits in reversed(done):
        value = jnp.concatenate(group_round(value, axis, bits, False))
    return value


def on_device(codes, owner_slot, edges, w_in, w_dt, dt_bias, decay_rate, grad_out):
    fl = jnp.float32
    half = jnp.bfloat16
    tok_rows = grad_out.shape[1]
    head_count = dt_bias.shape[0]
    inner_width = grad_out.shape[2]
    head_dim = inner_width // head_count
    state_dim = (w_in.shape[1] - inner_width) // 2
    n_blocks = lax.axis_size("tm")
    seq_len = tok_rows * n_blocks
    series_count = lax.axis_size("series")
    my_block = lax.axis_index("tm")

    ordered = jnp.take(codes, owner_slot, axis=0).astype(fl)
    outgoing = jnp.tile(ordered, (n_blocks, 1))
    reading = lax.all_to_all(outgoing, ("tm", "series"), split_axis=0, concat_axis=1, tiled=True)[0]
    sent, reading = lax.optimization_barrier((grad_out[0].astype(fl), reading))
    edge_float = edges.astype(fl)
    upper_edge = jnp.concatenate([edge_float[1:], jnp.full((1,), code_ceiling, fl)])
    onehot = (
        (edge_float[None, :] <= reading[:, None]) & (upper_edge[None, :] > reading[:, None])
    ).astype(fl)
    counts = jnp.sum(onehot, axis=0)
    before = jnp.cumsum(counts) - counts
    bin_table = jnp.stack([before, counts, edge_float, upper_edge - edge_float], axis=1)
    picked = jnp.dot(onehot, bin_table, precision=lax.Precision.HIGHEST)
    within_bin = (reading - picked[:, 2]) / picked[:, 3]
    quantile = (picked[:, 0] + picked[:, 1] * within_bin) / seq_len
    frequency = (jnp.arange(w_in.shape[0], dtype=fl) + 0.5) * math.pi
    features_all = jnp.cos(quantile[:, None] * frequency).astype(half)

    def mine(a):
        return lax.dynamic_index_in_dim(a, my_block, axis=0, keepdims=False)

    features_blocks = features_all.reshape(n_blocks, tok_rows, -1)
    features = mine(features_blocks)
    projected = jnp.dot(features, w_in, preferred_element_type=fl).astype(half)
    x_heads = projected[:, :inner_width].reshape(tok_rows, head_count, head_dim)
    b_proj = projected[:, inner_width : inner_width + state_dim]
    c_proj = projected[:, inner_width + state_dim :]
    step_size = jax.nn.softplus(dt_bias + jnp.dot(features, w_dt, preferred_element_type=fl))
    cum_decay = jnp.cumsum(-step_size * decay_rate, axis=0)
    tail_factor = jnp.exp(cum_decay[-1][None, :] - cum_decay) * step_size
    head_factor = jnp.exp(cum_decay)
    x_weighted = (x_heads * tail_factor[:, :, None]).astype(half)

    projected_all = jnp.dot(features_all, w_in, preferred_element_type=fl).astype(half)
    projected_all = projected_all.reshape(n_blocks, tok_rows, -1)
    x_all = projected_all[:, :, :inner_width].reshape(n_blocks, tok_rows, head_count, head_dim)
    b_all = projected_all[:, :, inner_width : inner_width + state_dim]
    step_all = jax.nn.softplus(
        dt_bias + jnp.dot(features_all, w_dt, preferred_element_type=fl)
    ).reshape(n_blocks, tok_rows, head_count)
    cum_all = jnp.cumsum(-step_all * decay_rate, axis=1)
    gate_all = jnp.exp(cum_all[:, -1])
    tail_all = jnp.exp(cum_all[:, -1:, :] - cum_all) * step_all
    head_all = jnp.exp(cum_all)
    earlier = n_blocks - 1
    xw_all = (x_all[:earlier] * tail_all[:earlier, :, :, None]).astype(half)
    state_local_all = jnp.einsum(
        "bthp,btn->bhpn", xw_all, b_all[:earlier], preferred_element_type=fl
    )

    state_in = jnp.zeros((head_count, head_dim, state_dim), fl)
    for k in range(n_blocks - 1):
        new = gate_all[k][:, None, None] * state_in + state_local_all[k]
        state_in = jnp.where(k < my_block, new, state_in)

    grad_heads = grad_out[0].reshape(tok_rows, head_count, head_dim)
    grad_weighted = (grad_heads * head_factor[:, :, None]).astype(half)
    adjoint_local = jnp.einsum("thp,tn->hpn", grad_weighted, c_proj, preferred_element_type=fl)
    adjoint_in = jnp.zeros((head_count, head_dim, state_dim), fl)
    if n_blocks == 4:
        along_x = lax.ppermute(sent, "tm", [(3, 2), (1, 0)])
        along_y = lax.ppermute(sent, "tm", [(3, 1), (2, 0)])
        diagonal = lax.ppermute(sent, "tm", [(2, 1), (3, 0)])
        seen = [
            along_x,
            jnp.where(my_block == 1, diagonal, along_y),
            jnp.where(my_block == 2, along_x, jnp.where(my_block == 1, along_y, diagonal)),
        ]
        c_all = projected_all[:, :, inner_width + state_dim :]
        for k in range(n_blocks - 1, 0, -1):
            later = seen[k - 1].reshape(tok_rows, head_count, head_dim)
            later_weighted = (later * head_all[k][:, :, None]).astype(half)
            later_local = jnp.einsum("thp,tn->hpn", later_weighted, c_all[k], preferred_element_type=fl)
            new = gate_all[k][:, None, None] * adjoint_in + later_local
            adjoint_in = jnp.where(k > my_block, new, adjoint_in)
    else:
        adjoint_all = lax.all_gather(adjoint_local, "tm")
        for k in range(n_blocks - 1, 0, -1):
            new = gate_all[k][:, None, None] * adjoint_in + adjoint_all[k]
            adjoint_in = jnp.where(k > my_block, new, adjoint_in)

    masked = decay_matrix(cum_decay) * step_size.T[:, None, :]
    scores = jnp.dot(c_proj, b_proj.T, preferred_element_type=fl)
    weights = (scores[None] * masked).astype(half)
    state_half = state_in.astype(half)
    adjoint_half = adjoint_in.astype(half)
    output = jnp.einsum("hts,shp->thp", weights, x_heads, preferred_element_type=fl)
    output = (
        output
        + jnp.einsum("tn,hpn->thp", c_proj, state_half, preferred_element_type=fl)
        * head_factor[:, :, None]
    )
    ssd_output = output.reshape(1, tok_rows, inner_width).astype(half)
    grad_x = jnp.einsum("hts,thp->shp", weights, grad_heads, preferred_element_type=fl)
    grad_x = (
        grad_x
        + jnp.einsum("sn,hpn->shp", b_proj, adjoint_half, preferred_element_type=fl)
        * tail_factor[:, :, None]
    )
    pair_scores = jnp.einsum("thp,shp->hts", grad_heads, x_heads, preferred_element_type=fl)
    pair_mixed = jnp.sum(pair_scores * masked, axis=0).astype(half)
    grad_b = jnp.dot(pair_mixed.T, c_proj, preferred_element_type=fl)
    grad_b = grad_b + jnp.einsum("shp,hpn->sn", x_weighted, adjoint_half, preferred_element_type=fl)
    grad_c = jnp.dot(pair_mixed, b_proj, preferred_element_type=fl)
    grad_c = grad_c + jnp.einsum(
        "thp,hpn->tn", grad_weighted, state_half, preferred_element_type=fl
    )
    grad_rows = jnp.concatenate(
        [
            grad_x.reshape(tok_rows, inner_width).astype(half),
            grad_b.astype(half),
            grad_c.astype(half),
        ],
        axis=1,
    )
    local_grad = jnp.einsum("tw,tf->wf", grad_rows, features, preferred_element_type=fl)
    total_grad = tree_psum(local_grad).T
    grad_in = total_grad / math.sqrt(series_count * seq_len)
    return (ssd_output, grad_in)


def solution(mesh):
    return jax.shard_map(
        on_device,
        mesh=mesh,
        in_specs=(P(None, ("tm", "series")), P(), P(), P(), P(), P(), P(), P("series", "tm", None)),
        out_specs=(P("series", "tm", None), P()),
        check_vma=False,
    )
```

```python
import math

import jax
import jax.numpy as jnp
from jax import lax
from jax.sharding import PartitionSpec as P

code_ceiling = 2097152.0


def decay_matrix(cum_decay):
    row_count = cum_decay.shape[0]
    causal = jnp.arange(row_count)[:, None] >= jnp.arange(row_count)[None, :]
    log_span = cum_decay.T[:, :, None] - cum_decay.T[:, None, :]
    return jnp.where(causal[None], jnp.exp(jnp.where(causal[None], log_span, -60.0)), 0.0)


def axis_bits(axis):
    size = lax.axis_size(axis)
    assert size & (size - 1) == 0
    return [1 << k for k in range(size.bit_length() - 1)]


def exchange(value, axis, flip):
    pairs = [(i, i ^ flip) for i in range(lax.axis_size(axis))]
    return lax.ppermute(value, axis, pairs)


def bit_groups():
    tm_bits, series_bits = axis_bits("tm"), axis_bits("series")
    groups = [("series", series_bits[:1])] if series_bits else []
    for axis, bits in (("tm", tm_bits), ("series", series_bits[1:])):
        groups += [(axis, bits[i : i + 2]) for i in range(0, len(bits), 2)]
    return groups


def group_round(value, axis, bits, scatter):
    index = lax.axis_index(axis)
    coord = sum(((index // b) % 2) * (1 << j) for j, b in enumerate(bits))
    size = 1 << len(bits)

    def flip_of(m):
        return sum(b for j, b in enumerate(bits) if (m >> j) & 1)

    rows = value.shape[0]
    if scatter:
        part = rows // size
        keep = lax.dynamic_slice_in_dim(value, coord * part, part)
        got = [
            exchange(lax.dynamic_slice_in_dim(value, (coord ^ m) * part, part), axis, flip_of(m))
            for m in range(1, size)
        ]
        for piece in got:
            keep = keep + piece
        return keep
    got = [value] + [exchange(value, axis, flip_of(m)) for m in range(1, size)]
    stacked = jnp.stack(got)
    return [lax.dynamic_index_in_dim(stacked, coord ^ q, 0, keepdims=False) for q in range(size)]


def tree_psum(value):
    done = []
    for axis, bits in bit_groups():
        if value.shape[0] % (8 << len(bits)) == 0:
            value = group_round(value, axis, bits, True)
            done.append((axis, bits))
        else:
            pieces = group_round(value, axis, bits, False)
            value = pieces[0]
            for piece in pieces[1:]:
                value = value + piece
    for axis, bits in reversed(done):
        value = jnp.concatenate(group_round(value, axis, bits, False))
    return value


def on_device(codes, owner_slot, edges, w_in, w_dt, dt_bias, decay_rate, grad_out):
    fl = jnp.float32
    half = jnp.bfloat16
    tok_rows = grad_out.shape[1]
    head_count = dt_bias.shape[0]
    inner_width = grad_out.shape[2]
    head_dim = inner_width // head_count
    state_dim = (w_in.shape[1] - inner_width) // 2
    n_blocks = lax.axis_size("tm")
    seq_len = tok_rows * n_blocks
    series_count = lax.axis_size("series")
    my_block = lax.axis_index("tm")

    ordered = jnp.take(codes, owner_slot, axis=0).astype(fl)
    outgoing = jnp.tile(ordered, (n_blocks, 1))
    reading = lax.all_to_all(outgoing, ("tm", "series"), split_axis=0, concat_axis=1, tiled=True)[0]
    edge_float = edges.astype(fl)
    upper_edge = jnp.concatenate([edge_float[1:], jnp.full((1,), code_ceiling, fl)])
    onehot = (
        (edge_float[None, :] <= reading[:, None]) & (upper_edge[None, :] > reading[:, None])
    ).astype(fl)
    counts = jnp.sum(onehot, axis=0)
    sent, counts = lax.optimization_barrier((grad_out[0].astype(fl), counts))
    before = jnp.cumsum(counts) - counts
    bin_table = jnp.stack([before, counts, edge_float, upper_edge - edge_float], axis=1)
    high = jnp.floor(bin_table / 65536.0) * 65536.0
    middle = jnp.floor((bin_table - high) / 256.0) * 256.0
    low = bin_table - high - middle
    pieces = jnp.concatenate([high, middle, low], axis=1).astype(half)
    picked3 = jnp.dot(onehot.astype(half), pieces, preferred_element_type=fl)
    width = bin_table.shape[1]
    picked = picked3[:, :width] + picked3[:, width : 2 * width] + picked3[:, 2 * width :]
    within_bin = (reading - picked[:, 2]) / picked[:, 3]
    quantile = (picked[:, 0] + picked[:, 1] * within_bin) / seq_len
    frequency = (jnp.arange(w_in.shape[0], dtype=fl) + 0.5) * math.pi
    features_all = jnp.cos(quantile[:, None] * frequency).astype(half)

    def mine(a):
        return lax.dynamic_index_in_dim(a, my_block, axis=0, keepdims=False)

    features_blocks = features_all.reshape(n_blocks, tok_rows, -1)
    features = mine(features_blocks)
    projected = jnp.dot(features, w_in, preferred_element_type=fl).astype(half)
    x_heads = projected[:, :inner_width].reshape(tok_rows, head_count, head_dim)
    b_proj = projected[:, inner_width : inner_width + state_dim]
    c_proj = projected[:, inner_width + state_dim :]
    step_size = jax.nn.softplus(dt_bias + jnp.dot(features, w_dt, preferred_element_type=fl))
    cum_decay = jnp.cumsum(-step_size * decay_rate, axis=0)
    tail_factor = jnp.exp(cum_decay[-1][None, :] - cum_decay) * step_size
    head_factor = jnp.exp(cum_decay)
    x_weighted = (x_heads * tail_factor[:, :, None]).astype(half)

    projected_all = jnp.dot(features_all, w_in, preferred_element_type=fl).astype(half)
    projected_all = projected_all.reshape(n_blocks, tok_rows, -1)
    x_all = projected_all[:, :, :inner_width].reshape(n_blocks, tok_rows, head_count, head_dim)
    b_all = projected_all[:, :, inner_width : inner_width + state_dim]
    step_all = jax.nn.softplus(
        dt_bias + jnp.dot(features_all, w_dt, preferred_element_type=fl)
    ).reshape(n_blocks, tok_rows, head_count)
    cum_all = jnp.cumsum(-step_all * decay_rate, axis=1)
    gate_all = jnp.exp(cum_all[:, -1])
    tail_all = jnp.exp(cum_all[:, -1:, :] - cum_all) * step_all
    head_all = jnp.exp(cum_all)
    earlier = n_blocks - 1
    xw_all = (x_all[:earlier] * tail_all[:earlier, :, :, None]).astype(half)
    state_local_all = jnp.einsum(
        "bthp,btn->bhpn", xw_all, b_all[:earlier], preferred_element_type=fl
    )

    state_in = jnp.zeros((head_count, head_dim, state_dim), fl)
    for k in range(n_blocks - 1):
        new = gate_all[k][:, None, None] * state_in + state_local_all[k]
        state_in = jnp.where(k < my_block, new, state_in)

    grad_heads = grad_out[0].reshape(tok_rows, head_count, head_dim)
    grad_weighted = (grad_heads * head_factor[:, :, None]).astype(half)
    adjoint_local = jnp.einsum("thp,tn->hpn", grad_weighted, c_proj, preferred_element_type=fl)
    adjoint_in = jnp.zeros((head_count, head_dim, state_dim), fl)
    if n_blocks == 4:
        along_x = lax.ppermute(sent, "tm", [(3, 2), (1, 0)])
        along_y = lax.ppermute(sent, "tm", [(3, 1), (2, 0)])
        diagonal = lax.ppermute(sent, "tm", [(2, 1), (3, 0)])
        seen = [
            along_x,
            jnp.where(my_block == 1, diagonal, along_y),
            jnp.where(my_block == 2, along_x, jnp.where(my_block == 1, along_y, diagonal)),
        ]
        c_all = projected_all[:, :, inner_width + state_dim :]
        for k in range(n_blocks - 1, 0, -1):
            later = seen[k - 1].reshape(tok_rows, head_count, head_dim)
            later_weighted = (later * head_all[k][:, :, None]).astype(half)
            later_local = jnp.einsum("thp,tn->hpn", later_weighted, c_all[k], preferred_element_type=fl)
            new = gate_all[k][:, None, None] * adjoint_in + later_local
            adjoint_in = jnp.where(k > my_block, new, adjoint_in)
    else:
        adjoint_all = lax.all_gather(adjoint_local, "tm")
        for k in range(n_blocks - 1, 0, -1):
            new = gate_all[k][:, None, None] * adjoint_in + adjoint_all[k]
            adjoint_in = jnp.where(k > my_block, new, adjoint_in)

    masked = decay_matrix(cum_decay) * step_size.T[:, None, :]
    scores = jnp.dot(c_proj, b_proj.T, preferred_element_type=fl)
    weights = (scores[None] * masked).astype(half)
    state_half = state_in.astype(half)
    adjoint_half = adjoint_in.astype(half)
    output = jnp.einsum("hts,shp->thp", weights, x_heads, preferred_element_type=fl)
    output = (
        output
        + jnp.einsum("tn,hpn->thp", c_proj, state_half, preferred_element_type=fl)
        * head_factor[:, :, None]
    )
    ssd_output = output.reshape(1, tok_rows, inner_width).astype(half)
    grad_x = jnp.einsum("hts,thp->shp", weights, grad_heads, preferred_element_type=fl)
    grad_x = (
        grad_x
        + jnp.einsum("sn,hpn->shp", b_proj, adjoint_half, preferred_element_type=fl)
        * tail_factor[:, :, None]
    )
    pair_scores = jnp.einsum("thp,shp->hts", grad_heads, x_heads, preferred_element_type=fl)
    pair_mixed = jnp.sum(pair_scores * masked, axis=0).astype(half)
    grad_b = jnp.dot(pair_mixed.T, c_proj, preferred_element_type=fl)
    grad_b = grad_b + jnp.einsum("shp,hpn->sn", x_weighted, adjoint_half, preferred_element_type=fl)
    grad_c = jnp.dot(pair_mixed, b_proj, preferred_element_type=fl)
    grad_c = grad_c + jnp.einsum(
        "thp,hpn->tn", grad_weighted, state_half, preferred_element_type=fl
    )
    grad_rows = jnp.concatenate(
        [
            grad_x.reshape(tok_rows, inner_width).astype(half),
            grad_b.astype(half),
            grad_c.astype(half),
        ],
        axis=1,
    )
    local_grad = jnp.einsum("tw,tf->wf", grad_rows, features, preferred_element_type=fl)
    total_grad = tree_psum(local_grad).T
    grad_in = total_grad / math.sqrt(series_count * seq_len)
    return (ssd_output, grad_in)


def solution(mesh):
    return jax.shard_map(
        on_device,
        mesh=mesh,
        in_specs=(P(None, ("tm", "series")), P(), P(), P(), P(), P(), P(), P("series", "tm", None)),
        out_specs=(P("series", "tm", None), P()),
        check_vma=False,
    )
```

```python
import math

import jax
import jax.numpy as jnp
from jax import lax
from jax.sharding import PartitionSpec as P

code_ceiling = 2097152.0


def decay_matrix(cum_decay):
    row_count = cum_decay.shape[0]
    causal = jnp.arange(row_count)[:, None] >= jnp.arange(row_count)[None, :]
    log_span = cum_decay.T[:, :, None] - cum_decay.T[:, None, :]
    return jnp.where(causal[None], jnp.exp(jnp.where(causal[None], log_span, -60.0)), 0.0)


def axis_bits(axis):
    size = lax.axis_size(axis)
    assert size & (size - 1) == 0
    return [1 << k for k in range(size.bit_length() - 1)]


def exchange(value, axis, flip):
    pairs = [(i, i ^ flip) for i in range(lax.axis_size(axis))]
    return lax.ppermute(value, axis, pairs)


def bit_groups():
    tm_bits, series_bits = axis_bits("tm"), axis_bits("series")
    groups = [("series", series_bits[:1])] if series_bits else []
    groups += [("tm", [b]) for b in tm_bits]
    rest = series_bits[1:]
    groups += [("series", rest[i : i + 2]) for i in range(0, len(rest), 2)]
    return groups


def group_round(value, axis, bits, scatter):
    index = lax.axis_index(axis)
    coord = sum(((index // b) % 2) * (1 << j) for j, b in enumerate(bits))
    size = 1 << len(bits)

    def flip_of(m):
        return sum(b for j, b in enumerate(bits) if (m >> j) & 1)

    rows = value.shape[0]
    if scatter:
        part = rows // size
        keep = lax.dynamic_slice_in_dim(value, coord * part, part)
        got = [
            exchange(lax.dynamic_slice_in_dim(value, (coord ^ m) * part, part), axis, flip_of(m))
            for m in range(1, size)
        ]
        for piece in got:
            keep = keep + piece
        return keep
    got = [value] + [exchange(value, axis, flip_of(m)) for m in range(1, size)]
    stacked = jnp.stack(got)
    return [lax.dynamic_index_in_dim(stacked, coord ^ q, 0, keepdims=False) for q in range(size)]


def tree_psum(value):
    done = []
    for axis, bits in bit_groups():
        if value.shape[0] % (8 << len(bits)) == 0:
            value = group_round(value, axis, bits, True)
            done.append((axis, bits))
        else:
            pieces = group_round(value, axis, bits, False)
            value = pieces[0]
            for piece in pieces[1:]:
                value = value + piece
    for axis, bits in reversed(done):
        value = jnp.concatenate(group_round(value, axis, bits, False))
    return value


def on_device(codes, owner_slot, edges, w_in, w_dt, dt_bias, decay_rate, grad_out):
    fl = jnp.float32
    half = jnp.bfloat16
    tok_rows = grad_out.shape[1]
    head_count = dt_bias.shape[0]
    inner_width = grad_out.shape[2]
    head_dim = inner_width // head_count
    state_dim = (w_in.shape[1] - inner_width) // 2
    n_blocks = lax.axis_size("tm")
    seq_len = tok_rows * n_blocks
    series_count = lax.axis_size("series")
    my_block = lax.axis_index("tm")

    ordered = jnp.take(codes, owner_slot, axis=0).astype(fl)
    outgoing = jnp.tile(ordered, (n_blocks, 1))
    reading = lax.all_to_all(outgoing, ("tm", "series"), split_axis=0, concat_axis=1, tiled=True)[0]
    edge_float = edges.astype(fl)
    upper_edge = jnp.concatenate([edge_float[1:], jnp.full((1,), code_ceiling, fl)])
    onehot = (
        (edge_float[None, :] <= reading[:, None]) & (upper_edge[None, :] > reading[:, None])
    ).astype(fl)
    counts = jnp.sum(onehot, axis=0)
    sent, counts = lax.optimization_barrier((grad_out[0].astype(fl), counts))
    before = jnp.cumsum(counts) - counts
    bin_table = jnp.stack([before, counts, edge_float, upper_edge - edge_float], axis=1)
    high = jnp.floor(bin_table / 65536.0) * 65536.0
    middle = jnp.floor((bin_table - high) / 256.0) * 256.0
    low = bin_table - high - middle
    pieces = jnp.concatenate([high, middle, low], axis=1).astype(half)
    picked3 = jnp.dot(onehot.astype(half), pieces, preferred_element_type=fl)
    width = bin_table.shape[1]
    picked = picked3[:, :width] + picked3[:, width : 2 * width] + picked3[:, 2 * width :]
    within_bin = (reading - picked[:, 2]) / picked[:, 3]
    quantile = (picked[:, 0] + picked[:, 1] * within_bin) / seq_len
    frequency = (jnp.arange(w_in.shape[0], dtype=fl) + 0.5) * math.pi
    features_all = jnp.cos(quantile[:, None] * frequency).astype(half)

    def mine(a):
        return lax.dynamic_index_in_dim(a, my_block, axis=0, keepdims=False)

    features_blocks = features_all.reshape(n_blocks, tok_rows, -1)
    features = mine(features_blocks)
    projected = jnp.dot(features, w_in, preferred_element_type=fl).astype(half)
    x_heads = projected[:, :inner_width].reshape(tok_rows, head_count, head_dim)
    b_proj = projected[:, inner_width : inner_width + state_dim]
    c_proj = projected[:, inner_width + state_dim :]
    step_size = jax.nn.softplus(dt_bias + jnp.dot(features, w_dt, preferred_element_type=fl))
    cum_decay = jnp.cumsum(-step_size * decay_rate, axis=0)
    tail_factor = jnp.exp(cum_decay[-1][None, :] - cum_decay) * step_size
    head_factor = jnp.exp(cum_decay)
    x_weighted = (x_heads * tail_factor[:, :, None]).astype(half)

    projected_all = jnp.dot(features_all, w_in, preferred_element_type=fl).astype(half)
    projected_all = projected_all.reshape(n_blocks, tok_rows, -1)
    x_all = projected_all[:, :, :inner_width].reshape(n_blocks, tok_rows, head_count, head_dim)
    b_all = projected_all[:, :, inner_width : inner_width + state_dim]
    step_all = jax.nn.softplus(
        dt_bias + jnp.dot(features_all, w_dt, preferred_element_type=fl)
    ).reshape(n_blocks, tok_rows, head_count)
    cum_all = jnp.cumsum(-step_all * decay_rate, axis=1)
    gate_all = jnp.exp(cum_all[:, -1])
    tail_all = jnp.exp(cum_all[:, -1:, :] - cum_all) * step_all
    head_all = jnp.exp(cum_all)
    earlier = n_blocks - 1
    xw_all = (x_all[:earlier] * tail_all[:earlier, :, :, None]).astype(half)
    state_local_all = jnp.einsum(
        "bthp,btn->bhpn", xw_all, b_all[:earlier], preferred_element_type=fl
    )

    state_in = jnp.zeros((head_count, head_dim, state_dim), fl)
    for k in range(n_blocks - 1):
        new = gate_all[k][:, None, None] * state_in + state_local_all[k]
        state_in = jnp.where(k < my_block, new, state_in)

    grad_heads = grad_out[0].reshape(tok_rows, head_count, head_dim)
    grad_weighted = (grad_heads * head_factor[:, :, None]).astype(half)
    adjoint_local = jnp.einsum("thp,tn->hpn", grad_weighted, c_proj, preferred_element_type=fl)
    adjoint_in = jnp.zeros((head_count, head_dim, state_dim), fl)
    if n_blocks == 4:
        along_x = lax.ppermute(sent, "tm", [(3, 2), (1, 0)])
        along_y = lax.ppermute(sent, "tm", [(3, 1), (2, 0)])
        diagonal = lax.ppermute(sent, "tm", [(2, 1), (3, 0)])
        seen = [
            along_x,
            jnp.where(my_block == 1, diagonal, along_y),
            jnp.where(my_block == 2, along_x, jnp.where(my_block == 1, along_y, diagonal)),
        ]
        c_all = projected_all[:, :, inner_width + state_dim :]
        for k in range(n_blocks - 1, 0, -1):
            later = seen[k - 1].reshape(tok_rows, head_count, head_dim)
            later_weighted = (later * head_all[k][:, :, None]).astype(half)
            later_local = jnp.einsum("thp,tn->hpn", later_weighted, c_all[k], preferred_element_type=fl)
            new = gate_all[k][:, None, None] * adjoint_in + later_local
            adjoint_in = jnp.where(k > my_block, new, adjoint_in)
    else:
        adjoint_all = lax.all_gather(adjoint_local, "tm")
        for k in range(n_blocks - 1, 0, -1):
            new = gate_all[k][:, None, None] * adjoint_in + adjoint_all[k]
            adjoint_in = jnp.where(k > my_block, new, adjoint_in)

    masked = decay_matrix(cum_decay) * step_size.T[:, None, :]
    scores = jnp.dot(c_proj, b_proj.T, preferred_element_type=fl)
    weights = (scores[None] * masked).astype(half)
    state_half = state_in.astype(half)
    adjoint_half = adjoint_in.astype(half)
    output = jnp.einsum("hts,shp->thp", weights, x_heads, preferred_element_type=fl)
    output = (
        output
        + jnp.einsum("tn,hpn->thp", c_proj, state_half, preferred_element_type=fl)
        * head_factor[:, :, None]
    )
    ssd_output = output.reshape(1, tok_rows, inner_width).astype(half)
    grad_x = jnp.einsum("hts,thp->shp", weights, grad_heads, preferred_element_type=fl)
    grad_x = (
        grad_x
        + jnp.einsum("sn,hpn->shp", b_proj, adjoint_half, preferred_element_type=fl)
        * tail_factor[:, :, None]
    )
    pair_scores = jnp.einsum("thp,shp->hts", grad_heads, x_heads, preferred_element_type=fl)
    pair_mixed = jnp.sum(pair_scores * masked, axis=0).astype(half)
    grad_b = jnp.dot(pair_mixed.T, c_proj, preferred_element_type=fl)
    grad_b = grad_b + jnp.einsum("shp,hpn->sn", x_weighted, adjoint_half, preferred_element_type=fl)
    grad_c = jnp.dot(pair_mixed, b_proj, preferred_element_type=fl)
    grad_c = grad_c + jnp.einsum(
        "thp,hpn->tn", grad_weighted, state_half, preferred_element_type=fl
    )
    grad_rows = jnp.concatenate(
        [
            grad_x.reshape(tok_rows, inner_width).astype(half),
            grad_b.astype(half),
            grad_c.astype(half),
        ],
        axis=1,
    )
    local_grad = jnp.einsum("tw,tf->wf", grad_rows, features, preferred_element_type=fl)
    total_grad = tree_psum(local_grad).T
    grad_in = total_grad / math.sqrt(series_count * seq_len)
    return (ssd_output, grad_in)


def solution(mesh):
    return jax.shard_map(
        on_device,
        mesh=mesh,
        in_specs=(P(None, ("tm", "series")), P(), P(), P(), P(), P(), P(), P("series", "tm", None)),
        out_specs=(P("series", "tm", None), P()),
        check_vma=False,
    )
```

```python
import math

import jax
import jax.numpy as jnp
from jax import lax
from jax.sharding import PartitionSpec as P

code_ceiling = 2097152.0


def decay_matrix(cum_decay):
    row_count = cum_decay.shape[0]
    causal = jnp.arange(row_count)[:, None] >= jnp.arange(row_count)[None, :]
    log_span = cum_decay.T[:, :, None] - cum_decay.T[:, None, :]
    return jnp.where(causal[None], jnp.exp(jnp.where(causal[None], log_span, -60.0)), 0.0)


def axis_bits(axis):
    size = lax.axis_size(axis)
    assert size & (size - 1) == 0
    return [1 << k for k in range(size.bit_length() - 1)]


def exchange(value, axis, flip):
    pairs = [(i, i ^ flip) for i in range(lax.axis_size(axis))]
    return lax.ppermute(value, axis, pairs)


def bit_groups():
    tm_bits, series_bits = axis_bits("tm"), axis_bits("series")
    groups = [("series", series_bits[:1])] if series_bits else []
    for axis, bits in (("tm", tm_bits), ("series", series_bits[1:])):
        groups += [(axis, bits[i : i + 2]) for i in range(0, len(bits), 2)]
    return groups


def group_round(value, axis, bits, scatter):
    index = lax.axis_index(axis)
    coord = sum(((index // b) % 2) * (1 << j) for j, b in enumerate(bits))
    size = 1 << len(bits)

    def flip_of(m):
        return sum(b for j, b in enumerate(bits) if (m >> j) & 1)

    rows = value.shape[0]
    if scatter:
        part = rows // size
        keep = lax.dynamic_slice_in_dim(value, coord * part, part)
        got = [
            exchange(lax.dynamic_slice_in_dim(value, (coord ^ m) * part, part), axis, flip_of(m))
            for m in range(1, size)
        ]
        for piece in got:
            keep = keep + piece
        return keep
    got = [value] + [exchange(value, axis, flip_of(m)) for m in range(1, size)]
    stacked = jnp.stack(got)
    return [lax.dynamic_index_in_dim(stacked, coord ^ q, 0, keepdims=False) for q in range(size)]


def tree_psum(value):
    done = []
    for axis, bits in bit_groups():
        if value.shape[0] % (8 << len(bits)) == 0:
            value = group_round(value, axis, bits, True)
            done.append((axis, bits))
        else:
            pieces = group_round(value, axis, bits, False)
            value = pieces[0]
            for piece in pieces[1:]:
                value = value + piece
    for axis, bits in reversed(done):
        value = jnp.concatenate(group_round(value, axis, bits, False))
    return value


def on_device(codes, owner_slot, edges, w_in, w_dt, dt_bias, decay_rate, grad_out):
    fl = jnp.float32
    half = jnp.bfloat16
    tok_rows = grad_out.shape[1]
    head_count = dt_bias.shape[0]
    inner_width = grad_out.shape[2]
    head_dim = inner_width // head_count
    state_dim = (w_in.shape[1] - inner_width) // 2
    n_blocks = lax.axis_size("tm")
    seq_len = tok_rows * n_blocks
    series_count = lax.axis_size("series")
    my_block = lax.axis_index("tm")

    outgoing = jnp.take(codes, jnp.tile(owner_slot, n_blocks), axis=0).astype(fl)
    reading = lax.all_to_all(outgoing, ("tm", "series"), split_axis=0, concat_axis=1, tiled=True)[0]
    edge_float = edges.astype(fl)
    upper_edge = jnp.concatenate([edge_float[1:], jnp.full((1,), code_ceiling, fl)])
    onehot = (
        (edge_float[None, :] <= reading[:, None]) & (upper_edge[None, :] > reading[:, None])
    ).astype(fl)
    counts = jnp.sum(onehot, axis=0)
    sent, counts = lax.optimization_barrier((grad_out[0].astype(fl), counts))
    before = jnp.cumsum(counts) - counts
    bin_table = jnp.stack([before, counts, edge_float, upper_edge - edge_float], axis=1)
    high = jnp.floor(bin_table / 65536.0) * 65536.0
    middle = jnp.floor((bin_table - high) / 256.0) * 256.0
    low = bin_table - high - middle
    pieces = jnp.concatenate([high, middle, low], axis=1).astype(half)
    picked3 = jnp.dot(onehot.astype(half), pieces, preferred_element_type=fl)
    width = bin_table.shape[1]
    picked = picked3[:, :width] + picked3[:, width : 2 * width] + picked3[:, 2 * width :]
    within_bin = (reading - picked[:, 2]) / picked[:, 3]
    quantile = (picked[:, 0] + picked[:, 1] * within_bin) / seq_len
    frequency = (jnp.arange(w_in.shape[0], dtype=fl) + 0.5) * math.pi
    features_all = jnp.cos(quantile[:, None] * frequency).astype(half)

    def mine(a):
        return lax.dynamic_index_in_dim(a, my_block, axis=0, keepdims=False)

    features_blocks = features_all.reshape(n_blocks, tok_rows, -1)
    features = mine(features_blocks)
    projected = jnp.dot(features, w_in, preferred_element_type=fl).astype(half)
    x_heads = projected[:, :inner_width].reshape(tok_rows, head_count, head_dim)
    b_proj = projected[:, inner_width : inner_width + state_dim]
    c_proj = projected[:, inner_width + state_dim :]
    step_size = jax.nn.softplus(dt_bias + jnp.dot(features, w_dt, preferred_element_type=fl))
    cum_decay = jnp.cumsum(-step_size * decay_rate, axis=0)
    tail_factor = jnp.exp(cum_decay[-1][None, :] - cum_decay) * step_size
    head_factor = jnp.exp(cum_decay)
    x_weighted = (x_heads * tail_factor[:, :, None]).astype(half)

    projected_all = jnp.dot(features_all, w_in, preferred_element_type=fl).astype(half)
    projected_all = projected_all.reshape(n_blocks, tok_rows, -1)
    x_all = projected_all[:, :, :inner_width].reshape(n_blocks, tok_rows, head_count, head_dim)
    b_all = projected_all[:, :, inner_width : inner_width + state_dim]
    step_all = jax.nn.softplus(
        dt_bias + jnp.dot(features_all, w_dt, preferred_element_type=fl)
    ).reshape(n_blocks, tok_rows, head_count)
    cum_all = jnp.cumsum(-step_all * decay_rate, axis=1)
    gate_all = jnp.exp(cum_all[:, -1])
    tail_all = jnp.exp(cum_all[:, -1:, :] - cum_all) * step_all
    head_all = jnp.exp(cum_all)
    earlier = n_blocks - 1
    xw_all = (x_all[:earlier] * tail_all[:earlier, :, :, None]).astype(half)
    state_local_all = jnp.einsum(
        "bthp,btn->bhpn", xw_all, b_all[:earlier], preferred_element_type=fl
    )

    state_in = jnp.zeros((head_count, head_dim, state_dim), fl)
    for k in range(n_blocks - 1):
        new = gate_all[k][:, None, None] * state_in + state_local_all[k]
        state_in = jnp.where(k < my_block, new, state_in)

    grad_heads = grad_out[0].reshape(tok_rows, head_count, head_dim)
    grad_weighted = (grad_heads * head_factor[:, :, None]).astype(half)
    adjoint_local = jnp.einsum("thp,tn->hpn", grad_weighted, c_proj, preferred_element_type=fl)
    adjoint_in = jnp.zeros((head_count, head_dim, state_dim), fl)
    if n_blocks == 4:
        along_x = lax.ppermute(sent, "tm", [(3, 2), (1, 0)])
        along_y = lax.ppermute(sent, "tm", [(3, 1), (2, 0)])
        diagonal = lax.ppermute(sent, "tm", [(2, 1), (3, 0)])
        seen = [
            along_x,
            jnp.where(my_block == 1, diagonal, along_y),
            jnp.where(my_block == 2, along_x, jnp.where(my_block == 1, along_y, diagonal)),
        ]
        c_all = projected_all[:, :, inner_width + state_dim :]
        for k in range(n_blocks - 1, 0, -1):
            later = seen[k - 1].reshape(tok_rows, head_count, head_dim)
            later_weighted = (later * head_all[k][:, :, None]).astype(half)
            later_local = jnp.einsum("thp,tn->hpn", later_weighted, c_all[k], preferred_element_type=fl)
            new = gate_all[k][:, None, None] * adjoint_in + later_local
            adjoint_in = jnp.where(k > my_block, new, adjoint_in)
    else:
        adjoint_all = lax.all_gather(adjoint_local, "tm")
        for k in range(n_blocks - 1, 0, -1):
            new = gate_all[k][:, None, None] * adjoint_in + adjoint_all[k]
            adjoint_in = jnp.where(k > my_block, new, adjoint_in)

    masked = decay_matrix(cum_decay) * step_size.T[:, None, :]
    scores = jnp.dot(c_proj, b_proj.T, preferred_element_type=fl)
    weights = (scores[None] * masked).astype(half)
    state_half = state_in.astype(half)
    adjoint_half = adjoint_in.astype(half)
    output = jnp.einsum("hts,shp->thp", weights, x_heads, preferred_element_type=fl)
    output = (
        output
        + jnp.einsum("tn,hpn->thp", c_proj, state_half, preferred_element_type=fl)
        * head_factor[:, :, None]
    )
    ssd_output = output.reshape(1, tok_rows, inner_width).astype(half)
    grad_x = jnp.einsum("hts,thp->shp", weights, grad_heads, preferred_element_type=fl)
    grad_x = (
        grad_x
        + jnp.einsum("sn,hpn->shp", b_proj, adjoint_half, preferred_element_type=fl)
        * tail_factor[:, :, None]
    )
    pair_scores = jnp.einsum("thp,shp->hts", grad_heads, x_heads, preferred_element_type=fl)
    pair_mixed = jnp.sum(pair_scores * masked, axis=0).astype(half)
    grad_b = jnp.dot(pair_mixed.T, c_proj, preferred_element_type=fl)
    grad_b = grad_b + jnp.einsum("shp,hpn->sn", x_weighted, adjoint_half, preferred_element_type=fl)
    grad_c = jnp.dot(pair_mixed, b_proj, preferred_element_type=fl)
    grad_c = grad_c + jnp.einsum(
        "thp,hpn->tn", grad_weighted, state_half, preferred_element_type=fl
    )
    grad_rows = jnp.concatenate(
        [
            grad_x.reshape(tok_rows, inner_width).astype(half),
            grad_b.astype(half),
            grad_c.astype(half),
        ],
        axis=1,
    )
    local_grad = jnp.einsum("tw,tf->wf", grad_rows, features, preferred_element_type=fl)
    total_grad = tree_psum(local_grad).T
    grad_in = total_grad / math.sqrt(series_count * seq_len)
    return (ssd_output, grad_in)


def solution(mesh):
    return jax.shard_map(
        on_device,
        mesh=mesh,
        in_specs=(P(None, ("tm", "series")), P(), P(), P(), P(), P(), P(), P("series", "tm", None)),
        out_specs=(P("series", "tm", None), P()),
        check_vma=False,
    )
```

```python
import math

import jax
import jax.numpy as jnp
from jax import lax
from jax.sharding import PartitionSpec as P

code_ceiling = 2097152.0


def decay_matrix(cum_decay):
    row_count = cum_decay.shape[0]
    causal = jnp.arange(row_count)[:, None] >= jnp.arange(row_count)[None, :]
    log_span = cum_decay.T[:, :, None] - cum_decay.T[:, None, :]
    return jnp.where(causal[None], jnp.exp(jnp.where(causal[None], log_span, -60.0)), 0.0)


def axis_bits(axis):
    size = lax.axis_size(axis)
    assert size & (size - 1) == 0
    return [1 << k for k in range(size.bit_length() - 1)]


def exchange(value, axis, flip):
    pairs = [(i, i ^ flip) for i in range(lax.axis_size(axis))]
    return lax.ppermute(value, axis, pairs)


def bit_groups():
    tm_bits, series_bits = axis_bits("tm"), axis_bits("series")
    groups = [("series", series_bits[:1])] if series_bits else []
    for axis, bits in (("tm", tm_bits), ("series", series_bits[1:])):
        groups += [(axis, bits[i : i + 2]) for i in range(0, len(bits), 2)]
    return groups


def group_round(value, axis, bits, scatter):
    index = lax.axis_index(axis)
    coord = sum(((index // b) % 2) * (1 << j) for j, b in enumerate(bits))
    size = 1 << len(bits)

    def flip_of(m):
        return sum(b for j, b in enumerate(bits) if (m >> j) & 1)

    rows = value.shape[0]
    if scatter:
        part = rows // size
        keep = lax.dynamic_slice_in_dim(value, coord * part, part)
        got = [
            exchange(lax.dynamic_slice_in_dim(value, (coord ^ m) * part, part), axis, flip_of(m))
            for m in range(1, size)
        ]
        for piece in got:
            keep = keep + piece
        return keep
    got = [value] + [exchange(value, axis, flip_of(m)) for m in range(1, size)]
    stacked = jnp.stack(got)
    return [lax.dynamic_index_in_dim(stacked, coord ^ q, 0, keepdims=False) for q in range(size)]


def tree_psum(value):
    done = []
    for axis, bits in bit_groups():
        if value.shape[0] % (8 << len(bits)) == 0:
            value = group_round(value, axis, bits, True)
            done.append((axis, bits))
        else:
            pieces = group_round(value, axis, bits, False)
            value = pieces[0]
            for piece in pieces[1:]:
                value = value + piece
    for axis, bits in reversed(done):
        value = jnp.concatenate(group_round(value, axis, bits, False))
    return value


def on_device(codes, owner_slot, edges, w_in, w_dt, dt_bias, decay_rate, grad_out):
    fl = jnp.float32
    half = jnp.bfloat16
    tok_rows = grad_out.shape[1]
    head_count = dt_bias.shape[0]
    inner_width = grad_out.shape[2]
    head_dim = inner_width // head_count
    state_dim = (w_in.shape[1] - inner_width) // 2
    n_blocks = lax.axis_size("tm")
    seq_len = tok_rows * n_blocks
    series_count = lax.axis_size("series")
    my_block = lax.axis_index("tm")

    outgoing = jnp.take(codes, jnp.tile(owner_slot, n_blocks), axis=0).astype(fl)
    reading = lax.all_to_all(outgoing, ("tm", "series"), split_axis=0, concat_axis=1, tiled=True)[0]
    edge_float = edges.astype(fl)
    upper_edge = jnp.concatenate([edge_float[1:], jnp.full((1,), code_ceiling, fl)])
    onehot = (
        (edge_float[None, :] <= reading[:, None]) & (upper_edge[None, :] > reading[:, None])
    ).astype(fl)
    counts = jnp.sum(onehot, axis=0)
    sent, counts = lax.optimization_barrier((grad_out[0].astype(fl), counts))
    before = jnp.cumsum(counts) - counts
    bin_table = jnp.stack([before, counts, edge_float, upper_edge - edge_float], axis=1)
    high = jnp.floor(bin_table / 65536.0) * 65536.0
    middle = jnp.floor((bin_table - high) / 256.0) * 256.0
    low = bin_table - high - middle
    pieces = jnp.concatenate([high, middle, low], axis=1).astype(half)
    picked3 = jnp.dot(onehot.astype(half), pieces, preferred_element_type=fl)
    width = bin_table.shape[1]
    picked = picked3[:, :width] + picked3[:, width : 2 * width] + picked3[:, 2 * width :]
    within_bin = (reading - picked[:, 2]) / picked[:, 3]
    quantile = (picked[:, 0] + picked[:, 1] * within_bin) / seq_len
    frequency = (jnp.arange(w_in.shape[0], dtype=fl) + 0.5) * math.pi
    features_all = jnp.cos(quantile[:, None] * frequency).astype(half)

    def mine(a):
        return lax.dynamic_index_in_dim(a, my_block, axis=0, keepdims=False)

    features_blocks = features_all.reshape(n_blocks, tok_rows, -1)
    features = mine(features_blocks)
    projected = jnp.dot(features, w_in, preferred_element_type=fl).astype(half)
    x_heads = projected[:, :inner_width].reshape(tok_rows, head_count, head_dim)
    b_proj = projected[:, inner_width : inner_width + state_dim]
    c_proj = projected[:, inner_width + state_dim :]
    step_size = jax.nn.softplus(dt_bias + jnp.dot(features, w_dt, preferred_element_type=fl))
    cum_decay = jnp.cumsum(-step_size * decay_rate, axis=0)
    tail_factor = jnp.exp(cum_decay[-1][None, :] - cum_decay) * step_size
    head_factor = jnp.exp(cum_decay)
    x_weighted = (x_heads * tail_factor[:, :, None]).astype(half)

    projected_all = jnp.dot(features_all, w_in, preferred_element_type=fl).astype(half)
    projected_all = projected_all.reshape(n_blocks, tok_rows, -1)
    x_all = projected_all[:, :, :inner_width].reshape(n_blocks, tok_rows, head_count, head_dim)
    b_all = projected_all[:, :, inner_width : inner_width + state_dim]
    step_all = jax.nn.softplus(
        dt_bias + jnp.dot(features_all, w_dt, preferred_element_type=fl)
    ).reshape(n_blocks, tok_rows, head_count)
    cum_all = jnp.cumsum(-step_all * decay_rate, axis=1)
    gate_all = jnp.exp(cum_all[:, -1])
    tail_all = jnp.exp(cum_all[:, -1:, :] - cum_all) * step_all
    head_all = jnp.exp(cum_all)
    earlier = n_blocks - 1
    xw_all = (x_all[:earlier] * tail_all[:earlier, :, :, None]).astype(half)
    xw_all = lax.optimization_barrier(xw_all)
    state_local_all = jnp.einsum(
        "bthp,btn->bhpn", xw_all, b_all[:earlier], preferred_element_type=fl
    )

    state_in = jnp.zeros((head_count, head_dim, state_dim), fl)
    for k in range(n_blocks - 1):
        new = gate_all[k][:, None, None] * state_in + state_local_all[k]
        state_in = jnp.where(k < my_block, new, state_in)

    grad_heads = grad_out[0].reshape(tok_rows, head_count, head_dim)
    grad_weighted = (grad_heads * head_factor[:, :, None]).astype(half)
    adjoint_local = jnp.einsum("thp,tn->hpn", grad_weighted, c_proj, preferred_element_type=fl)
    adjoint_in = jnp.zeros((head_count, head_dim, state_dim), fl)
    if n_blocks == 4:
        along_x = lax.ppermute(sent, "tm", [(3, 2), (1, 0)])
        along_y = lax.ppermute(sent, "tm", [(3, 1), (2, 0)])
        diagonal = lax.ppermute(sent, "tm", [(2, 1), (3, 0)])
        seen = [
            along_x,
            jnp.where(my_block == 1, diagonal, along_y),
            jnp.where(my_block == 2, along_x, jnp.where(my_block == 1, along_y, diagonal)),
        ]
        c_all = projected_all[:, :, inner_width + state_dim :]
        for k in range(n_blocks - 1, 0, -1):
            later = seen[k - 1].reshape(tok_rows, head_count, head_dim)
            later_weighted = (later * head_all[k][:, :, None]).astype(half)
            later_local = jnp.einsum("thp,tn->hpn", later_weighted, c_all[k], preferred_element_type=fl)
            new = gate_all[k][:, None, None] * adjoint_in + later_local
            adjoint_in = jnp.where(k > my_block, new, adjoint_in)
    else:
        adjoint_all = lax.all_gather(adjoint_local, "tm")
        for k in range(n_blocks - 1, 0, -1):
            new = gate_all[k][:, None, None] * adjoint_in + adjoint_all[k]
            adjoint_in = jnp.where(k > my_block, new, adjoint_in)

    masked = decay_matrix(cum_decay) * step_size.T[:, None, :]
    scores = jnp.dot(c_proj, b_proj.T, preferred_element_type=fl)
    weights = (scores[None] * masked).astype(half)
    state_half = state_in.astype(half)
    adjoint_half = adjoint_in.astype(half)
    output = jnp.einsum("hts,shp->thp", weights, x_heads, preferred_element_type=fl)
    output = (
        output
        + jnp.einsum("tn,hpn->thp", c_proj, state_half, preferred_element_type=fl)
        * head_factor[:, :, None]
    )
    ssd_output = output.reshape(1, tok_rows, inner_width).astype(half)
    grad_x = jnp.einsum("hts,thp->shp", weights, grad_heads, preferred_element_type=fl)
    grad_x = (
        grad_x
        + jnp.einsum("sn,hpn->shp", b_proj, adjoint_half, preferred_element_type=fl)
        * tail_factor[:, :, None]
    )
    pair_scores = jnp.einsum("thp,shp->hts", grad_heads, x_heads, preferred_element_type=fl)
    pair_mixed = jnp.sum(pair_scores * masked, axis=0).astype(half)
    grad_b = jnp.dot(pair_mixed.T, c_proj, preferred_element_type=fl)
    grad_b = grad_b + jnp.einsum("shp,hpn->sn", x_weighted, adjoint_half, preferred_element_type=fl)
    grad_c = jnp.dot(pair_mixed, b_proj, preferred_element_type=fl)
    grad_c = grad_c + jnp.einsum(
        "thp,hpn->tn", grad_weighted, state_half, preferred_element_type=fl
    )
    grad_rows = jnp.concatenate(
        [
            grad_x.reshape(tok_rows, inner_width).astype(half),
            grad_b.astype(half),
            grad_c.astype(half),
        ],
        axis=1,
    )
    local_grad = jnp.einsum("tw,tf->wf", grad_rows, features, preferred_element_type=fl)
    total_grad = tree_psum(local_grad).T
    grad_in = total_grad / math.sqrt(series_count * seq_len)
    return (ssd_output, grad_in)


def solution(mesh):
    return jax.shard_map(
        on_device,
        mesh=mesh,
        in_specs=(P(None, ("tm", "series")), P(), P(), P(), P(), P(), P(), P("series", "tm", None)),
        out_specs=(P("series", "tm", None), P()),
        check_vma=False,
    )
```

```python
import math

import jax
import jax.numpy as jnp
from jax import lax
from jax.sharding import PartitionSpec as P

code_ceiling = 2097152.0


def decay_matrix(cum_decay):
    row_count = cum_decay.shape[0]
    causal = jnp.arange(row_count)[:, None] >= jnp.arange(row_count)[None, :]
    log_span = cum_decay.T[:, :, None] - cum_decay.T[:, None, :]
    return jnp.where(causal[None], jnp.exp(jnp.where(causal[None], log_span, -60.0)), 0.0)


def axis_bits(axis):
    size = lax.axis_size(axis)
    assert size & (size - 1) == 0
    return [1 << k for k in range(size.bit_length() - 1)]


def exchange(value, axis, flip):
    pairs = [(i, i ^ flip) for i in range(lax.axis_size(axis))]
    return lax.ppermute(value, axis, pairs)


def bit_groups():
    tm_bits, series_bits = axis_bits("tm"), axis_bits("series")
    groups = [("series", series_bits[:1])] if series_bits else []
    for axis, bits in (("tm", tm_bits), ("series", series_bits[1:])):
        groups += [(axis, bits[i : i + 2]) for i in range(0, len(bits), 2)]
    return groups


def group_round(value, axis, bits, scatter):
    index = lax.axis_index(axis)
    coord = sum(((index // b) % 2) * (1 << j) for j, b in enumerate(bits))
    size = 1 << len(bits)

    def flip_of(m):
        return sum(b for j, b in enumerate(bits) if (m >> j) & 1)

    rows = value.shape[0]
    if scatter:
        part = rows // size
        keep = lax.dynamic_slice_in_dim(value, coord * part, part)
        got = [
            exchange(lax.dynamic_slice_in_dim(value, (coord ^ m) * part, part), axis, flip_of(m))
            for m in range(1, size)
        ]
        for piece in got:
            keep = keep + piece
        return keep
    got = [value] + [exchange(value, axis, flip_of(m)) for m in range(1, size)]
    stacked = jnp.stack(got)
    return [lax.dynamic_index_in_dim(stacked, coord ^ q, 0, keepdims=False) for q in range(size)]


def tree_psum(value):
    done = []
    for axis, bits in bit_groups():
        if value.shape[0] % (8 << len(bits)) == 0:
            value = group_round(value, axis, bits, True)
            done.append((axis, bits))
        else:
            pieces = group_round(value, axis, bits, False)
            value = pieces[0]
            for piece in pieces[1:]:
                value = value + piece
    for axis, bits in reversed(done):
        value = jnp.concatenate(group_round(value, axis, bits, False))
    return value


def on_device(codes, owner_slot, edges, w_in, w_dt, dt_bias, decay_rate, grad_out):
    fl = jnp.float32
    half = jnp.bfloat16
    tok_rows = grad_out.shape[1]
    head_count = dt_bias.shape[0]
    inner_width = grad_out.shape[2]
    head_dim = inner_width // head_count
    state_dim = (w_in.shape[1] - inner_width) // 2
    n_blocks = lax.axis_size("tm")
    seq_len = tok_rows * n_blocks
    series_count = lax.axis_size("series")
    my_block = lax.axis_index("tm")

    outgoing = jnp.take(codes, jnp.tile(owner_slot, n_blocks), axis=0).astype(fl)
    reading = lax.all_to_all(outgoing, ("tm", "series"), split_axis=0, concat_axis=1, tiled=True)[0]
    edge_float = edges.astype(fl)
    upper_edge = jnp.concatenate([edge_float[1:], jnp.full((1,), code_ceiling, fl)])
    onehot = (
        (edge_float[None, :] <= reading[:, None]) & (upper_edge[None, :] > reading[:, None])
    ).astype(fl)
    counts = jnp.sum(onehot, axis=0)
    sent, counts = lax.optimization_barrier((grad_out[0].astype(fl), counts))
    before = jnp.cumsum(counts) - counts
    bin_table = jnp.stack([before, counts, edge_float, upper_edge - edge_float], axis=1)
    high = jnp.floor(bin_table / 65536.0) * 65536.0
    middle = jnp.floor((bin_table - high) / 256.0) * 256.0
    low = bin_table - high - middle
    pieces = jnp.concatenate([high, middle, low], axis=1).astype(half)
    picked3 = jnp.dot(onehot.astype(half), pieces, preferred_element_type=fl)
    width = bin_table.shape[1]
    picked = picked3[:, :width] + picked3[:, width : 2 * width] + picked3[:, 2 * width :]
    within_bin = (reading - picked[:, 2]) / picked[:, 3]
    quantile = (picked[:, 0] + picked[:, 1] * within_bin) / seq_len
    frequency = (jnp.arange(w_in.shape[0], dtype=fl) + 0.5) * math.pi
    features_all = jnp.cos(quantile[:, None] * frequency).astype(half)

    def mine(a):
        return lax.dynamic_index_in_dim(a, my_block, axis=0, keepdims=False)

    features_blocks = features_all.reshape(n_blocks, tok_rows, -1)
    features = mine(features_blocks)
    projected = jnp.dot(features, w_in, preferred_element_type=fl).astype(half)
    x_heads = projected[:, :inner_width].reshape(tok_rows, head_count, head_dim)
    b_proj = projected[:, inner_width : inner_width + state_dim]
    c_proj = projected[:, inner_width + state_dim :]
    step_size = jax.nn.softplus(dt_bias + jnp.dot(features, w_dt, preferred_element_type=fl))
    cum_decay = jnp.cumsum(-step_size * decay_rate, axis=0)
    tail_factor = jnp.exp(cum_decay[-1][None, :] - cum_decay) * step_size
    head_factor = jnp.exp(cum_decay)
    x_weighted = (x_heads * tail_factor[:, :, None]).astype(half)

    projected_all = jnp.dot(features_all, w_in, preferred_element_type=fl).astype(half)
    projected_all = projected_all.reshape(n_blocks, tok_rows, -1)
    x_all = projected_all[:, :, :inner_width].reshape(n_blocks, tok_rows, head_count, head_dim)
    b_all = projected_all[:, :, inner_width : inner_width + state_dim]
    step_all = jax.nn.softplus(
        dt_bias + jnp.dot(features_all, w_dt, preferred_element_type=fl)
    ).reshape(n_blocks, tok_rows, head_count)
    cum_all = jnp.cumsum(-step_all * decay_rate, axis=1)
    gate_all = jnp.exp(cum_all[:, -1])
    tail_all = jnp.exp(cum_all[:, -1:, :] - cum_all) * step_all
    head_all = jnp.exp(cum_all)
    earlier = n_blocks - 1
    xw_all = (x_all[:earlier] * tail_all[:earlier, :, :, None]).astype(half)
    state_local_all = jnp.einsum(
        "bthp,btn->bhpn", xw_all, b_all[:earlier], preferred_element_type=fl
    )

    state_in = jnp.zeros((head_count, head_dim, state_dim), fl)
    for k in range(n_blocks - 1):
        new = gate_all[k][:, None, None] * state_in + state_local_all[k]
        state_in = jnp.where(k < my_block, new, state_in)

    grad_heads = grad_out[0].reshape(tok_rows, head_count, head_dim)
    grad_weighted = (grad_heads * head_factor[:, :, None]).astype(half)
    adjoint_local = jnp.einsum("thp,tn->hpn", grad_weighted, c_proj, preferred_element_type=fl)
    adjoint_in = jnp.zeros((head_count, head_dim, state_dim), fl)
    if n_blocks == 4:
        along_x = lax.ppermute(sent, "tm", [(3, 2), (1, 0)])
        along_y = lax.ppermute(sent, "tm", [(3, 1), (2, 0)])
        half_rows = tok_rows // 2
        direct = lax.ppermute(sent[:half_rows], "tm", [(2, 1), (3, 0)])
        held, state_in = lax.optimization_barrier((along_y[half_rows:], state_in))
        relayed = lax.ppermute(held, "tm", [(1, 0), (0, 1)])
        diagonal = jnp.concatenate([direct, relayed])
        seen = [
            along_x,
            jnp.where(my_block == 1, diagonal, along_y),
            jnp.where(my_block == 2, along_x, jnp.where(my_block == 1, along_y, diagonal)),
        ]
        c_all = projected_all[:, :, inner_width + state_dim :]
        for k in range(n_blocks - 1, 0, -1):
            later = seen[k - 1].reshape(tok_rows, head_count, head_dim)
            later_weighted = (later * head_all[k][:, :, None]).astype(half)
            later_local = jnp.einsum("thp,tn->hpn", later_weighted, c_all[k], preferred_element_type=fl)
            new = gate_all[k][:, None, None] * adjoint_in + later_local
            adjoint_in = jnp.where(k > my_block, new, adjoint_in)
    else:
        adjoint_all = lax.all_gather(adjoint_local, "tm")
        for k in range(n_blocks - 1, 0, -1):
            new = gate_all[k][:, None, None] * adjoint_in + adjoint_all[k]
            adjoint_in = jnp.where(k > my_block, new, adjoint_in)

    masked = decay_matrix(cum_decay) * step_size.T[:, None, :]
    scores = jnp.dot(c_proj, b_proj.T, preferred_element_type=fl)
    weights = (scores[None] * masked).astype(half)
    state_half = state_in.astype(half)
    adjoint_half = adjoint_in.astype(half)
    output = jnp.einsum("hts,shp->thp", weights, x_heads, preferred_element_type=fl)
    output = (
        output
        + jnp.einsum("tn,hpn->thp", c_proj, state_half, preferred_element_type=fl)
        * head_factor[:, :, None]
    )
    ssd_output = output.reshape(1, tok_rows, inner_width).astype(half)
    grad_x = jnp.einsum("hts,thp->shp", weights, grad_heads, preferred_element_type=fl)
    grad_x = (
        grad_x
        + jnp.einsum("sn,hpn->shp", b_proj, adjoint_half, preferred_element_type=fl)
        * tail_factor[:, :, None]
    )
    pair_scores = jnp.einsum("thp,shp->hts", grad_heads, x_heads, preferred_element_type=fl)
    pair_mixed = jnp.sum(pair_scores * masked, axis=0).astype(half)
    grad_b = jnp.dot(pair_mixed.T, c_proj, preferred_element_type=fl)
    grad_b = grad_b + jnp.einsum("shp,hpn->sn", x_weighted, adjoint_half, preferred_element_type=fl)
    grad_c = jnp.dot(pair_mixed, b_proj, preferred_element_type=fl)
    grad_c = grad_c + jnp.einsum(
        "thp,hpn->tn", grad_weighted, state_half, preferred_element_type=fl
    )
    grad_rows = jnp.concatenate(
        [
            grad_x.reshape(tok_rows, inner_width).astype(half),
            grad_b.astype(half),
            grad_c.astype(half),
        ],
        axis=1,
    )
    local_grad = jnp.einsum("tw,tf->wf", grad_rows, features, preferred_element_type=fl)
    total_grad = tree_psum(local_grad).T
    grad_in = total_grad / math.sqrt(series_count * seq_len)
    return (ssd_output, grad_in)


def solution(mesh):
    return jax.shard_map(
        on_device,
        mesh=mesh,
        in_specs=(P(None, ("tm", "series")), P(), P(), P(), P(), P(), P(), P("series", "tm", None)),
        out_specs=(P("series", "tm", None), P()),
        check_vma=False,
    )
```

```python
import math

import jax
import jax.numpy as jnp
from jax import lax
from jax.sharding import PartitionSpec as P

code_ceiling = 2097152.0


def decay_matrix(cum_decay):
    row_count = cum_decay.shape[0]
    causal = jnp.arange(row_count)[:, None] >= jnp.arange(row_count)[None, :]
    log_span = cum_decay.T[:, :, None] - cum_decay.T[:, None, :]
    return jnp.where(causal[None], jnp.exp(jnp.where(causal[None], log_span, -60.0)), 0.0)


def axis_bits(axis):
    size = lax.axis_size(axis)
    assert size & (size - 1) == 0
    return [1 << k for k in range(size.bit_length() - 1)]


def exchange(value, axis, flip):
    pairs = [(i, i ^ flip) for i in range(lax.axis_size(axis))]
    return lax.ppermute(value, axis, pairs)


def bit_groups():
    tm_bits, series_bits = axis_bits("tm"), axis_bits("series")
    groups = [("series", series_bits[:1])] if series_bits else []
    for axis, bits in (("tm", tm_bits), ("series", series_bits[1:])):
        groups += [(axis, bits[i : i + 2]) for i in range(0, len(bits), 2)]
    return groups


def group_round(value, axis, bits, scatter):
    index = lax.axis_index(axis)
    coord = sum(((index // b) % 2) * (1 << j) for j, b in enumerate(bits))
    size = 1 << len(bits)

    def flip_of(m):
        return sum(b for j, b in enumerate(bits) if (m >> j) & 1)

    rows = value.shape[0]
    if scatter:
        part = rows // size
        keep = lax.dynamic_slice_in_dim(value, coord * part, part)
        got = [
            exchange(lax.dynamic_slice_in_dim(value, (coord ^ m) * part, part), axis, flip_of(m))
            for m in range(1, size)
        ]
        for piece in got:
            keep = keep + piece
        return keep
    got = [value] + [exchange(value, axis, flip_of(m)) for m in range(1, size)]
    stacked = jnp.stack(got)
    return [lax.dynamic_index_in_dim(stacked, coord ^ q, 0, keepdims=False) for q in range(size)]


def tree_psum(value, finish):
    done = []
    for axis, bits in bit_groups():
        if value.shape[0] % (8 << len(bits)) == 0:
            value = group_round(value, axis, bits, True)
            done.append((axis, bits))
        else:
            pieces = group_round(value, axis, bits, False)
            value = pieces[0]
            for piece in pieces[1:]:
                value = value + piece
    for axis, bits in reversed(done[1:]):
        value = jnp.concatenate(group_round(value, axis, bits, False))
    axis, bits = done[0]
    return jnp.concatenate(group_round(finish(value).T, axis, bits, False), axis=1)


def on_device(codes, owner_slot, edges, w_in, w_dt, dt_bias, decay_rate, grad_out):
    fl = jnp.float32
    half = jnp.bfloat16
    tok_rows = grad_out.shape[1]
    head_count = dt_bias.shape[0]
    inner_width = grad_out.shape[2]
    head_dim = inner_width // head_count
    state_dim = (w_in.shape[1] - inner_width) // 2
    n_blocks = lax.axis_size("tm")
    seq_len = tok_rows * n_blocks
    series_count = lax.axis_size("series")
    my_block = lax.axis_index("tm")

    outgoing = jnp.take(codes, jnp.tile(owner_slot, n_blocks), axis=0).astype(fl)
    reading = lax.all_to_all(outgoing, ("tm", "series"), split_axis=0, concat_axis=1, tiled=True)[0]
    edge_float = edges.astype(fl)
    upper_edge = jnp.concatenate([edge_float[1:], jnp.full((1,), code_ceiling, fl)])
    onehot = (
        (edge_float[None, :] <= reading[:, None]) & (upper_edge[None, :] > reading[:, None])
    ).astype(fl)
    counts = jnp.sum(onehot, axis=0)
    sent, counts = lax.optimization_barrier((grad_out[0].astype(fl), counts))
    before = jnp.cumsum(counts) - counts
    bin_table = jnp.stack([before, counts, edge_float, upper_edge - edge_float], axis=1)
    high = jnp.floor(bin_table / 65536.0) * 65536.0
    middle = jnp.floor((bin_table - high) / 256.0) * 256.0
    low = bin_table - high - middle
    pieces = jnp.concatenate([high, middle, low], axis=1).astype(half)
    picked3 = jnp.dot(onehot.astype(half), pieces, preferred_element_type=fl)
    width = bin_table.shape[1]
    picked = picked3[:, :width] + picked3[:, width : 2 * width] + picked3[:, 2 * width :]
    within_bin = (reading - picked[:, 2]) / picked[:, 3]
    quantile = (picked[:, 0] + picked[:, 1] * within_bin) / seq_len
    frequency = (jnp.arange(w_in.shape[0], dtype=fl) + 0.5) * math.pi
    features_all = jnp.cos(quantile[:, None] * frequency).astype(half)

    def mine(a):
        return lax.dynamic_index_in_dim(a, my_block, axis=0, keepdims=False)

    features_blocks = features_all.reshape(n_blocks, tok_rows, -1)
    features = mine(features_blocks)
    projected = jnp.dot(features, w_in, preferred_element_type=fl).astype(half)
    x_heads = projected[:, :inner_width].reshape(tok_rows, head_count, head_dim)
    b_proj = projected[:, inner_width : inner_width + state_dim]
    c_proj = projected[:, inner_width + state_dim :]
    step_size = jax.nn.softplus(dt_bias + jnp.dot(features, w_dt, preferred_element_type=fl))
    cum_decay = jnp.cumsum(-step_size * decay_rate, axis=0)
    tail_factor = jnp.exp(cum_decay[-1][None, :] - cum_decay) * step_size
    head_factor = jnp.exp(cum_decay)
    x_weighted = (x_heads * tail_factor[:, :, None]).astype(half)

    projected_all = jnp.dot(features_all, w_in, preferred_element_type=fl).astype(half)
    projected_all = projected_all.reshape(n_blocks, tok_rows, -1)
    x_all = projected_all[:, :, :inner_width].reshape(n_blocks, tok_rows, head_count, head_dim)
    b_all = projected_all[:, :, inner_width : inner_width + state_dim]
    step_all = jax.nn.softplus(
        dt_bias + jnp.dot(features_all, w_dt, preferred_element_type=fl)
    ).reshape(n_blocks, tok_rows, head_count)
    cum_all = jnp.cumsum(-step_all * decay_rate, axis=1)
    gate_all = jnp.exp(cum_all[:, -1])
    tail_all = jnp.exp(cum_all[:, -1:, :] - cum_all) * step_all
    head_all = jnp.exp(cum_all)
    earlier = n_blocks - 1
    xw_all = (x_all[:earlier] * tail_all[:earlier, :, :, None]).astype(half)
    state_local_all = jnp.einsum(
        "bthp,btn->bhpn", xw_all, b_all[:earlier], preferred_element_type=fl
    )

    state_in = jnp.zeros((head_count, head_dim, state_dim), fl)
    for k in range(n_blocks - 1):
        new = gate_all[k][:, None, None] * state_in + state_local_all[k]
        state_in = jnp.where(k < my_block, new, state_in)

    grad_heads = grad_out[0].reshape(tok_rows, head_count, head_dim)
    grad_weighted = (grad_heads * head_factor[:, :, None]).astype(half)
    adjoint_local = jnp.einsum("thp,tn->hpn", grad_weighted, c_proj, preferred_element_type=fl)
    adjoint_in = jnp.zeros((head_count, head_dim, state_dim), fl)
    if n_blocks == 4:
        along_x = lax.ppermute(sent, "tm", [(3, 2), (1, 0)])
        along_y = lax.ppermute(sent, "tm", [(3, 1), (2, 0)])
        diagonal = lax.ppermute(sent, "tm", [(2, 1), (3, 0)])
        seen = [
            along_x,
            jnp.where(my_block == 1, diagonal, along_y),
            jnp.where(my_block == 2, along_x, jnp.where(my_block == 1, along_y, diagonal)),
        ]
        c_all = projected_all[:, :, inner_width + state_dim :]
        for k in range(n_blocks - 1, 0, -1):
            later = seen[k - 1].reshape(tok_rows, head_count, head_dim)
            later_weighted = (later * head_all[k][:, :, None]).astype(half)
            later_local = jnp.einsum("thp,tn->hpn", later_weighted, c_all[k], preferred_element_type=fl)
            new = gate_all[k][:, None, None] * adjoint_in + later_local
            adjoint_in = jnp.where(k > my_block, new, adjoint_in)
    else:
        adjoint_all = lax.all_gather(adjoint_local, "tm")
        for k in range(n_blocks - 1, 0, -1):
            new = gate_all[k][:, None, None] * adjoint_in + adjoint_all[k]
            adjoint_in = jnp.where(k > my_block, new, adjoint_in)

    masked = decay_matrix(cum_decay) * step_size.T[:, None, :]
    scores = jnp.dot(c_proj, b_proj.T, preferred_element_type=fl)
    weights = (scores[None] * masked).astype(half)
    state_half = state_in.astype(half)
    adjoint_half = adjoint_in.astype(half)
    output = jnp.einsum("hts,shp->thp", weights, x_heads, preferred_element_type=fl)
    output = (
        output
        + jnp.einsum("tn,hpn->thp", c_proj, state_half, preferred_element_type=fl)
        * head_factor[:, :, None]
    )
    ssd_output = output.reshape(1, tok_rows, inner_width).astype(half)
    grad_x = jnp.einsum("hts,thp->shp", weights, grad_heads, preferred_element_type=fl)
    grad_x = (
        grad_x
        + jnp.einsum("sn,hpn->shp", b_proj, adjoint_half, preferred_element_type=fl)
        * tail_factor[:, :, None]
    )
    pair_scores = jnp.einsum("thp,shp->hts", grad_heads, x_heads, preferred_element_type=fl)
    pair_mixed = jnp.sum(pair_scores * masked, axis=0).astype(half)
    grad_b = jnp.dot(pair_mixed.T, c_proj, preferred_element_type=fl)
    grad_b = grad_b + jnp.einsum("shp,hpn->sn", x_weighted, adjoint_half, preferred_element_type=fl)
    grad_c = jnp.dot(pair_mixed, b_proj, preferred_element_type=fl)
    grad_c = grad_c + jnp.einsum(
        "thp,hpn->tn", grad_weighted, state_half, preferred_element_type=fl
    )
    grad_rows = jnp.concatenate(
        [
            grad_x.reshape(tok_rows, inner_width).astype(half),
            grad_b.astype(half),
            grad_c.astype(half),
        ],
        axis=1,
    )
    local_grad = jnp.einsum("tw,tf->wf", grad_rows, features, preferred_element_type=fl)
    scale = math.sqrt(series_count * seq_len)
    grad_in = tree_psum(local_grad, lambda share: share / scale)
    return (ssd_output, grad_in)


def solution(mesh):
    return jax.shard_map(
        on_device,
        mesh=mesh,
        in_specs=(P(None, ("tm", "series")), P(), P(), P(), P(), P(), P(), P("series", "tm", None)),
        out_specs=(P("series", "tm", None), P()),
        check_vma=False,
    )
```

```python
import math

import jax
import jax.numpy as jnp
from jax import lax
from jax.sharding import PartitionSpec as P

code_ceiling = 2097152.0


def decay_matrix(cum_decay):
    row_count = cum_decay.shape[0]
    causal = jnp.arange(row_count)[:, None] >= jnp.arange(row_count)[None, :]
    log_span = cum_decay.T[:, :, None] - cum_decay.T[:, None, :]
    return jnp.where(causal[None], jnp.exp(jnp.where(causal[None], log_span, -60.0)), 0.0)


def axis_bits(axis):
    size = lax.axis_size(axis)
    assert size & (size - 1) == 0
    return [1 << k for k in range(size.bit_length() - 1)]


def exchange(value, axis, flip):
    pairs = [(i, i ^ flip) for i in range(lax.axis_size(axis))]
    return lax.ppermute(value, axis, pairs)


def bit_groups():
    tm_bits, series_bits = axis_bits("tm"), axis_bits("series")
    groups = [("series", series_bits[:1])] if series_bits else []
    groups += [("tm", tm_bits[i : i + 2]) for i in range(0, len(tm_bits), 2)]
    groups += [("series", [b]) for b in series_bits[1:]]
    return groups


def group_round(value, axis, bits, scatter):
    index = lax.axis_index(axis)
    coord = sum(((index // b) % 2) * (1 << j) for j, b in enumerate(bits))
    size = 1 << len(bits)

    def flip_of(m):
        return sum(b for j, b in enumerate(bits) if (m >> j) & 1)

    rows = value.shape[0]
    if scatter:
        part = rows // size
        keep = lax.dynamic_slice_in_dim(value, coord * part, part)
        got = [
            exchange(lax.dynamic_slice_in_dim(value, (coord ^ m) * part, part), axis, flip_of(m))
            for m in range(1, size)
        ]
        for piece in got:
            keep = keep + piece
        return keep
    got = [value] + [exchange(value, axis, flip_of(m)) for m in range(1, size)]
    stacked = jnp.stack(got)
    return [lax.dynamic_index_in_dim(stacked, coord ^ q, 0, keepdims=False) for q in range(size)]


def tree_psum(value):
    done = []
    for axis, bits in bit_groups():
        if value.shape[0] % (8 << len(bits)) == 0:
            value = group_round(value, axis, bits, True)
            done.append((axis, bits))
        else:
            pieces = group_round(value, axis, bits, False)
            value = pieces[0]
            for piece in pieces[1:]:
                value = value + piece
    for axis, bits in reversed(done):
        value = jnp.concatenate(group_round(value, axis, bits, False))
    return value


def on_device(codes, owner_slot, edges, w_in, w_dt, dt_bias, decay_rate, grad_out):
    fl = jnp.float32
    half = jnp.bfloat16
    tok_rows = grad_out.shape[1]
    head_count = dt_bias.shape[0]
    inner_width = grad_out.shape[2]
    head_dim = inner_width // head_count
    state_dim = (w_in.shape[1] - inner_width) // 2
    n_blocks = lax.axis_size("tm")
    seq_len = tok_rows * n_blocks
    series_count = lax.axis_size("series")
    my_block = lax.axis_index("tm")

    outgoing = jnp.take(codes, jnp.tile(owner_slot, n_blocks), axis=0).astype(fl)
    reading = lax.all_to_all(outgoing, ("tm", "series"), split_axis=0, concat_axis=1, tiled=True)[0]
    edge_float = edges.astype(fl)
    upper_edge = jnp.concatenate([edge_float[1:], jnp.full((1,), code_ceiling, fl)])
    onehot = (
        (edge_float[None, :] <= reading[:, None]) & (upper_edge[None, :] > reading[:, None])
    ).astype(fl)
    counts = jnp.sum(onehot, axis=0)
    sent, counts = lax.optimization_barrier((grad_out[0].astype(fl), counts))
    before = jnp.cumsum(counts) - counts
    bin_table = jnp.stack([before, counts, edge_float, upper_edge - edge_float], axis=1)
    high = jnp.floor(bin_table / 65536.0) * 65536.0
    middle = jnp.floor((bin_table - high) / 256.0) * 256.0
    low = bin_table - high - middle
    pieces = jnp.concatenate([high, middle, low], axis=1).astype(half)
    picked3 = jnp.dot(onehot.astype(half), pieces, preferred_element_type=fl)
    width = bin_table.shape[1]
    picked = picked3[:, :width] + picked3[:, width : 2 * width] + picked3[:, 2 * width :]
    within_bin = (reading - picked[:, 2]) / picked[:, 3]
    quantile = (picked[:, 0] + picked[:, 1] * within_bin) / seq_len
    frequency = (jnp.arange(w_in.shape[0], dtype=fl) + 0.5) * math.pi
    features_all = jnp.cos(quantile[:, None] * frequency).astype(half)

    def mine(a):
        return lax.dynamic_index_in_dim(a, my_block, axis=0, keepdims=False)

    features_blocks = features_all.reshape(n_blocks, tok_rows, -1)
    features = mine(features_blocks)
    projected = jnp.dot(features, w_in, preferred_element_type=fl).astype(half)
    x_heads = projected[:, :inner_width].reshape(tok_rows, head_count, head_dim)
    b_proj = projected[:, inner_width : inner_width + state_dim]
    c_proj = projected[:, inner_width + state_dim :]
    step_size = jax.nn.softplus(dt_bias + jnp.dot(features, w_dt, preferred_element_type=fl))
    cum_decay = jnp.cumsum(-step_size * decay_rate, axis=0)
    tail_factor = jnp.exp(cum_decay[-1][None, :] - cum_decay) * step_size
    head_factor = jnp.exp(cum_decay)
    x_weighted = (x_heads * tail_factor[:, :, None]).astype(half)

    projected_all = jnp.dot(features_all, w_in, preferred_element_type=fl).astype(half)
    projected_all = projected_all.reshape(n_blocks, tok_rows, -1)
    x_all = projected_all[:, :, :inner_width].reshape(n_blocks, tok_rows, head_count, head_dim)
    b_all = projected_all[:, :, inner_width : inner_width + state_dim]
    step_all = jax.nn.softplus(
        dt_bias + jnp.dot(features_all, w_dt, preferred_element_type=fl)
    ).reshape(n_blocks, tok_rows, head_count)
    cum_all = jnp.cumsum(-step_all * decay_rate, axis=1)
    gate_all = jnp.exp(cum_all[:, -1])
    tail_all = jnp.exp(cum_all[:, -1:, :] - cum_all) * step_all
    head_all = jnp.exp(cum_all)
    earlier = n_blocks - 1
    xw_all = (x_all[:earlier] * tail_all[:earlier, :, :, None]).astype(half)
    state_local_all = jnp.einsum(
        "bthp,btn->bhpn", xw_all, b_all[:earlier], preferred_element_type=fl
    )

    state_in = jnp.zeros((head_count, head_dim, state_dim), fl)
    for k in range(n_blocks - 1):
        new = gate_all[k][:, None, None] * state_in + state_local_all[k]
        state_in = jnp.where(k < my_block, new, state_in)

    grad_heads = grad_out[0].reshape(tok_rows, head_count, head_dim)
    grad_weighted = (grad_heads * head_factor[:, :, None]).astype(half)
    adjoint_local = jnp.einsum("thp,tn->hpn", grad_weighted, c_proj, preferred_element_type=fl)
    adjoint_in = jnp.zeros((head_count, head_dim, state_dim), fl)
    if n_blocks == 4:
        along_x = lax.ppermute(sent, "tm", [(3, 2), (1, 0)])
        along_y = lax.ppermute(sent, "tm", [(3, 1), (2, 0)])
        diagonal = lax.ppermute(sent, "tm", [(2, 1), (3, 0)])
        seen = [
            along_x,
            jnp.where(my_block == 1, diagonal, along_y),
            jnp.where(my_block == 2, along_x, jnp.where(my_block == 1, along_y, diagonal)),
        ]
        c_all = projected_all[:, :, inner_width + state_dim :]
        for k in range(n_blocks - 1, 0, -1):
            later = seen[k - 1].reshape(tok_rows, head_count, head_dim)
            later_weighted = (later * head_all[k][:, :, None]).astype(half)
            later_local = jnp.einsum("thp,tn->hpn", later_weighted, c_all[k], preferred_element_type=fl)
            new = gate_all[k][:, None, None] * adjoint_in + later_local
            adjoint_in = jnp.where(k > my_block, new, adjoint_in)
    else:
        adjoint_all = lax.all_gather(adjoint_local, "tm")
        for k in range(n_blocks - 1, 0, -1):
            new = gate_all[k][:, None, None] * adjoint_in + adjoint_all[k]
            adjoint_in = jnp.where(k > my_block, new, adjoint_in)

    masked = decay_matrix(cum_decay) * step_size.T[:, None, :]
    scores = jnp.dot(c_proj, b_proj.T, preferred_element_type=fl)
    weights = (scores[None] * masked).astype(half)
    state_half = state_in.astype(half)
    adjoint_half = adjoint_in.astype(half)
    output = jnp.einsum("hts,shp->thp", weights, x_heads, preferred_element_type=fl)
    output = (
        output
        + jnp.einsum("tn,hpn->thp", c_proj, state_half, preferred_element_type=fl)
        * head_factor[:, :, None]
    )
    ssd_output = output.reshape(1, tok_rows, inner_width).astype(half)
    grad_x = jnp.einsum("hts,thp->shp", weights, grad_heads, preferred_element_type=fl)
    grad_x = (
        grad_x
        + jnp.einsum("sn,hpn->shp", b_proj, adjoint_half, preferred_element_type=fl)
        * tail_factor[:, :, None]
    )
    pair_scores = jnp.einsum("thp,shp->hts", grad_heads, x_heads, preferred_element_type=fl)
    pair_mixed = jnp.sum(pair_scores * masked, axis=0).astype(half)
    grad_b = jnp.dot(pair_mixed.T, c_proj, preferred_element_type=fl)
    grad_b = grad_b + jnp.einsum("shp,hpn->sn", x_weighted, adjoint_half, preferred_element_type=fl)
    grad_c = jnp.dot(pair_mixed, b_proj, preferred_element_type=fl)
    grad_c = grad_c + jnp.einsum(
        "thp,hpn->tn", grad_weighted, state_half, preferred_element_type=fl
    )
    grad_rows = jnp.concatenate(
        [
            grad_x.reshape(tok_rows, inner_width).astype(half),
            grad_b.astype(half),
            grad_c.astype(half),
        ],
        axis=1,
    )
    local_grad = jnp.einsum("tw,tf->wf", grad_rows, features, preferred_element_type=fl)
    total_grad = tree_psum(local_grad).T
    grad_in = total_grad / math.sqrt(series_count * seq_len)
    return (ssd_output, grad_in)


def solution(mesh):
    return jax.shard_map(
        on_device,
        mesh=mesh,
        in_specs=(P(None, ("tm", "series")), P(), P(), P(), P(), P(), P(), P("series", "tm", None)),
        out_specs=(P("series", "tm", None), P()),
        check_vma=False,
    )
```
